32 devices in a mesh: section: 2 (over core), ctx: 4 (over y, x), tp: 4 (over z).
Axes of the slice: x: 2, y: 2, z: 4, core: 2. Of those that a mesh axis runs over, the one named last changes fastest.
Arguments:
- enc_out: bfloat16 [768, 4096], P(('section', 'tp'), 'ctx'), may hold values from -6 to 6
- enc_lengths: int32 [8], replicated, may hold values from 1 to 384, 768 in all
- dec_lengths: int32 [8], replicated, may hold values from 1 to 112, 224 in all
- queries: bfloat16 [2, 224, 4096], P('section', None, 'tp'), may hold values from -140 to 140
- key_weight: bfloat16 [2, 4096, 4096], P('section', 'ctx', 'tp'), may hold values from -0.09375 to 0.09375
- value_weight: bfloat16 [2, 4096, 4096], P('section', 'ctx', 'tp'), may hold values from -0.09375 to 0.09375
Outputs:
- context: bfloat16 [2, 224, 4096], P('section', 'ctx', 'tp')
The draws below stay inside these ranges and needn't reach their ends.
Inputs may be any that keep to these rules, and one draw needn't show every extreme that they name: `enc_lengths`: positive lengths that sum to 768; the longest is exactly 384. Encoder document g and decoder document g are the same document. `dec_lengths`: positive lengths that sum to 224; the longest is exactly 112.
All inputs are finite; a program needn't handle non-finite values.
Results may differ from the reference program's by a relative error of at most 0.04.
Values may be sent and summed in bfloat16 or wider, within the bound.
No kernel may reach another device: no remote copies, remote signals or barrier semaphores. Data moves between devices by JAX's collectives and lax.ppermute only.
A program may use at most 64 MiB of HBM per device.

```python
import math
import jax
import jax.numpy as jnp
import numpy as np
from jax import lax

H = 64
HD = 64
D = 4096
SEGS = 8
ENC = 768
DEC = 224
SECTIONS = 2
N_CTX = 4


def draw_queries(key, part):
    first_key, second_key = jax.random.split(key, 2)
    row_scale = jnp.exp(jax.random.uniform(second_key, (SECTIONS, DEC, 1), jnp.float32, math.log(0.5), math.log(4.0)))
    base = jnp.clip(jax.random.normal(first_key, (SECTIONS, DEC, D), jnp.float32), -6.0, 6.0)
    return (base * row_scale).astype(jnp.bfloat16)


def block_levels(own_key, shape, cuts, low, high):
    def one(dim, parts):
        heights = jax.random.uniform(jax.random.fold_in(jax.random.fold_in(own_key, 6), dim), (parts,), jnp.float32, low / len(cuts), high / len(cuts))
        return jnp.repeat(jnp.exp(heights), shape[dim] // parts).reshape((-1,) + (1,) * (len(shape) - dim - 1))

    gain = one(*cuts[0])
    for cut in cuts[1:]:
        gain = gain * one(*cut)
    return gain


def profile(count, total, bound, lean):
    loads = [(1 << 20) // math.isqrt(standing ** lean) + 1 for standing in range(2, count + 1)]
    spare, counts = total - bound - (count - 1), [1] * (count - 1)
    while spare > 0:
        movable = [i for i in range(count - 1) if counts[i] < bound]
        whole, remaining = sum([loads[i] for i in movable]), spare
        for i in movable:
            extra = min(bound - counts[i], max(1, remaining * loads[i] // whole), spare)
            counts[i] = counts[i] + extra
            spare = spare - extra
    return np.array([bound] + counts)


def ragged_sizes(stream_key, count, total, reach, lean):
    if count == 2:
        one = jax.random.randint(stream_key, (), max(1, total - reach), min(reach, total - 1) + 1)
        return jnp.stack([one, total - one])
    sizes = jnp.asarray(profile(count, total, reach, lean), jnp.int32)
    pairs = (count - 1) // 2
    giver, sink = sizes[1:1 + 2 * pairs:2], sizes[2:2 + 2 * pairs:2]
    slack = jnp.minimum(giver - 1, reach - sink)
    passed = jax.random.randint(jax.random.fold_in(stream_key, 1), (pairs,), 0, 1 << 20) % (slack + 1)
    sizes = sizes.at[1:1 + 2 * pairs:2].set(giver - passed).at[2:2 + 2 * pairs:2].set(sink + passed)
    return sizes[jax.random.permutation(jax.random.fold_in(stream_key, 2), count)]


def centred(own_key, extent, deviation, bound, shards=(), kind=jnp.bfloat16):
    array = deviation * jax.random.normal(own_key, extent, jnp.float32)
    if shards:
        array = array * block_levels(own_key, extent, shards, -0.22, 0.18)
    return jnp.clip(array, -bound, bound).astype(kind)


def setup_inputs(seed: int = 0) -> dict:
    splits = jax.random.split(jax.random.key(seed), 7)
    return {
        "enc_out": centred(splits[0], (ENC, D), 1.0, 6.0, ((0, 8), (1, 4))),
        "enc_lengths": ragged_sizes(splits[1], SEGS, ENC, ENC // 2, 2).astype(jnp.int32),
        "dec_lengths": ragged_sizes(splits[2], SEGS, DEC, DEC // 2, 2).astype(jnp.int32),
        "queries": draw_queries(jax.random.fold_in(splits[6], 71), 0),
        "key_weight": centred(splits[4], (SECTIONS, D, D), D ** -0.5, 0.09375, ((0, 2), (1, 4), (2, 4))),
        "value_weight": centred(splits[5], (SECTIONS, D, D), D ** -0.5, 0.09375, ((0, 2), (1, 4), (2, 4))),
    }


def document_ids(lengths, total):
    ends = jnp.cumsum(lengths).astype(jnp.int32)
    places = jnp.arange(total, dtype=jnp.int32)
    return lax.optimization_barrier(jnp.sum((places[:, None] >= ends[None, :]).astype(jnp.int32), axis=1)).astype(jnp.int32)

def project(enc_out, weight):
    width = D // N_CTX

    def add_group(running, group):
        first = (group * width).astype(jnp.int32)
        part = lax.dynamic_slice_in_dim(enc_out, first, width, 1)
        rows = lax.dynamic_slice_in_dim(weight, first, width, 0)
        term = jnp.dot(part, rows, preferred_element_type=jnp.float32).astype(jnp.bfloat16)
        term = lax.optimization_barrier(term)
        return (running + term.astype(jnp.float32), None)
    running, _ = lax.scan(add_group, jnp.zeros((ENC, D), jnp.float32), jnp.arange(N_CTX, dtype=jnp.int32))
    return running.astype(jnp.bfloat16)

def reference(enc_out, enc_lengths, dec_lengths, queries, key_weight, value_weight):
    enc_doc = document_ids(enc_lengths, ENC)
    dec_doc = document_ids(dec_lengths, DEC)
    allowed = dec_doc[:, None] == enc_doc[None, :]
    factor = 1.0 / math.sqrt(HD)

    def one_section(packed):
        section_queries, section_keys_w, section_values_w = packed
        keys = project(enc_out, section_keys_w)
        values = project(enc_out, section_values_w)

        def one_head(head):
            first = (head * HD).astype(jnp.int32)
            query_cols = lax.dynamic_slice_in_dim(section_queries, first, HD, 1)
            key_cols = lax.dynamic_slice_in_dim(keys, first, HD, 1)
            value_cols = lax.dynamic_slice_in_dim(values, first, HD, 1)
            scores = jnp.dot(query_cols, key_cols.T, preferred_element_type=jnp.float32) * factor
            scores = jnp.where(allowed, scores, jnp.float32(-1e+30))
            top = lax.optimization_barrier(jnp.max(scores, axis=1, keepdims=True))
            weights = jnp.where(allowed, jnp.exp(scores - top), jnp.float32(0.0))
            total = lax.optimization_barrier(jnp.sum(weights, axis=1, keepdims=True))
            numer = jnp.dot(weights.astype(jnp.bfloat16), value_cols, preferred_element_type=jnp.float32)
            return numer / total
        heads_out = lax.map(one_head, jnp.arange(H, dtype=jnp.int32))
        return jnp.transpose(heads_out, (1, 0, 2)).reshape(DEC, D).astype(jnp.bfloat16)
    return lax.map(one_section, (queries, key_weight, value_weight))
```

```python
import math

import jax
import jax.numpy as jnp
from jax import lax
from jax.sharding import PartitionSpec as P

HD = 64
N_CHUNKS = 1


def document_ids(lengths, places):
    ends = jnp.cumsum(lengths)
    return jnp.sum((places[:, None] >= ends[None, :]).astype(jnp.int32), axis=1)


def on_device(enc_out, enc_lengths, dec_lengths, queries, key_weight, value_weight):
    gathered = lax.all_gather(enc_out, ("section", "tp"), axis=0, tiled=True)
    head_width = key_weight.shape[2]
    heads_here = head_width // HD
    both_weights = jnp.concatenate([key_weight[0], value_weight[0]], axis=1)
    summed = lax.psum_scatter(
        jnp.dot(gathered, both_weights, preferred_element_type=jnp.float32).astype(jnp.bfloat16),
        "ctx",
        scatter_dimension=0,
        tiled=True,
    )
    local_keys = summed[:, :head_width]
    local_values = summed[:, head_width:]
    key_count = local_keys.shape[0]
    key_places = lax.axis_index("ctx") * key_count + jnp.arange(key_count, dtype=jnp.int32)
    enc_doc = document_ids(enc_lengths, key_places)
    section_queries = queries[0]
    query_count = section_queries.shape[0]
    dec_doc = document_ids(dec_lengths, jnp.arange(query_count, dtype=jnp.int32))
    allowed = dec_doc[:, None] == enc_doc[None, :]
    factor = 1.0 / math.sqrt(HD)
    query_heads = section_queries.reshape(query_count, heads_here, HD)
    key_heads = local_keys.reshape(key_count, heads_here, HD)
    value_heads = local_values.reshape(key_count, heads_here, HD)
    scores = (
        jnp.einsum("qhd,khd->hqk", query_heads, key_heads, preferred_element_type=jnp.float32)
        * factor
    )
    scores = jnp.where(allowed[None], scores, jnp.float32(-1e30))
    local_top = jnp.max(scores, axis=2)
    top = lax.pmax(local_top, "ctx")
    weights = jnp.where(allowed[None], jnp.exp(scores - top[:, :, None]), jnp.float32(0.0))
    totals = jnp.sum(weights, axis=2)
    numer = jnp.einsum(
        "hqk,khd->qhd",
        weights.astype(jnp.bfloat16),
        value_heads,
        preferred_element_type=jnp.float32,
    )
    numer = numer.reshape(query_count, head_width)
    numer_share, total_share = (
        lax.psum_scatter(numer.astype(jnp.bfloat16), "ctx", scatter_dimension=0, tiled=True).astype(
            jnp.float32
        ),
        lax.psum_scatter(
            totals.T.astype(jnp.bfloat16), "ctx", scatter_dimension=0, tiled=True
        ).astype(jnp.float32),
    )
    share_rows = numer_share.shape[0]
    result = numer_share.reshape(share_rows, heads_here, HD) / total_share[:, :, None]
    return result.reshape(1, share_rows, head_width).astype(jnp.bfloat16)


def shift_perm(n, d):
    return [(i, (i + d) % n) for i in range(n)]


def xor_perm(n, b):
    return [(i, i ^ b) for i in range(n)]


def make_fast(n_sec, n_ctx, n_tp, n_chunks):
    def fast(enc_out, enc_lengths, dec_lengths, queries, key_weight, value_weight):
        f32, bf16 = jnp.float32, jnp.bfloat16
        s = lax.axis_index("section")
        c = lax.axis_index("ctx")
        t = lax.axis_index("tp")
        rows, feat = enc_out.shape
        head_width = key_weight.shape[2]
        sub = head_width // n_ctx
        cr = rows // n_chunks
        wk = key_weight[0].reshape(feat, n_ctx, sub)
        wv = value_weight[0].reshape(feat, n_ctx, sub)
        yb = c // 2
        xb = c % 2

        def pick(x, i, axis):
            return lax.dynamic_index_in_dim(x, i, axis, keepdims=False)

        def add(a, b):
            return (a.astype(f32) + b.astype(f32)).astype(bf16)

        key_parts, value_parts, places = [], [], []
        for k in range(n_chunks):
            mine = enc_out[k * cr:(k + 1) * cr]
            blocks = [mine]
            for d in range(1, n_tp):
                blocks.append(lax.ppermute(mine, "tp", shift_perm(n_tp, d)))
            tp_stack = jnp.stack(blocks)
            sec_blocks = [tp_stack]
            for d in range(1, n_sec):
                sec_blocks.append(lax.ppermute(tp_stack, "section", shift_perm(n_sec, d)))
            e = jnp.stack(sec_blocks).reshape(n_sec * n_tp * cr, feat)
            d_sec = jnp.arange(n_sec, dtype=jnp.int32)[:, None, None]
            d_tp = jnp.arange(n_tp, dtype=jnp.int32)[None, :, None]
            r = jnp.arange(cr, dtype=jnp.int32)[None, None, :]
            src = ((s - d_sec) % n_sec) * n_tp + (t - d_tp) % n_tp
            places.append((src * rows + k * cr + r).reshape(-1))
            tokens = e.shape[0]
            half = tokens // 2
            pk = jnp.einsum("tf,fgc->gtc", e, wk, preferred_element_type=f32).astype(bf16)
            pv = jnp.einsum("tf,fgc->gtc", e, wv, preferred_element_type=f32).astype(bf16)
            pk = pk.reshape(2, 2, tokens, sub)
            pv = pv.reshape(2, 2, tokens, sub)
            a_pk, a_pv = pk[:, :, :half], pv[:, :, :half]
            got = lax.ppermute((pick(a_pk, 1 - yb, 0), pick(a_pv, 1 - yb, 0)), "ctx", xor_perm(n_ctx, 2))
            s1k = add(pick(a_pk, yb, 0), got[0])
            s1v = add(pick(a_pv, yb, 0), got[1])
            got = lax.ppermute((pick(s1k, 1 - xb, 0), pick(s1v, 1 - xb, 0)), "ctx", xor_perm(n_ctx, 1))
            fa_k = add(pick(s1k, xb, 0), got[0])
            fa_v = add(pick(s1v, xb, 0), got[1])
            b_pk, b_pv = pk[:, :, half:], pv[:, :, half:]
            got = lax.ppermute((pick(b_pk, 1 - xb, 1), pick(b_pv, 1 - xb, 1)), "ctx", xor_perm(n_ctx, 1))
            s2k = add(pick(b_pk, xb, 1), got[0])
            s2v = add(pick(b_pv, xb, 1), got[1])
            got = lax.ppermute((pick(s2k, 1 - yb, 0), pick(s2v, 1 - yb, 0)), "ctx", xor_perm(n_ctx, 2))
            fb_k = add(pick(s2k, yb, 0), got[0])
            fb_v = add(pick(s2v, yb, 0), got[1])
            key_parts += [fa_k, fb_k]
            value_parts += [fa_v, fb_v]

        keys = jnp.concatenate(key_parts, axis=0)
        values = jnp.concatenate(value_parts, axis=0)
        key_places = jnp.concatenate(places)
        key_count = keys.shape[0]
        heads = sub // HD
        enc_doc = document_ids(enc_lengths, key_places)
        section_queries = lax.dynamic_slice_in_dim(queries[0], c * sub, sub, axis=1)
        query_count = section_queries.shape[0]
        dec_doc = document_ids(dec_lengths, jnp.arange(query_count, dtype=jnp.int32))
        allowed = dec_doc[:, None] == enc_doc[None, :]
        factor = 1.0 / math.sqrt(HD)
        query_heads = section_queries.reshape(query_count, heads, HD)
        key_heads = keys.reshape(key_count, heads, HD)
        value_heads = values.reshape(key_count, heads, HD)
        scores = (
            jnp.einsum("qhd,khd->hqk", query_heads, key_heads, preferred_element_type=f32)
            * factor
        )
        scores = jnp.where(allowed[None], scores, f32(-1e30))
        top = jnp.max(scores, axis=2, keepdims=True)
        weights = jnp.where(allowed[None], jnp.exp(scores - top), f32(0.0))
        totals = jnp.sum(weights, axis=2)
        numer = jnp.einsum("hqk,khd->qhd", weights.astype(bf16), value_heads, preferred_element_type=f32)
        context = (numer / totals.T[:, :, None]).astype(bf16).reshape(query_count, sub)
        share = query_count // n_ctx
        blocks = context.reshape(n_ctx, share, sub)
        pieces = [pick(blocks, c, 0)]
        for d in range(1, n_ctx):
            pieces.append(lax.ppermute(pick(blocks, (c + d) % n_ctx, 0), "ctx", shift_perm(n_ctx, d)))
        pieces = jnp.stack(pieces)
        order = (c - jnp.arange(n_ctx, dtype=jnp.int32)) % n_ctx
        out = jnp.take(pieces, order, axis=0)
        return jnp.transpose(out, (1, 0, 2)).reshape(1, share, head_width)

    return fast


def solution(mesh):
    in_specs = (
        P(("section", "tp"), "ctx"),
        P(),
        P(),
        P("section", None, "tp"),
        P("section", "ctx", "tp"),
        P("section", "ctx", "tp"),
    )
    out_specs = P("section", "ctx", "tp")
    n_sec, n_ctx, n_tp = mesh.shape["section"], mesh.shape["ctx"], mesh.shape["tp"]
    return jax.shard_map(
        lambda *a: choose(n_sec, n_ctx, n_tp, *a), mesh=mesh, in_specs=in_specs, out_specs=out_specs, check_vma=False
    )


def choose(n_sec, n_ctx, n_tp, enc_out, enc_lengths, dec_lengths, queries, key_weight, value_weight):
    rows = enc_out.shape[0]
    head_width = key_weight.shape[2]
    query_count = queries.shape[1]
    ok = (
        n_ctx == 4
        and head_width % (n_ctx * HD) == 0
        and rows % N_CHUNKS == 0
        and (n_sec * n_tp * (rows // N_CHUNKS)) % 2 == 0
        and query_count % n_ctx == 0
    )
    args = (enc_out, enc_lengths, dec_lengths, queries, key_weight, value_weight)
    if ok:
        return make_fast(n_sec, n_ctx, n_tp, N_CHUNKS)(*args)
    return on_device(*args)
```

```python
import math

import jax
import jax.numpy as jnp
from jax import lax
from jax.sharding import PartitionSpec as P

HD = 64
N_CHUNKS = 2


def document_ids(lengths, places):
    ends = jnp.cumsum(lengths)
    return jnp.sum((places[:, None] >= ends[None, :]).astype(jnp.int32), axis=1)


def on_device(enc_out, enc_lengths, dec_lengths, queries, key_weight, value_weight):
    gathered = lax.all_gather(enc_out, ("section", "tp"), axis=0, tiled=True)
    head_width = key_weight.shape[2]
    heads_here = head_width // HD
    both_weights = jnp.concatenate([key_weight[0], value_weight[0]], axis=1)
    summed = lax.psum_scatter(
        jnp.dot(gathered, both_weights, preferred_element_type=jnp.float32).astype(jnp.bfloat16),
        "ctx",
        scatter_dimension=0,
        tiled=True,
    )
    local_keys = summed[:, :head_width]
    local_values = summed[:, head_width:]
    key_count = local_keys.shape[0]
    key_places = lax.axis_index("ctx") * key_count + jnp.arange(key_count, dtype=jnp.int32)
    enc_doc = document_ids(enc_lengths, key_places)
    section_queries = queries[0]
    query_count = section_queries.shape[0]
    dec_doc = document_ids(dec_lengths, jnp.arange(query_count, dtype=jnp.int32))
    allowed = dec_doc[:, None] == enc_doc[None, :]
    factor = 1.0 / math.sqrt(HD)
    query_heads = section_queries.reshape(query_count, heads_here, HD)
    key_heads = local_keys.reshape(key_count, heads_here, HD)
    value_heads = local_values.reshape(key_count, heads_here, HD)
    scores = (
        jnp.einsum("qhd,khd->hqk", query_heads, key_heads, preferred_element_type=jnp.float32)
        * factor
    )
    scores = jnp.where(allowed[None], scores, jnp.float32(-1e30))
    local_top = jnp.max(scores, axis=2)
    top = lax.pmax(local_top, "ctx")
    weights = jnp.where(allowed[None], jnp.exp(scores - top[:, :, None]), jnp.float32(0.0))
    totals = jnp.sum(weights, axis=2)
    numer = jnp.einsum(
        "hqk,khd->qhd",
        weights.astype(jnp.bfloat16),
        value_heads,
        preferred_element_type=jnp.float32,
    )
    numer = numer.reshape(query_count, head_width)
    numer_share, total_share = (
        lax.psum_scatter(numer.astype(jnp.bfloat16), "ctx", scatter_dimension=0, tiled=True).astype(
            jnp.float32
        ),
        lax.psum_scatter(
            totals.T.astype(jnp.bfloat16), "ctx", scatter_dimension=0, tiled=True
        ).astype(jnp.float32),
    )
    share_rows = numer_share.shape[0]
    result = numer_share.reshape(share_rows, heads_here, HD) / total_share[:, :, None]
    return result.reshape(1, share_rows, head_width).astype(jnp.bfloat16)


def shift_perm(n, d):
    return [(i, (i + d) % n) for i in range(n)]


def xor_perm(n, b):
    return [(i, i ^ b) for i in range(n)]


def make_fast(n_sec, n_ctx, n_tp, n_chunks):
    def fast(enc_out, enc_lengths, dec_lengths, queries, key_weight, value_weight):
        f32, bf16 = jnp.float32, jnp.bfloat16
        s = lax.axis_index("section")
        c = lax.axis_index("ctx")
        t = lax.axis_index("tp")
        rows, feat = enc_out.shape
        head_width = key_weight.shape[2]
        sub = head_width // n_ctx
        cr = rows // n_chunks
        wk = key_weight[0]
        wv = value_weight[0]
        yb = c // 2
        xb = c % 2

        def pick(x, i, axis):
            return lax.dynamic_index_in_dim(x, i, axis, keepdims=False)

        def add(a, b):
            return (a.astype(f32) + b.astype(f32)).astype(bf16)

        key_parts, value_parts, places = [], [], []
        e = None
        for k in range(n_chunks):
            mine = enc_out[k * cr:(k + 1) * cr]
            if e is not None:
                mine, _ = lax.optimization_barrier((mine, e))
            blocks = [mine]
            for d in range(1, n_tp):
                blocks.append(lax.ppermute(mine, "tp", shift_perm(n_tp, d)))
            tp_stack = jnp.stack(blocks)
            sec_blocks = [tp_stack]
            for d in range(1, n_sec):
                sec_blocks.append(lax.ppermute(tp_stack, "section", shift_perm(n_sec, d)))
            e = jnp.stack(sec_blocks).reshape(n_sec * n_tp * cr, feat)
            d_sec = jnp.arange(n_sec, dtype=jnp.int32)[:, None, None]
            d_tp = jnp.arange(n_tp, dtype=jnp.int32)[None, :, None]
            r = jnp.arange(cr, dtype=jnp.int32)[None, None, :]
            src = ((s - d_sec) % n_sec) * n_tp + (t - d_tp) % n_tp
            places.append((src * rows + k * cr + r).reshape(-1))
            tokens = e.shape[0]
            half = tokens // 2
            pk = jnp.dot(e, wk, preferred_element_type=f32).astype(bf16)
            pv = jnp.dot(e, wv, preferred_element_type=f32).astype(bf16)
            pk = jnp.transpose(pk.reshape(tokens, 2, 2, sub), (1, 2, 0, 3))
            pv = jnp.transpose(pv.reshape(tokens, 2, 2, sub), (1, 2, 0, 3))
            a_pk, a_pv = pk[:, :, :half], pv[:, :, :half]
            got = lax.ppermute((pick(a_pk, 1 - yb, 0), pick(a_pv, 1 - yb, 0)), "ctx", xor_perm(n_ctx, 2))
            s1k = add(pick(a_pk, yb, 0), got[0])
            s1v = add(pick(a_pv, yb, 0), got[1])
            got = lax.ppermute((pick(s1k, 1 - xb, 0), pick(s1v, 1 - xb, 0)), "ctx", xor_perm(n_ctx, 1))
            fa_k = add(pick(s1k, xb, 0), got[0])
            fa_v = add(pick(s1v, xb, 0), got[1])
            b_pk, b_pv = pk[:, :, half:], pv[:, :, half:]
            got = lax.ppermute((pick(b_pk, 1 - xb, 1), pick(b_pv, 1 - xb, 1)), "ctx", xor_perm(n_ctx, 1))
            s2k = add(pick(b_pk, xb, 1), got[0])
            s2v = add(pick(b_pv, xb, 1), got[1])
            got = lax.ppermute((pick(s2k, 1 - yb, 0), pick(s2v, 1 - yb, 0)), "ctx", xor_perm(n_ctx, 2))
            fb_k = add(pick(s2k, yb, 0), got[0])
            fb_v = add(pick(s2v, yb, 0), got[1])
            key_parts += [fa_k, fb_k]
            value_parts += [fa_v, fb_v]

        keys = jnp.concatenate(key_parts, axis=0)
        values = jnp.concatenate(value_parts, axis=0)
        key_places = jnp.concatenate(places)
        key_count = keys.shape[0]
        heads = sub // HD
        enc_doc = document_ids(enc_lengths, key_places)
        section_queries = lax.dynamic_slice_in_dim(queries[0], c * sub, sub, axis=1)
        query_count = section_queries.shape[0]
        dec_doc = document_ids(dec_lengths, jnp.arange(query_count, dtype=jnp.int32))
        allowed = dec_doc[:, None] == enc_doc[None, :]
        factor = 1.0 / math.sqrt(HD)
        query_heads = section_queries.reshape(query_count, heads, HD)
        key_heads = keys.reshape(key_count, heads, HD)
        value_heads = values.reshape(key_count, heads, HD)
        scores = (
            jnp.einsum("qhd,khd->hqk", query_heads, key_heads, preferred_element_type=f32)
            * factor
        )
        scores = jnp.where(allowed[None], scores, f32(-1e30))
        top = jnp.max(scores, axis=2, keepdims=True)
        weights = jnp.where(allowed[None], jnp.exp(scores - top), f32(0.0))
        totals = jnp.sum(weights, axis=2)
        numer = jnp.einsum("hqk,khd->qhd", weights.astype(bf16), value_heads, preferred_element_type=f32)
        context = (numer / totals.T[:, :, None]).astype(bf16).reshape(query_count, sub)
        share = query_count // n_ctx
        blocks = context.reshape(n_ctx, share, sub)
        pieces = [pick(blocks, c, 0)]
        for d in range(1, n_ctx):
            pieces.append(lax.ppermute(pick(blocks, (c + d) % n_ctx, 0), "ctx", shift_perm(n_ctx, d)))
        pieces = jnp.stack(pieces)
        order = (c - jnp.arange(n_ctx, dtype=jnp.int32)) % n_ctx
        out = jnp.take(pieces, order, axis=0)
        return jnp.transpose(out, (1, 0, 2)).reshape(1, share, head_width)

    return fast


def solution(mesh):
    in_specs = (
        P(("section", "tp"), "ctx"),
        P(),
        P(),
        P("section", None, "tp"),
        P("section", "ctx", "tp"),
        P("section", "ctx", "tp"),
    )
    out_specs = P("section", "ctx", "tp")
    n_sec, n_ctx, n_tp = mesh.shape["section"], mesh.shape["ctx"], mesh.shape["tp"]
    return jax.shard_map(
        lambda *a: choose(n_sec, n_ctx, n_tp, *a), mesh=mesh, in_specs=in_specs, out_specs=out_specs, check_vma=False
    )


def choose(n_sec, n_ctx, n_tp, enc_out, enc_lengths, dec_lengths, queries, key_weight, value_weight):
    rows = enc_out.shape[0]
    head_width = key_weight.shape[2]
    query_count = queries.shape[1]
    ok = (
        n_ctx == 4
        and head_width % (n_ctx * HD) == 0
        and rows % N_CHUNKS == 0
        and (n_sec * n_tp * (rows // N_CHUNKS)) % 2 == 0
        and query_count % n_ctx == 0
    )
    args = (enc_out, enc_lengths, dec_lengths, queries, key_weight, value_weight)
    if ok:
        return make_fast(n_sec, n_ctx, n_tp, N_CHUNKS)(*args)
    return on_device(*args)
```

```python
import math

import jax
import jax.numpy as jnp
from jax import lax
from jax.sharding import PartitionSpec as P

HD = 64
N_CHUNKS = 1


def document_ids(lengths, places):
    ends = jnp.cumsum(lengths)
    return jnp.sum((places[:, None] >= ends[None, :]).astype(jnp.int32), axis=1)


def on_device(enc_out, enc_lengths, dec_lengths, queries, key_weight, value_weight):
    gathered = lax.all_gather(enc_out, ("section", "tp"), axis=0, tiled=True)
    head_width = key_weight.shape[2]
    heads_here = head_width // HD
    both_weights = jnp.concatenate([key_weight[0], value_weight[0]], axis=1)
    summed = lax.psum_scatter(
        jnp.dot(gathered, both_weights, preferred_element_type=jnp.float32).astype(jnp.bfloat16),
        "ctx",
        scatter_dimension=0,
        tiled=True,
    )
    local_keys = summed[:, :head_width]
    local_values = summed[:, head_width:]
    key_count = local_keys.shape[0]
    key_places = lax.axis_index("ctx") * key_count + jnp.arange(key_count, dtype=jnp.int32)
    enc_doc = document_ids(enc_lengths, key_places)
    section_queries = queries[0]
    query_count = section_queries.shape[0]
    dec_doc = document_ids(dec_lengths, jnp.arange(query_count, dtype=jnp.int32))
    allowed = dec_doc[:, None] == enc_doc[None, :]
    factor = 1.0 / math.sqrt(HD)
    query_heads = section_queries.reshape(query_count, heads_here, HD)
    key_heads = local_keys.reshape(key_count, heads_here, HD)
    value_heads = local_values.reshape(key_count, heads_here, HD)
    scores = (
        jnp.einsum("qhd,khd->hqk", query_heads, key_heads, preferred_element_type=jnp.float32)
        * factor
    )
    scores = jnp.where(allowed[None], scores, jnp.float32(-1e30))
    local_top = jnp.max(scores, axis=2)
    top = lax.pmax(local_top, "ctx")
    weights = jnp.where(allowed[None], jnp.exp(scores - top[:, :, None]), jnp.float32(0.0))
    totals = jnp.sum(weights, axis=2)
    numer = jnp.einsum(
        "hqk,khd->qhd",
        weights.astype(jnp.bfloat16),
        value_heads,
        preferred_element_type=jnp.float32,
    )
    numer = numer.reshape(query_count, head_width)
    numer_share, total_share = (
        lax.psum_scatter(numer.astype(jnp.bfloat16), "ctx", scatter_dimension=0, tiled=True).astype(
            jnp.float32
        ),
        lax.psum_scatter(
            totals.T.astype(jnp.bfloat16), "ctx", scatter_dimension=0, tiled=True
        ).astype(jnp.float32),
    )
    share_rows = numer_share.shape[0]
    result = numer_share.reshape(share_rows, heads_here, HD) / total_share[:, :, None]
    return result.reshape(1, share_rows, head_width).astype(jnp.bfloat16)


def shift_perm(n, d):
    return [(i, (i + d) % n) for i in range(n)]


def xor_perm(n, b):
    return [(i, i ^ b) for i in range(n)]


def make_fast(n_sec, n_ctx, n_tp, n_chunks):
    def fast(enc_out, enc_lengths, dec_lengths, queries, key_weight, value_weight):
        f32, bf16 = jnp.float32, jnp.bfloat16
        s = lax.axis_index("section")
        c = lax.axis_index("ctx")
        t = lax.axis_index("tp")
        rows, feat = enc_out.shape
        head_width = key_weight.shape[2]
        sub = head_width // n_ctx
        cr = rows // n_chunks
        w_all = jnp.transpose(
            jnp.concatenate(
                [key_weight[0].reshape(feat, n_ctx, sub), value_weight[0].reshape(feat, n_ctx, sub)], axis=2
            ),
            (1, 0, 2),
        )
        yb = c // 2
        xb = c % 2

        def pick(x, i, axis):
            return lax.dynamic_index_in_dim(x, i, axis, keepdims=False)

        def add(a, b):
            return (a.astype(f32) + b.astype(f32)).astype(bf16)

        key_parts, value_parts, places = [], [], []
        e = None
        for k in range(n_chunks):
            mine = enc_out[k * cr:(k + 1) * cr]
            if e is not None:
                mine, _ = lax.optimization_barrier((mine, e))
            blocks = [mine]
            for d in range(1, n_tp):
                blocks.append(lax.ppermute(mine, "tp", shift_perm(n_tp, d)))
            tp_stack = jnp.stack(blocks)
            sec_blocks = [tp_stack]
            for d in range(1, n_sec):
                sec_blocks.append(lax.ppermute(tp_stack, "section", shift_perm(n_sec, d)))
            e = jnp.stack(sec_blocks).reshape(n_sec * n_tp * cr, feat)
            d_sec = jnp.arange(n_sec, dtype=jnp.int32)[:, None, None]
            d_tp = jnp.arange(n_tp, dtype=jnp.int32)[None, :, None]
            r = jnp.arange(cr, dtype=jnp.int32)[None, None, :]
            src = ((s - d_sec) % n_sec) * n_tp + (t - d_tp) % n_tp
            places.append((src * rows + k * cr + r).reshape(-1))
            tokens = e.shape[0]
            half = tokens // 2
            part = jnp.einsum("tf,gfc->gtc", e, w_all, preferred_element_type=f32).astype(bf16)
            part = part.reshape(2, 2, tokens, 2 * sub)
            a = part[:, :, :half]
            got = lax.ppermute(pick(a, 1 - yb, 0), "ctx", xor_perm(n_ctx, 2))
            s1 = add(pick(a, yb, 0), got)
            got = lax.ppermute(pick(s1, 1 - xb, 0), "ctx", xor_perm(n_ctx, 1))
            fa = add(pick(s1, xb, 0), got)
            b = part[:, :, half:]
            got = lax.ppermute(pick(b, 1 - xb, 1), "ctx", xor_perm(n_ctx, 1))
            s2 = add(pick(b, xb, 1), got)
            got = lax.ppermute(pick(s2, 1 - yb, 0), "ctx", xor_perm(n_ctx, 2))
            fb = add(pick(s2, yb, 0), got)
            key_parts += [fa[:, :sub], fb[:, :sub]]
            value_parts += [fa[:, sub:], fb[:, sub:]]

        keys = jnp.concatenate(key_parts, axis=0)
        values = jnp.concatenate(value_parts, axis=0)
        key_places = jnp.concatenate(places)
        key_count = keys.shape[0]
        heads = sub // HD
        enc_doc = document_ids(enc_lengths, key_places)
        section_queries = lax.dynamic_slice_in_dim(queries[0], c * sub, sub, axis=1)
        query_count = section_queries.shape[0]
        dec_doc = document_ids(dec_lengths, jnp.arange(query_count, dtype=jnp.int32))
        allowed = dec_doc[:, None] == enc_doc[None, :]
        factor = 1.0 / math.sqrt(HD)
        query_heads = section_queries.reshape(query_count, heads, HD)
        key_heads = keys.reshape(key_count, heads, HD)
        value_heads = values.reshape(key_count, heads, HD)
        scores = (
            jnp.einsum("qhd,khd->hqk", query_heads, key_heads, preferred_element_type=f32)
            * factor
        )
        scores = jnp.where(allowed[None], scores, f32(-1e30))
        top = jnp.max(scores, axis=2, keepdims=True)
        weights = jnp.where(allowed[None], jnp.exp(scores - top), f32(0.0))
        totals = jnp.sum(weights, axis=2)
        numer = jnp.einsum("hqk,khd->qhd", weights.astype(bf16), value_heads, preferred_element_type=f32)
        context = (numer / totals.T[:, :, None]).astype(bf16).reshape(query_count, sub)
        share = query_count // n_ctx
        blocks = context.reshape(n_ctx, share, sub)
        pieces = [pick(blocks, c, 0)]
        for d in range(1, n_ctx):
            pieces.append(lax.ppermute(pick(blocks, (c + d) % n_ctx, 0), "ctx", shift_perm(n_ctx, d)))
        pieces = jnp.stack(pieces)
        order = (c - jnp.arange(n_ctx, dtype=jnp.int32)) % n_ctx
        out = jnp.take(pieces, order, axis=0)
        return jnp.transpose(out, (1, 0, 2)).reshape(1, share, head_width)

    return fast


def solution(mesh):
    in_specs = (
        P(("section", "tp"), "ctx"),
        P(),
        P(),
        P("section", None, "tp"),
        P("section", "ctx", "tp"),
        P("section", "ctx", "tp"),
    )
    out_specs = P("section", "ctx", "tp")
    n_sec, n_ctx, n_tp = mesh.shape["section"], mesh.shape["ctx"], mesh.shape["tp"]
    return jax.shard_map(
        lambda *a: choose(n_sec, n_ctx, n_tp, *a), mesh=mesh, in_specs=in_specs, out_specs=out_specs, check_vma=False
    )


def choose(n_sec, n_ctx, n_tp, enc_out, enc_lengths, dec_lengths, queries, key_weight, value_weight):
    rows = enc_out.shape[0]
    head_width = key_weight.shape[2]
    query_count = queries.shape[1]
    ok = (
        n_ctx == 4
        and head_width % (n_ctx * HD) == 0
        and rows % N_CHUNKS == 0
        and (n_sec * n_tp * (rows // N_CHUNKS)) % 2 == 0
        and query_count % n_ctx == 0
    )
    args = (enc_out, enc_lengths, dec_lengths, queries, key_weight, value_weight)
    if ok:
        return make_fast(n_sec, n_ctx, n_tp, N_CHUNKS)(*args)
    return on_device(*args)
```

```python
import math

import jax
import jax.numpy as jnp
from jax import lax
from jax.sharding import PartitionSpec as P

HD = 64
N_CHUNKS = 2


def document_ids(lengths, places):
    ends = jnp.cumsum(lengths)
    return jnp.sum((places[:, None] >= ends[None, :]).astype(jnp.int32), axis=1)


def on_device(enc_out, enc_lengths, dec_lengths, queries, key_weight, value_weight):
    gathered = lax.all_gather(enc_out, ("section", "tp"), axis=0, tiled=True)
    head_width = key_weight.shape[2]
    heads_here = head_width // HD
    both_weights = jnp.concatenate([key_weight[0], value_weight[0]], axis=1)
    summed = lax.psum_scatter(
        jnp.dot(gathered, both_weights, preferred_element_type=jnp.float32).astype(jnp.bfloat16),
        "ctx",
        scatter_dimension=0,
        tiled=True,
    )
    local_keys = summed[:, :head_width]
    local_values = summed[:, head_width:]
    key_count = local_keys.shape[0]
    key_places = lax.axis_index("ctx") * key_count + jnp.arange(key_count, dtype=jnp.int32)
    enc_doc = document_ids(enc_lengths, key_places)
    section_queries = queries[0]
    query_count = section_queries.shape[0]
    dec_doc = document_ids(dec_lengths, jnp.arange(query_count, dtype=jnp.int32))
    allowed = dec_doc[:, None] == enc_doc[None, :]
    factor = 1.0 / math.sqrt(HD)
    query_heads = section_queries.reshape(query_count, heads_here, HD)
    key_heads = local_keys.reshape(key_count, heads_here, HD)
    value_heads = local_values.reshape(key_count, heads_here, HD)
    scores = (
        jnp.einsum("qhd,khd->hqk", query_heads, key_heads, preferred_element_type=jnp.float32)
        * factor
    )
    scores = jnp.where(allowed[None], scores, jnp.float32(-1e30))
    local_top = jnp.max(scores, axis=2)
    top = lax.pmax(local_top, "ctx")
    weights = jnp.where(allowed[None], jnp.exp(scores - top[:, :, None]), jnp.float32(0.0))
    totals = jnp.sum(weights, axis=2)
    numer = jnp.einsum(
        "hqk,khd->qhd",
        weights.astype(jnp.bfloat16),
        value_heads,
        preferred_element_type=jnp.float32,
    )
    numer = numer.reshape(query_count, head_width)
    numer_share, total_share = (
        lax.psum_scatter(numer.astype(jnp.bfloat16), "ctx", scatter_dimension=0, tiled=True).astype(
            jnp.float32
        ),
        lax.psum_scatter(
            totals.T.astype(jnp.bfloat16), "ctx", scatter_dimension=0, tiled=True
        ).astype(jnp.float32),
    )
    share_rows = numer_share.shape[0]
    result = numer_share.reshape(share_rows, heads_here, HD) / total_share[:, :, None]
    return result.reshape(1, share_rows, head_width).astype(jnp.bfloat16)


def shift_perm(n, d):
    return [(i, (i + d) % n) for i in range(n)]


def xor_perm(n, b):
    return [(i, i ^ b) for i in range(n)]


def make_fast(n_sec, n_ctx, n_tp, n_chunks):
    def fast(enc_out, enc_lengths, dec_lengths, queries, key_weight, value_weight):
        f32, bf16 = jnp.float32, jnp.bfloat16
        s = lax.axis_index("section")
        c = lax.axis_index("ctx")
        t = lax.axis_index("tp")
        rows, feat = enc_out.shape
        head_width = key_weight.shape[2]
        sub = head_width // n_ctx
        cr = rows // n_chunks
        wk = key_weight[0]
        wv = value_weight[0]
        yb = c // 2
        xb = c % 2

        def pick(x, i, axis):
            return lax.dynamic_index_in_dim(x, i, axis, keepdims=False)

        def add(a, b):
            return (a.astype(f32) + b.astype(f32)).astype(bf16)

        key_parts, value_parts, places = [], [], []
        ready = None
        for k in range(n_chunks):
            mine = enc_out[k * cr:(k + 1) * cr]
            if ready is not None:
                mine, _ = lax.optimization_barrier((mine, ready))
            blocks = [mine]
            for d in range(1, n_tp):
                blocks.append(lax.ppermute(mine, "tp", shift_perm(n_tp, d)))
            tp_stack = jnp.stack(blocks)
            if k > 0:
                tp_stack, _ = lax.optimization_barrier((tp_stack, landed))
            sec_blocks = [tp_stack]
            for d in range(1, n_sec):
                sec_blocks.append(lax.ppermute(tp_stack, "section", shift_perm(n_sec, d)))
            e = jnp.stack(sec_blocks).reshape(n_sec * n_tp * cr, feat)
            d_sec = jnp.arange(n_sec, dtype=jnp.int32)[:, None, None]
            d_tp = jnp.arange(n_tp, dtype=jnp.int32)[None, :, None]
            r = jnp.arange(cr, dtype=jnp.int32)[None, None, :]
            src = ((s - d_sec) % n_sec) * n_tp + (t - d_tp) % n_tp
            places.append((src * rows + k * cr + r).reshape(-1))
            tokens = e.shape[0]
            half = tokens // 2
            pk = jnp.dot(e, wk, preferred_element_type=f32).astype(bf16)
            pv = jnp.dot(e, wv, preferred_element_type=f32).astype(bf16)

            def blk(g, rows_):
                return [p[rows_, g * sub:(g + 1) * sub] for p in (pk, pv)]

            def sel(cond, a, b):
                return [jnp.where(cond, u, w) for u, w in zip(a, b)]

            lo, hi = slice(0, half), slice(half, tokens)
            send = sum([sel(yb == 0, blk(2 + x, lo), blk(x, lo)) for x in range(2)], [])
            own = sum([sel(yb == 0, blk(x, lo), blk(2 + x, lo)) for x in range(2)], [])
            send_a, own_a = jnp.stack(send), jnp.stack(own)
            send = sum([sel(xb == 0, blk(2 * y + 1, hi), blk(2 * y, hi)) for y in range(2)], [])
            own = sum([sel(xb == 0, blk(2 * y, hi), blk(2 * y + 1, hi)) for y in range(2)], [])
            send_b, own_b = jnp.stack(send), jnp.stack(own)
            ready = (send_a, send_b)
            got = lax.ppermute(send_a, "ctx", xor_perm(n_ctx, 2))
            landed = got
            s1 = add(own_a, got)
            send = sel(xb == 0, [s1[2], s1[3]], [s1[0], s1[1]])
            own = sel(xb == 0, [s1[0], s1[1]], [s1[2], s1[3]])
            got = lax.ppermute(jnp.stack(send), "ctx", xor_perm(n_ctx, 1))
            fa = add(jnp.stack(own), got)
            got = lax.ppermute(send_b, "ctx", xor_perm(n_ctx, 1))
            s2 = add(own_b, got)
            send = sel(yb == 0, [s2[2], s2[3]], [s2[0], s2[1]])
            own = sel(yb == 0, [s2[0], s2[1]], [s2[2], s2[3]])
            got = lax.ppermute(jnp.stack(send), "ctx", xor_perm(n_ctx, 2))
            fb = add(jnp.stack(own), got)
            key_parts += [fa[0], fb[0]]
            value_parts += [fa[1], fb[1]]

        keys = jnp.concatenate(key_parts, axis=0)
        values = jnp.concatenate(value_parts, axis=0)
        key_places = jnp.concatenate(places)
        key_count = keys.shape[0]
        heads = sub // HD
        enc_doc = document_ids(enc_lengths, key_places)
        section_queries = lax.dynamic_slice_in_dim(queries[0], c * sub, sub, axis=1)
        query_count = section_queries.shape[0]
        dec_doc = document_ids(dec_lengths, jnp.arange(query_count, dtype=jnp.int32))
        allowed = dec_doc[:, None] == enc_doc[None, :]
        factor = 1.0 / math.sqrt(HD)
        query_heads = section_queries.reshape(query_count, heads, HD)
        key_heads = keys.reshape(key_count, heads, HD)
        value_heads = values.reshape(key_count, heads, HD)
        scores = (
            jnp.einsum("qhd,khd->hqk", query_heads, key_heads, preferred_element_type=f32)
            * factor
        )
        scores = jnp.where(allowed[None], scores, f32(-1e30))
        top = jnp.max(scores, axis=2, keepdims=True)
        weights = jnp.where(allowed[None], jnp.exp(scores - top), f32(0.0))
        totals = jnp.sum(weights, axis=2)
        numer = jnp.einsum("hqk,khd->qhd", weights.astype(bf16), value_heads, preferred_element_type=f32)
        context = (numer / totals.T[:, :, None]).astype(bf16).reshape(query_count, sub)
        share = query_count // n_ctx
        blocks = context.reshape(n_ctx, share, sub)
        pieces = [pick(blocks, c, 0)]
        for d in range(1, n_ctx):
            pieces.append(lax.ppermute(pick(blocks, (c + d) % n_ctx, 0), "ctx", shift_perm(n_ctx, d)))
        pieces = jnp.stack(pieces)
        order = (c - jnp.arange(n_ctx, dtype=jnp.int32)) % n_ctx
        out = jnp.take(pieces, order, axis=0)
        return jnp.transpose(out, (1, 0, 2)).reshape(1, share, head_width)

    return fast


def solution(mesh):
    in_specs = (
        P(("section", "tp"), "ctx"),
        P(),
        P(),
        P("section", None, "tp"),
        P("section", "ctx", "tp"),
        P("section", "ctx", "tp"),
    )
    out_specs = P("section", "ctx", "tp")
    n_sec, n_ctx, n_tp = mesh.shape["section"], mesh.shape["ctx"], mesh.shape["tp"]
    return jax.shard_map(
        lambda *a: choose(n_sec, n_ctx, n_tp, *a), mesh=mesh, in_specs=in_specs, out_specs=out_specs, check_vma=False
    )


def choose(n_sec, n_ctx, n_tp, enc_out, enc_lengths, dec_lengths, queries, key_weight, value_weight):
    rows = enc_out.shape[0]
    head_width = key_weight.shape[2]
    query_count = queries.shape[1]
    ok = (
        n_ctx == 4
        and head_width % (n_ctx * HD) == 0
        and rows % N_CHUNKS == 0
        and (n_sec * n_tp * (rows // N_CHUNKS)) % 2 == 0
        and query_count % n_ctx == 0
    )
    args = (enc_out, enc_lengths, dec_lengths, queries, key_weight, value_weight)
    if ok:
        return make_fast(n_sec, n_ctx, n_tp, N_CHUNKS)(*args)
    return on_device(*args)
```

```python
import math

import jax
import jax.numpy as jnp
from jax import lax
from jax.sharding import PartitionSpec as P

HD = 64
N_CHUNKS = 1


def document_ids(lengths, places):
    ends = jnp.cumsum(lengths)
    return jnp.sum((places[:, None] >= ends[None, :]).astype(jnp.int32), axis=1)


def on_device(enc_out, enc_lengths, dec_lengths, queries, key_weight, value_weight):
    gathered = lax.all_gather(enc_out, ("section", "tp"), axis=0, tiled=True)
    head_width = key_weight.shape[2]
    heads_here = head_width // HD
    both_weights = jnp.concatenate([key_weight[0], value_weight[0]], axis=1)
    summed = lax.psum_scatter(
        jnp.dot(gathered, both_weights, preferred_element_type=jnp.float32).astype(jnp.bfloat16),
        "ctx",
        scatter_dimension=0,
        tiled=True,
    )
    local_keys = summed[:, :head_width]
    local_values = summed[:, head_width:]
    key_count = local_keys.shape[0]
    key_places = lax.axis_index("ctx") * key_count + jnp.arange(key_count, dtype=jnp.int32)
    enc_doc = document_ids(enc_lengths, key_places)
    section_queries = queries[0]
    query_count = section_queries.shape[0]
    dec_doc = document_ids(dec_lengths, jnp.arange(query_count, dtype=jnp.int32))
    allowed = dec_doc[:, None] == enc_doc[None, :]
    factor = 1.0 / math.sqrt(HD)
    query_heads = section_queries.reshape(query_count, heads_here, HD)
    key_heads = local_keys.reshape(key_count, heads_here, HD)
    value_heads = local_values.reshape(key_count, heads_here, HD)
    scores = (
        jnp.einsum("qhd,khd->hqk", query_heads, key_heads, preferred_element_type=jnp.float32)
        * factor
    )
    scores = jnp.where(allowed[None], scores, jnp.float32(-1e30))
    local_top = jnp.max(scores, axis=2)
    top = lax.pmax(local_top, "ctx")
    weights = jnp.where(allowed[None], jnp.exp(scores - top[:, :, None]), jnp.float32(0.0))
    totals = jnp.sum(weights, axis=2)
    numer = jnp.einsum(
        "hqk,khd->qhd",
        weights.astype(jnp.bfloat16),
        value_heads,
        preferred_element_type=jnp.float32,
    )
    numer = numer.reshape(query_count, head_width)
    numer_share, total_share = (
        lax.psum_scatter(numer.astype(jnp.bfloat16), "ctx", scatter_dimension=0, tiled=True).astype(
            jnp.float32
        ),
        lax.psum_scatter(
            totals.T.astype(jnp.bfloat16), "ctx", scatter_dimension=0, tiled=True
        ).astype(jnp.float32),
    )
    share_rows = numer_share.shape[0]
    result = numer_share.reshape(share_rows, heads_here, HD) / total_share[:, :, None]
    return result.reshape(1, share_rows, head_width).astype(jnp.bfloat16)


def shift_perm(n, d):
    return [(i, (i + d) % n) for i in range(n)]


def xor_perm(n, b):
    return [(i, i ^ b) for i in range(n)]


def make_fast(n_sec, n_ctx, n_tp, n_chunks):
    def fast(enc_out, enc_lengths, dec_lengths, queries, key_weight, value_weight):
        f32, bf16 = jnp.float32, jnp.bfloat16
        s = lax.axis_index("section")
        c = lax.axis_index("ctx")
        t = lax.axis_index("tp")
        rows, feat = enc_out.shape
        head_width = key_weight.shape[2]
        sub = head_width // n_ctx
        cr = rows // n_chunks
        wk = key_weight[0].reshape(feat, n_ctx, sub)
        wv = value_weight[0].reshape(feat, n_ctx, sub)
        yb = c // 2
        xb = c % 2

        def pick(x, i, axis):
            return lax.dynamic_index_in_dim(x, i, axis, keepdims=False)

        def add(a, b):
            return (a.astype(f32) + b.astype(f32)).astype(bf16)

        key_parts, value_parts, places = [], [], []
        for k in range(n_chunks):
            mine = enc_out[k * cr:(k + 1) * cr]
            tp_stack = lax.all_to_all(jnp.broadcast_to(mine[None], (n_tp,) + mine.shape), "tp", 0, 0)
            sec_blocks = [tp_stack]
            for d in range(1, n_sec):
                sec_blocks.append(lax.ppermute(tp_stack, "section", shift_perm(n_sec, d)))
            e = jnp.stack(sec_blocks).reshape(n_sec * n_tp * cr, feat)
            d_sec = jnp.arange(n_sec, dtype=jnp.int32)[:, None, None]
            d_tp = jnp.arange(n_tp, dtype=jnp.int32)[None, :, None]
            r = jnp.arange(cr, dtype=jnp.int32)[None, None, :]
            src = ((s - d_sec) % n_sec) * n_tp + d_tp
            places.append((src * rows + k * cr + r).reshape(-1))
            tokens = e.shape[0]
            half = tokens // 2
            pk = jnp.einsum("tf,fgc->gtc", e, wk, preferred_element_type=f32).astype(bf16)
            pv = jnp.einsum("tf,fgc->gtc", e, wv, preferred_element_type=f32).astype(bf16)
            pk = pk.reshape(2, 2, tokens, sub)
            pv = pv.reshape(2, 2, tokens, sub)
            a_pk, a_pv = pk[:, :, :half], pv[:, :, :half]
            got = lax.ppermute((pick(a_pk, 1 - yb, 0), pick(a_pv, 1 - yb, 0)), "ctx", xor_perm(n_ctx, 2))
            s1k = add(pick(a_pk, yb, 0), got[0])
            s1v = add(pick(a_pv, yb, 0), got[1])
            got = lax.ppermute((pick(s1k, 1 - xb, 0), pick(s1v, 1 - xb, 0)), "ctx", xor_perm(n_ctx, 1))
            fa_k = add(pick(s1k, xb, 0), got[0])
            fa_v = add(pick(s1v, xb, 0), got[1])
            b_pk, b_pv = pk[:, :, half:], pv[:, :, half:]
            got = lax.ppermute((pick(b_pk, 1 - xb, 1), pick(b_pv, 1 - xb, 1)), "ctx", xor_perm(n_ctx, 1))
            s2k = add(pick(b_pk, xb, 1), got[0])
            s2v = add(pick(b_pv, xb, 1), got[1])
            got = lax.ppermute((pick(s2k, 1 - yb, 0), pick(s2v, 1 - yb, 0)), "ctx", xor_perm(n_ctx, 2))
            fb_k = add(pick(s2k, yb, 0), got[0])
            fb_v = add(pick(s2v, yb, 0), got[1])
            key_parts += [fa_k, fb_k]
            value_parts += [fa_v, fb_v]

        keys = jnp.concatenate(key_parts, axis=0)
        values = jnp.concatenate(value_parts, axis=0)
        key_places = jnp.concatenate(places)
        key_count = keys.shape[0]
        heads = sub // HD
        enc_doc = document_ids(enc_lengths, key_places)
        section_queries = lax.dynamic_slice_in_dim(queries[0], c * sub, sub, axis=1)
        query_count = section_queries.shape[0]
        dec_doc = document_ids(dec_lengths, jnp.arange(query_count, dtype=jnp.int32))
        allowed = dec_doc[:, None] == enc_doc[None, :]
        factor = 1.0 / math.sqrt(HD)
        query_heads = section_queries.reshape(query_count, heads, HD)
        key_heads = keys.reshape(key_count, heads, HD)
        value_heads = values.reshape(key_count, heads, HD)
        scores = (
            jnp.einsum("qhd,khd->hqk", query_heads, key_heads, preferred_element_type=f32)
            * factor
        )
        scores = jnp.where(allowed[None], scores, f32(-1e30))
        top = jnp.max(scores, axis=2, keepdims=True)
        weights = jnp.where(allowed[None], jnp.exp(scores - top), f32(0.0))
        totals = jnp.sum(weights, axis=2)
        numer = jnp.einsum("hqk,khd->qhd", weights.astype(bf16), value_heads, preferred_element_type=f32)
        context = (numer / totals.T[:, :, None]).astype(bf16).reshape(query_count, sub)
        share = query_count // n_ctx
        blocks = context.reshape(n_ctx, share, sub)
        out = lax.all_to_all(blocks, "ctx", 0, 0)
        return jnp.transpose(out, (1, 0, 2)).reshape(1, share, head_width)

    return fast


def solution(mesh):
    in_specs = (
        P(("section", "tp"), "ctx"),
        P(),
        P(),
        P("section", None, "tp"),
        P("section", "ctx", "tp"),
        P("section", "ctx", "tp"),
    )
    out_specs = P("section", "ctx", "tp")
    n_sec, n_ctx, n_tp = mesh.shape["section"], mesh.shape["ctx"], mesh.shape["tp"]
    return jax.shard_map(
        lambda *a: choose(n_sec, n_ctx, n_tp, *a), mesh=mesh, in_specs=in_specs, out_specs=out_specs, check_vma=False
    )


def choose(n_sec, n_ctx, n_tp, enc_out, enc_lengths, dec_lengths, queries, key_weight, value_weight):
    rows = enc_out.shape[0]
    head_width = key_weight.shape[2]
    query_count = queries.shape[1]
    ok = (
        n_ctx == 4
        and head_width % (n_ctx * HD) == 0
        and rows % N_CHUNKS == 0
        and (n_sec * n_tp * (rows // N_CHUNKS)) % 2 == 0
        and query_count % n_ctx == 0
    )
    args = (enc_out, enc_lengths, dec_lengths, queries, key_weight, value_weight)
    if ok:
        return make_fast(n_sec, n_ctx, n_tp, N_CHUNKS)(*args)
    return on_device(*args)
```

```python
import math

import jax
import jax.numpy as jnp
from jax import lax
from jax.sharding import PartitionSpec as P

HD = 64


def document_ids(lengths, places):
    ends = jnp.cumsum(lengths)
    return jnp.sum((places[:, None] >= ends[None, :]).astype(jnp.int32), axis=1)


def on_device(enc_out, enc_lengths, dec_lengths, queries, key_weight, value_weight):
    gathered = lax.all_gather(enc_out, ("section", "tp"), axis=0, tiled=True)
    head_width = key_weight.shape[2]
    heads_here = head_width // HD
    both_weights = jnp.concatenate([key_weight[0], value_weight[0]], axis=1)
    summed = lax.psum_scatter(
        jnp.dot(gathered, both_weights, preferred_element_type=jnp.float32).astype(jnp.bfloat16),
        "ctx",
        scatter_dimension=0,
        tiled=True,
    )
    local_keys = summed[:, :head_width]
    local_values = summed[:, head_width:]
    key_count = local_keys.shape[0]
    key_places = lax.axis_index("ctx") * key_count + jnp.arange(key_count, dtype=jnp.int32)
    enc_doc = document_ids(enc_lengths, key_places)
    section_queries = queries[0]
    query_count = section_queries.shape[0]
    dec_doc = document_ids(dec_lengths, jnp.arange(query_count, dtype=jnp.int32))
    allowed = dec_doc[:, None] == enc_doc[None, :]
    factor = 1.0 / math.sqrt(HD)
    query_heads = section_queries.reshape(query_count, heads_here, HD)
    key_heads = local_keys.reshape(key_count, heads_here, HD)
    value_heads = local_values.reshape(key_count, heads_here, HD)
    scores = (
        jnp.einsum("qhd,khd->hqk", query_heads, key_heads, preferred_element_type=jnp.float32)
        * factor
    )
    scores = jnp.where(allowed[None], scores, jnp.float32(-1e30))
    local_top = jnp.max(scores, axis=2)
    top = lax.pmax(local_top, "ctx")
    weights = jnp.where(allowed[None], jnp.exp(scores - top[:, :, None]), jnp.float32(0.0))
    totals = jnp.sum(weights, axis=2)
    numer = jnp.einsum(
        "hqk,khd->qhd",
        weights.astype(jnp.bfloat16),
        value_heads,
        preferred_element_type=jnp.float32,
    )
    numer = numer.reshape(query_count, head_width)
    numer_share, total_share = (
        lax.psum_scatter(numer.astype(jnp.bfloat16), "ctx", scatter_dimension=0, tiled=True).astype(
            jnp.float32
        ),
        lax.psum_scatter(
            totals.T.astype(jnp.bfloat16), "ctx", scatter_dimension=0, tiled=True
        ).astype(jnp.float32),
    )
    share_rows = numer_share.shape[0]
    result = numer_share.reshape(share_rows, heads_here, HD) / total_share[:, :, None]
    return result.reshape(1, share_rows, head_width).astype(jnp.bfloat16)


def shift_perm(n, d):
    return [(i, (i + d) % n) for i in range(n)]


def xor_perm(n, b):
    return [(i, i ^ b) for i in range(n)]


def make_fast(n_sec, n_ctx, n_tp):
    def fast(enc_out, enc_lengths, dec_lengths, queries, key_weight, value_weight):
        f32, bf16 = jnp.float32, jnp.bfloat16
        s = lax.axis_index("section")
        c = lax.axis_index("ctx")
        t = lax.axis_index("tp")
        rows, feat = enc_out.shape
        head_width = key_weight.shape[2]
        sub = head_width // n_ctx
        wk = key_weight[0]
        wv = value_weight[0]
        yb = c // 2
        xb = c % 2

        def pick(x, i, axis):
            return lax.dynamic_index_in_dim(x, i, axis, keepdims=False)

        def add(a, b):
            return (a.astype(f32) + b.astype(f32)).astype(bf16)

        key_parts, value_parts, places = [], [], []
        blocks = [enc_out]
        for d in range(1, n_tp):
            blocks.append(lax.ppermute(enc_out, "tp", shift_perm(n_tp, d)))
        tp_stack = jnp.stack(blocks)
        d_tp = jnp.arange(n_tp, dtype=jnp.int32)[:, None]
        r = jnp.arange(rows, dtype=jnp.int32)[None, :]
        for d in range(n_sec):
            if d == 0:
                stack = tp_stack
            else:
                stack = lax.ppermute(tp_stack, "section", shift_perm(n_sec, d))
            e = stack.reshape(n_tp * rows, feat)
            src = ((s - d) % n_sec) * n_tp + (t - d_tp) % n_tp
            places.append((src * rows + r).reshape(-1))
            tokens = e.shape[0]
            half = tokens // 2
            pk = jnp.dot(e, wk, preferred_element_type=f32).astype(bf16)
            pv = jnp.dot(e, wv, preferred_element_type=f32).astype(bf16)

            def blk(g, rows_):
                return [p[rows_, g * sub:(g + 1) * sub] for p in (pk, pv)]

            def sel(cond, a, b):
                return [jnp.where(cond, u, w) for u, w in zip(a, b)]

            lo, hi = slice(0, half), slice(half, tokens)
            send = sum([sel(yb == 0, blk(2 + x, lo), blk(x, lo)) for x in range(2)], [])
            own = sum([sel(yb == 0, blk(x, lo), blk(2 + x, lo)) for x in range(2)], [])
            send_a, own_a = jnp.stack(send), jnp.stack(own)
            send = sum([sel(xb == 0, blk(2 * y + 1, hi), blk(2 * y, hi)) for y in range(2)], [])
            own = sum([sel(xb == 0, blk(2 * y, hi), blk(2 * y + 1, hi)) for y in range(2)], [])
            send_b, own_b = jnp.stack(send), jnp.stack(own)
            ready = (send_a, send_b)
            got = lax.ppermute(send_a, "ctx", xor_perm(n_ctx, 2))
            s1 = add(own_a, got)
            send = sel(xb == 0, [s1[2], s1[3]], [s1[0], s1[1]])
            own = sel(xb == 0, [s1[0], s1[1]], [s1[2], s1[3]])
            got = lax.ppermute(jnp.stack(send), "ctx", xor_perm(n_ctx, 1))
            fa = add(jnp.stack(own), got)
            got = lax.ppermute(send_b, "ctx", xor_perm(n_ctx, 1))
            s2 = add(own_b, got)
            send = sel(yb == 0, [s2[2], s2[3]], [s2[0], s2[1]])
            own = sel(yb == 0, [s2[0], s2[1]], [s2[2], s2[3]])
            got = lax.ppermute(jnp.stack(send), "ctx", xor_perm(n_ctx, 2))
            fb = add(jnp.stack(own), got)
            key_parts += [fa[0], fb[0]]
            value_parts += [fa[1], fb[1]]

        keys = jnp.concatenate(key_parts, axis=0)
        values = jnp.concatenate(value_parts, axis=0)
        key_places = jnp.concatenate(places)
        key_count = keys.shape[0]
        heads = sub // HD
        enc_doc = document_ids(enc_lengths, key_places)
        section_queries = lax.dynamic_slice_in_dim(queries[0], c * sub, sub, axis=1)
        query_count = section_queries.shape[0]
        dec_doc = document_ids(dec_lengths, jnp.arange(query_count, dtype=jnp.int32))
        allowed = dec_doc[:, None] == enc_doc[None, :]
        factor = 1.0 / math.sqrt(HD)
        query_heads = section_queries.reshape(query_count, heads, HD)
        key_heads = keys.reshape(key_count, heads, HD)
        value_heads = values.reshape(key_count, heads, HD)
        scores = (
            jnp.einsum("qhd,khd->hqk", query_heads, key_heads, preferred_element_type=f32)
            * factor
        )
        scores = jnp.where(allowed[None], scores, f32(-1e30))
        top = jnp.max(scores, axis=2, keepdims=True)
        weights = jnp.where(allowed[None], jnp.exp(scores - top), f32(0.0))
        totals = jnp.sum(weights, axis=2)
        numer = jnp.einsum("hqk,khd->qhd", weights.astype(bf16), value_heads, preferred_element_type=f32)
        context = (numer / totals.T[:, :, None]).astype(bf16).reshape(query_count, sub)
        share = query_count // n_ctx
        blocks = context.reshape(n_ctx, share, sub)
        pieces = [pick(blocks, c, 0)]
        for d in range(1, n_ctx):
            pieces.append(lax.ppermute(pick(blocks, (c + d) % n_ctx, 0), "ctx", shift_perm(n_ctx, d)))
        pieces = jnp.stack(pieces)
        order = (c - jnp.arange(n_ctx, dtype=jnp.int32)) % n_ctx
        out = jnp.take(pieces, order, axis=0)
        return jnp.transpose(out, (1, 0, 2)).reshape(1, share, head_width)

    return fast


def solution(mesh):
    in_specs = (
        P(("section", "tp"), "ctx"),
        P(),
        P(),
        P("section", None, "tp"),
        P("section", "ctx", "tp"),
        P("section", "ctx", "tp"),
    )
    out_specs = P("section", "ctx", "tp")
    n_sec, n_ctx, n_tp = mesh.shape["section"], mesh.shape["ctx"], mesh.shape["tp"]
    return jax.shard_map(
        lambda *a: choose(n_sec, n_ctx, n_tp, *a), mesh=mesh, in_specs=in_specs, out_specs=out_specs, check_vma=False
    )


def choose(n_sec, n_ctx, n_tp, enc_out, enc_lengths, dec_lengths, queries, key_weight, value_weight):
    rows = enc_out.shape[0]
    head_width = key_weight.shape[2]
    query_count = queries.shape[1]
    ok = (
        n_ctx == 4
        and head_width % (n_ctx * HD) == 0
        and (n_tp * rows) % 2 == 0
        and query_count % n_ctx == 0
    )
    args = (enc_out, enc_lengths, dec_lengths, queries, key_weight, value_weight)
    if ok:
        return make_fast(n_sec, n_ctx, n_tp)(*args)
    return on_device(*args)
```

```python
import math

import jax
import jax.numpy as jnp
from jax import lax
from jax.sharding import PartitionSpec as P

HD = 64


def document_ids(lengths, places):
    ends = jnp.cumsum(lengths)
    return jnp.sum((places[:, None] >= ends[None, :]).astype(jnp.int32), axis=1)


def on_device(enc_out, enc_lengths, dec_lengths, queries, key_weight, value_weight):
    gathered = lax.all_gather(enc_out, ("section", "tp"), axis=0, tiled=True)
    head_width = key_weight.shape[2]
    heads_here = head_width // HD
    both_weights = jnp.concatenate([key_weight[0], value_weight[0]], axis=1)
    summed = lax.psum_scatter(
        jnp.dot(gathered, both_weights, preferred_element_type=jnp.float32).astype(jnp.bfloat16),
        "ctx",
        scatter_dimension=0,
        tiled=True,
    )
    local_keys = summed[:, :head_width]
    local_values = summed[:, head_width:]
    key_count = local_keys.shape[0]
    key_places = lax.axis_index("ctx") * key_count + jnp.arange(key_count, dtype=jnp.int32)
    enc_doc = document_ids(enc_lengths, key_places)
    section_queries = queries[0]
    query_count = section_queries.shape[0]
    dec_doc = document_ids(dec_lengths, jnp.arange(query_count, dtype=jnp.int32))
    allowed = dec_doc[:, None] == enc_doc[None, :]
    factor = 1.0 / math.sqrt(HD)
    query_heads = section_queries.reshape(query_count, heads_here, HD)
    key_heads = local_keys.reshape(key_count, heads_here, HD)
    value_heads = local_values.reshape(key_count, heads_here, HD)
    scores = (
        jnp.einsum("qhd,khd->hqk", query_heads, key_heads, preferred_element_type=jnp.float32)
        * factor
    )
    scores = jnp.where(allowed[None], scores, jnp.float32(-1e30))
    local_top = jnp.max(scores, axis=2)
    top = lax.pmax(local_top, "ctx")
    weights = jnp.where(allowed[None], jnp.exp(scores - top[:, :, None]), jnp.float32(0.0))
    totals = jnp.sum(weights, axis=2)
    numer = jnp.einsum(
        "hqk,khd->qhd",
        weights.astype(jnp.bfloat16),
        value_heads,
        preferred_element_type=jnp.float32,
    )
    numer = numer.reshape(query_count, head_width)
    numer_share, total_share = (
        lax.psum_scatter(numer.astype(jnp.bfloat16), "ctx", scatter_dimension=0, tiled=True).astype(
            jnp.float32
        ),
        lax.psum_scatter(
            totals.T.astype(jnp.bfloat16), "ctx", scatter_dimension=0, tiled=True
        ).astype(jnp.float32),
    )
    share_rows = numer_share.shape[0]
    result = numer_share.reshape(share_rows, heads_here, HD) / total_share[:, :, None]
    return result.reshape(1, share_rows, head_width).astype(jnp.bfloat16)


def shift_perm(n, d):
    return [(i, (i + d) % n) for i in range(n)]


def xor_perm(n, b):
    return [(i, i ^ b) for i in range(n)]


def make_fast(n_sec, n_ctx, n_tp):
    def fast(enc_out, enc_lengths, dec_lengths, queries, key_weight, value_weight):
        f32, bf16 = jnp.float32, jnp.bfloat16
        s = lax.axis_index("section")
        c = lax.axis_index("ctx")
        t = lax.axis_index("tp")
        rows, feat = enc_out.shape
        head_width = key_weight.shape[2]
        sub = head_width // n_ctx
        w_all = jnp.concatenate(
            [key_weight[0].reshape(feat, n_ctx, sub), value_weight[0].reshape(feat, n_ctx, sub)], axis=1
        )
        yb = c // 2
        xb = c % 2

        def pick(x, i, axis):
            return lax.dynamic_index_in_dim(x, i, axis, keepdims=False)

        def add(a, b):
            return (a.astype(f32) + b.astype(f32)).astype(bf16)

        key_parts, value_parts, places = [], [], []
        blocks = [enc_out]
        for d in range(1, n_tp):
            blocks.append(lax.ppermute(enc_out, "tp", shift_perm(n_tp, d)))
        tp_stack = jnp.stack(blocks)
        d_tp = jnp.arange(n_tp, dtype=jnp.int32)[:, None]
        r = jnp.arange(rows, dtype=jnp.int32)[None, :]
        for d in range(n_sec):
            if d == 0:
                stack = tp_stack
            else:
                stack = lax.ppermute(tp_stack, "section", shift_perm(n_sec, d))
            e = stack.reshape(n_tp * rows, feat)
            src = ((s - d) % n_sec) * n_tp + (t - d_tp) % n_tp
            places.append((src * rows + r).reshape(-1))
            tokens = e.shape[0]
            half = tokens // 2
            part = jnp.einsum("tf,fgc->gtc", e, w_all, preferred_element_type=f32).astype(bf16)
            part = part.reshape(2, 2, 2, tokens, sub)
            a = part[:, :, :, :half]
            got = lax.ppermute(pick(a, 1 - yb, 1), "ctx", xor_perm(n_ctx, 2))
            s1 = add(pick(a, yb, 1), got)
            got = lax.ppermute(pick(s1, 1 - xb, 1), "ctx", xor_perm(n_ctx, 1))
            fa = add(pick(s1, xb, 1), got)
            b = part[:, :, :, half:]
            got = lax.ppermute(pick(b, 1 - xb, 2), "ctx", xor_perm(n_ctx, 1))
            s2 = add(pick(b, xb, 2), got)
            got = lax.ppermute(pick(s2, 1 - yb, 1), "ctx", xor_perm(n_ctx, 2))
            fb = add(pick(s2, yb, 1), got)
            key_parts += [fa[0], fb[0]]
            value_parts += [fa[1], fb[1]]

        keys = jnp.concatenate(key_parts, axis=0)
        values = jnp.concatenate(value_parts, axis=0)
        key_places = jnp.concatenate(places)
        key_count = keys.shape[0]
        heads = sub // HD
        enc_doc = document_ids(enc_lengths, key_places)
        section_queries = lax.dynamic_slice_in_dim(queries[0], c * sub, sub, axis=1)
        query_count = section_queries.shape[0]
        dec_doc = document_ids(dec_lengths, jnp.arange(query_count, dtype=jnp.int32))
        allowed = dec_doc[:, None] == enc_doc[None, :]
        factor = 1.0 / math.sqrt(HD)
        query_heads = section_queries.reshape(query_count, heads, HD)
        key_heads = keys.reshape(key_count, heads, HD)
        value_heads = values.reshape(key_count, heads, HD)
        scores = (
            jnp.einsum("qhd,khd->hqk", query_heads, key_heads, preferred_element_type=f32)
            * factor
        )
        scores = jnp.where(allowed[None], scores, f32(-1e30))
        top = jnp.max(scores, axis=2, keepdims=True)
        weights = jnp.where(allowed[None], jnp.exp(scores - top), f32(0.0))
        totals = jnp.sum(weights, axis=2)
        numer = jnp.einsum("hqk,khd->qhd", weights.astype(bf16), value_heads, preferred_element_type=f32)
        context = (numer / totals.T[:, :, None]).astype(bf16).reshape(query_count, sub)
        share = query_count // n_ctx
        blocks = context.reshape(n_ctx, share, sub)
        pieces = [pick(blocks, c, 0)]
        for d in range(1, n_ctx):
            pieces.append(lax.ppermute(pick(blocks, (c + d) % n_ctx, 0), "ctx", shift_perm(n_ctx, d)))
        pieces = jnp.stack(pieces)
        order = (c - jnp.arange(n_ctx, dtype=jnp.int32)) % n_ctx
        out = jnp.take(pieces, order, axis=0)
        return jnp.transpose(out, (1, 0, 2)).reshape(1, share, head_width)

    return fast


def solution(mesh):
    in_specs = (
        P(("section", "tp"), "ctx"),
        P(),
        P(),
        P("section", None, "tp"),
        P("section", "ctx", "tp"),
        P("section", "ctx", "tp"),
    )
    out_specs = P("section", "ctx", "tp")
    n_sec, n_ctx, n_tp = mesh.shape["section"], mesh.shape["ctx"], mesh.shape["tp"]
    return jax.shard_map(
        lambda *a: choose(n_sec, n_ctx, n_tp, *a), mesh=mesh, in_specs=in_specs, out_specs=out_specs, check_vma=False
    )


def choose(n_sec, n_ctx, n_tp, enc_out, enc_lengths, dec_lengths, queries, key_weight, value_weight):
    rows = enc_out.shape[0]
    head_width = key_weight.shape[2]
    query_count = queries.shape[1]
    ok = (
        n_ctx == 4
        and head_width % (n_ctx * HD) == 0
        and (n_tp * rows) % 2 == 0
        and query_count % n_ctx == 0
    )
    args = (enc_out, enc_lengths, dec_lengths, queries, key_weight, value_weight)
    if ok:
        return make_fast(n_sec, n_ctx, n_tp)(*args)
    return on_device(*args)
```

```python
import math

import jax
import jax.numpy as jnp
from jax import lax
from jax.sharding import PartitionSpec as P

HD = 64
N_CHUNKS = 1


def document_ids(lengths, places):
    ends = jnp.cumsum(lengths)
    return jnp.sum((places[:, None] >= ends[None, :]).astype(jnp.int32), axis=1)


def on_device(enc_out, enc_lengths, dec_lengths, queries, key_weight, value_weight):
    gathered = lax.all_gather(enc_out, ("section", "tp"), axis=0, tiled=True)
    head_width = key_weight.shape[2]
    heads_here = head_width // HD
    both_weights = jnp.concatenate([key_weight[0], value_weight[0]], axis=1)
    summed = lax.psum_scatter(
        jnp.dot(gathered, both_weights, preferred_element_type=jnp.float32).astype(jnp.bfloat16),
        "ctx",
        scatter_dimension=0,
        tiled=True,
    )
    local_keys = summed[:, :head_width]
    local_values = summed[:, head_width:]
    key_count = local_keys.shape[0]
    key_places = lax.axis_index("ctx") * key_count + jnp.arange(key_count, dtype=jnp.int32)
    enc_doc = document_ids(enc_lengths, key_places)
    section_queries = queries[0]
    query_count = section_queries.shape[0]
    dec_doc = document_ids(dec_lengths, jnp.arange(query_count, dtype=jnp.int32))
    allowed = dec_doc[:, None] == enc_doc[None, :]
    factor = 1.0 / math.sqrt(HD)
    query_heads = section_queries.reshape(query_count, heads_here, HD)
    key_heads = local_keys.reshape(key_count, heads_here, HD)
    value_heads = local_values.reshape(key_count, heads_here, HD)
    scores = (
        jnp.einsum("qhd,khd->hqk", query_heads, key_heads, preferred_element_type=jnp.float32)
        * factor
    )
    scores = jnp.where(allowed[None], scores, jnp.float32(-1e30))
    local_top = jnp.max(scores, axis=2)
    top = lax.pmax(local_top, "ctx")
    weights = jnp.where(allowed[None], jnp.exp(scores - top[:, :, None]), jnp.float32(0.0))
    totals = jnp.sum(weights, axis=2)
    numer = jnp.einsum(
        "hqk,khd->qhd",
        weights.astype(jnp.bfloat16),
        value_heads,
        preferred_element_type=jnp.float32,
    )
    numer = numer.reshape(query_count, head_width)
    numer_share, total_share = (
        lax.psum_scatter(numer.astype(jnp.bfloat16), "ctx", scatter_dimension=0, tiled=True).astype(
            jnp.float32
        ),
        lax.psum_scatter(
            totals.T.astype(jnp.bfloat16), "ctx", scatter_dimension=0, tiled=True
        ).astype(jnp.float32),
    )
    share_rows = numer_share.shape[0]
    result = numer_share.reshape(share_rows, heads_here, HD) / total_share[:, :, None]
    return result.reshape(1, share_rows, head_width).astype(jnp.bfloat16)


def shift_perm(n, d):
    return [(i, (i + d) % n) for i in range(n)]


def xor_perm(n, b):
    return [(i, i ^ b) for i in range(n)]


def make_fast(n_sec, n_ctx, n_tp, n_chunks):
    def fast(enc_out, enc_lengths, dec_lengths, queries, key_weight, value_weight):
        f32, bf16 = jnp.float32, jnp.bfloat16
        s = lax.axis_index("section")
        c = lax.axis_index("ctx")
        t = lax.axis_index("tp")
        rows, feat = enc_out.shape
        head_width = key_weight.shape[2]
        sub = head_width // n_ctx
        cr = rows // n_chunks
        wk = key_weight[0].reshape(feat, n_ctx, sub)
        wv = value_weight[0].reshape(feat, n_ctx, sub)
        yb = c // 2
        xb = c % 2

        def pick(x, i, axis):
            return lax.dynamic_index_in_dim(x, i, axis, keepdims=False)

        def add(a, b):
            return (a.astype(f32) + b.astype(f32)).astype(bf16)

        key_parts, value_parts, places = [], [], []
        for k in range(n_chunks):
            mine = enc_out[k * cr:(k + 1) * cr]
            blocks = [mine]
            for d in range(1, n_tp):
                blocks.append(lax.ppermute(mine, "tp", shift_perm(n_tp, d)))
            tp_stack = jnp.stack(blocks)
            sec_blocks = [tp_stack]
            for d in range(1, n_sec):
                sec_blocks.append(lax.ppermute(tp_stack, "section", shift_perm(n_sec, d)))
            d_sec = jnp.arange(n_sec, dtype=jnp.int32)[:, None, None]
            d_tp = jnp.arange(n_tp, dtype=jnp.int32)[None, :, None]
            r = jnp.arange(cr, dtype=jnp.int32)[None, None, :]
            src = ((s - d_sec) % n_sec) * n_tp + (t - d_tp) % n_tp
            places.append((src * rows + k * cr + r).reshape(-1))
            halves = []
            for blk in sec_blocks:
                e = blk.reshape(n_tp * cr, feat)
                pk = jnp.einsum("tf,fgc->gtc", e, wk, preferred_element_type=f32).astype(bf16)
                pv = jnp.einsum("tf,fgc->gtc", e, wv, preferred_element_type=f32).astype(bf16)
                halves.append((pk.reshape(2, 2, n_tp * cr, sub), pv.reshape(2, 2, n_tp * cr, sub)))
            a_pk, a_pv = halves[0]
            got = lax.ppermute((pick(a_pk, 1 - yb, 0), pick(a_pv, 1 - yb, 0)), "ctx", xor_perm(n_ctx, 2))
            s1k = add(pick(a_pk, yb, 0), got[0])
            s1v = add(pick(a_pv, yb, 0), got[1])
            got = lax.ppermute((pick(s1k, 1 - xb, 0), pick(s1v, 1 - xb, 0)), "ctx", xor_perm(n_ctx, 1))
            fa_k = add(pick(s1k, xb, 0), got[0])
            fa_v = add(pick(s1v, xb, 0), got[1])
            b_pk, b_pv = halves[1]
            got = lax.ppermute((pick(b_pk, 1 - xb, 1), pick(b_pv, 1 - xb, 1)), "ctx", xor_perm(n_ctx, 1))
            s2k = add(pick(b_pk, xb, 1), got[0])
            s2v = add(pick(b_pv, xb, 1), got[1])
            got = lax.ppermute((pick(s2k, 1 - yb, 0), pick(s2v, 1 - yb, 0)), "ctx", xor_perm(n_ctx, 2))
            fb_k = add(pick(s2k, yb, 0), got[0])
            fb_v = add(pick(s2v, yb, 0), got[1])
            key_parts += [fa_k, fb_k]
            value_parts += [fa_v, fb_v]

        keys = jnp.concatenate(key_parts, axis=0)
        values = jnp.concatenate(value_parts, axis=0)
        key_places = jnp.concatenate(places)
        key_count = keys.shape[0]
        heads = sub // HD
        enc_doc = document_ids(enc_lengths, key_places)
        section_queries = lax.dynamic_slice_in_dim(queries[0], c * sub, sub, axis=1)
        query_count = section_queries.shape[0]
        dec_doc = document_ids(dec_lengths, jnp.arange(query_count, dtype=jnp.int32))
        allowed = dec_doc[:, None] == enc_doc[None, :]
        factor = 1.0 / math.sqrt(HD)
        query_heads = section_queries.reshape(query_count, heads, HD)
        key_heads = keys.reshape(key_count, heads, HD)
        value_heads = values.reshape(key_count, heads, HD)
        scores = (
            jnp.einsum("qhd,khd->hqk", query_heads, key_heads, preferred_element_type=f32)
            * factor
        )
        scores = jnp.where(allowed[None], scores, f32(-1e30))
        top = jnp.max(scores, axis=2, keepdims=True)
        weights = jnp.where(allowed[None], jnp.exp(scores - top), f32(0.0))
        totals = jnp.sum(weights, axis=2)
        numer = jnp.einsum("hqk,khd->qhd", weights.astype(bf16), value_heads, preferred_element_type=f32)
        context = (numer / totals.T[:, :, None]).astype(bf16).reshape(query_count, sub)
        share = query_count // n_ctx
        blocks = context.reshape(n_ctx, share, sub)
        pieces = [pick(blocks, c, 0)]
        for d in range(1, n_ctx):
            pieces.append(lax.ppermute(pick(blocks, (c + d) % n_ctx, 0), "ctx", shift_perm(n_ctx, d)))
        pieces = jnp.stack(pieces)
        order = (c - jnp.arange(n_ctx, dtype=jnp.int32)) % n_ctx
        out = jnp.take(pieces, order, axis=0)
        return jnp.transpose(out, (1, 0, 2)).reshape(1, share, head_width)

    return fast


def solution(mesh):
    in_specs = (
        P(("section", "tp"), "ctx"),
        P(),
        P(),
        P("section", None, "tp"),
        P("section", "ctx", "tp"),
        P("section", "ctx", "tp"),
    )
    out_specs = P("section", "ctx", "tp")
    n_sec, n_ctx, n_tp = mesh.shape["section"], mesh.shape["ctx"], mesh.shape["tp"]
    return jax.shard_map(
        lambda *a: choose(n_sec, n_ctx, n_tp, *a), mesh=mesh, in_specs=in_specs, out_specs=out_specs, check_vma=False
    )


def choose(n_sec, n_ctx, n_tp, enc_out, enc_lengths, dec_lengths, queries, key_weight, value_weight):
    rows = enc_out.shape[0]
    head_width = key_weight.shape[2]
    query_count = queries.shape[1]
    ok = (
        n_ctx == 4
        and n_sec == 2
        and head_width % (n_ctx * HD) == 0
        and rows % N_CHUNKS == 0
        and (n_sec * n_tp * (rows // N_CHUNKS)) % 2 == 0
        and query_count % n_ctx == 0
    )
    args = (enc_out, enc_lengths, dec_lengths, queries, key_weight, value_weight)
    if ok:
        return make_fast(n_sec, n_ctx, n_tp, N_CHUNKS)(*args)
    return on_device(*args)
```

```python
import math

import jax
import jax.numpy as jnp
from jax import lax
from jax.sharding import PartitionSpec as P

HD = 64
N_CHUNKS = 1


def document_ids(lengths, places):
    ends = jnp.cumsum(lengths)
    return jnp.sum((places[:, None] >= ends[None, :]).astype(jnp.int32), axis=1)


def on_device(enc_out, enc_lengths, dec_lengths, queries, key_weight, value_weight):
    gathered = lax.all_gather(enc_out, ("section", "tp"), axis=0, tiled=True)
    head_width = key_weight.shape[2]
    heads_here = head_width // HD
    both_weights = jnp.concatenate([key_weight[0], value_weight[0]], axis=1)
    summed = lax.psum_scatter(
        jnp.dot(gathered, both_weights, preferred_element_type=jnp.float32).astype(jnp.bfloat16),
        "ctx",
        scatter_dimension=0,
        tiled=True,
    )
    local_keys = summed[:, :head_width]
    local_values = summed[:, head_width:]
    key_count = local_keys.shape[0]
    key_places = lax.axis_index("ctx") * key_count + jnp.arange(key_count, dtype=jnp.int32)
    enc_doc = document_ids(enc_lengths, key_places)
    section_queries = queries[0]
    query_count = section_queries.shape[0]
    dec_doc = document_ids(dec_lengths, jnp.arange(query_count, dtype=jnp.int32))
    allowed = dec_doc[:, None] == enc_doc[None, :]
    factor = 1.0 / math.sqrt(HD)
    query_heads = section_queries.reshape(query_count, heads_here, HD)
    key_heads = local_keys.reshape(key_count, heads_here, HD)
    value_heads = local_values.reshape(key_count, heads_here, HD)
    scores = (
        jnp.einsum("qhd,khd->hqk", query_heads, key_heads, preferred_element_type=jnp.float32)
        * factor
    )
    scores = jnp.where(allowed[None], scores, jnp.float32(-1e30))
    local_top = jnp.max(scores, axis=2)
    top = lax.pmax(local_top, "ctx")
    weights = jnp.where(allowed[None], jnp.exp(scores - top[:, :, None]), jnp.float32(0.0))
    totals = jnp.sum(weights, axis=2)
    numer = jnp.einsum(
        "hqk,khd->qhd",
        weights.astype(jnp.bfloat16),
        value_heads,
        preferred_element_type=jnp.float32,
    )
    numer = numer.reshape(query_count, head_width)
    numer_share, total_share = (
        lax.psum_scatter(numer.astype(jnp.bfloat16), "ctx", scatter_dimension=0, tiled=True).astype(
            jnp.float32
        ),
        lax.psum_scatter(
            totals.T.astype(jnp.bfloat16), "ctx", scatter_dimension=0, tiled=True
        ).astype(jnp.float32),
    )
    share_rows = numer_share.shape[0]
    result = numer_share.reshape(share_rows, heads_here, HD) / total_share[:, :, None]
    return result.reshape(1, share_rows, head_width).astype(jnp.bfloat16)


def shift_perm(n, d):
    return [(i, (i + d) % n) for i in range(n)]


def xor_perm(n, b):
    return [(i, i ^ b) for i in range(n)]


def make_fast(n_sec, n_ctx, n_tp, n_chunks):
    def fast(enc_out, enc_lengths, dec_lengths, queries, key_weight, value_weight):
        f32, bf16 = jnp.float32, jnp.bfloat16
        s = lax.axis_index("section")
        c = lax.axis_index("ctx")
        t = lax.axis_index("tp")
        rows, feat = enc_out.shape
        head_width = key_weight.shape[2]
        sub = head_width // n_ctx
        cr = rows // n_chunks
        wk = key_weight[0].reshape(feat, n_ctx, sub)
        wv = value_weight[0].reshape(feat, n_ctx, sub)
        yb = c // 2
        xb = c % 2

        def pick(x, i, axis):
            return lax.dynamic_index_in_dim(x, i, axis, keepdims=False)

        def add(a, b):
            return (a.astype(f32) + b.astype(f32)).astype(bf16)

        key_parts, value_parts, places = [], [], []
        for k in range(n_chunks):
            mine = enc_out[k * cr:(k + 1) * cr]
            blocks = [mine]
            for d in range(1, n_tp):
                blocks.append(lax.ppermute(mine, "tp", shift_perm(n_tp, d)))
            tp_stack = jnp.stack(blocks)
            sec_blocks = [tp_stack]
            for d in range(1, n_sec):
                sec_blocks.append(lax.ppermute(tp_stack, "section", shift_perm(n_sec, d)))
            e = jnp.stack(sec_blocks).reshape(n_sec * n_tp * cr, feat)
            d_sec = jnp.arange(n_sec, dtype=jnp.int32)[:, None, None]
            d_tp = jnp.arange(n_tp, dtype=jnp.int32)[None, :, None]
            r = jnp.arange(cr, dtype=jnp.int32)[None, None, :]
            src = ((s - d_sec) % n_sec) * n_tp + (t - d_tp) % n_tp
            places.append((src * rows + k * cr + r).reshape(-1))
            tokens = e.shape[0]
            half = tokens // 2
            pk = jnp.einsum("tf,fgc->gtc", e, wk, preferred_element_type=f32).astype(bf16)
            pv = jnp.einsum("tf,fgc->gtc", e, wv, preferred_element_type=f32).astype(bf16)
            pk = pk.reshape(2, 2, tokens, sub)
            pv = pv.reshape(2, 2, tokens, sub)
            a_pk, a_pv = pk[:, :, :half], pv[:, :, :half]
            got = lax.ppermute((pick(a_pk, 1 - yb, 0), pick(a_pv, 1 - yb, 0)), "ctx", xor_perm(n_ctx, 2))
            s1k = add(pick(a_pk, yb, 0), got[0])
            s1v = add(pick(a_pv, yb, 0), got[1])
            got = lax.ppermute((pick(s1k, 1 - xb, 0), pick(s1v, 1 - xb, 0)), "ctx", xor_perm(n_ctx, 1))
            fa_k = add(pick(s1k, xb, 0), got[0])
            fa_v = add(pick(s1v, xb, 0), got[1])
            b_pk, b_pv = pk[:, :, half:], pv[:, :, half:]
            got = lax.ppermute((pick(b_pk, 1 - xb, 1), pick(b_pv, 1 - xb, 1)), "ctx", xor_perm(n_ctx, 1))
            s2k = add(pick(b_pk, xb, 1), got[0])
            s2v = add(pick(b_pv, xb, 1), got[1])
            got = lax.ppermute((pick(s2k, 1 - yb, 0), pick(s2v, 1 - yb, 0)), "ctx", xor_perm(n_ctx, 2))
            fb_k = add(pick(s2k, yb, 0), got[0])
            fb_v = add(pick(s2v, yb, 0), got[1])
            key_parts += [fa_k, fb_k]
            value_parts += [fa_v, fb_v]

        keys = jnp.concatenate(key_parts, axis=0)
        values = jnp.concatenate(value_parts, axis=0)
        key_places = jnp.concatenate(places)
        key_count = keys.shape[0]
        heads = sub // HD
        enc_doc = document_ids(enc_lengths, key_places)
        section_queries = lax.dynamic_slice_in_dim(queries[0], c * sub, sub, axis=1)
        query_count = section_queries.shape[0]
        share = query_count // n_ctx
        factor = 1.0 / math.sqrt(HD)
        key_heads = keys.reshape(key_count, heads, HD)
        value_heads = values.reshape(key_count, heads, HD)

        def attend(dest):
            first = dest * share
            query_heads = lax.dynamic_slice_in_dim(section_queries, first, share, axis=0).reshape(share, heads, HD)
            dec_doc = document_ids(dec_lengths, first + jnp.arange(share, dtype=jnp.int32))
            allowed = dec_doc[:, None] == enc_doc[None, :]
            scores = (
                jnp.einsum("qhd,khd->hqk", query_heads, key_heads, preferred_element_type=f32)
                * factor
            )
            scores = jnp.where(allowed[None], scores, f32(-1e30))
            top = jnp.max(scores, axis=2, keepdims=True)
            weights = jnp.where(allowed[None], jnp.exp(scores - top), f32(0.0))
            totals = jnp.sum(weights, axis=2)
            numer = jnp.einsum("hqk,khd->qhd", weights.astype(bf16), value_heads, preferred_element_type=f32)
            return (numer / totals.T[:, :, None]).astype(bf16).reshape(share, sub)

        pieces = [None] * n_ctx
        for d in range(1, n_ctx):
            pieces[d] = lax.ppermute(attend((c + d) % n_ctx), "ctx", shift_perm(n_ctx, d))
        pieces[0] = attend(c)
        pieces = jnp.stack(pieces)
        order = (c - jnp.arange(n_ctx, dtype=jnp.int32)) % n_ctx
        out = jnp.take(pieces, order, axis=0)
        return jnp.transpose(out, (1, 0, 2)).reshape(1, share, head_width)

    return fast


def solution(mesh):
    in_specs = (
        P(("section", "tp"), "ctx"),
        P(),
        P(),
        P("section", None, "tp"),
        P("section", "ctx", "tp"),
        P("section", "ctx", "tp"),
    )
    out_specs = P("section", "ctx", "tp")
    n_sec, n_ctx, n_tp = mesh.shape["section"], mesh.shape["ctx"], mesh.shape["tp"]
    return jax.shard_map(
        lambda *a: choose(n_sec, n_ctx, n_tp, *a), mesh=mesh, in_specs=in_specs, out_specs=out_specs, check_vma=False
    )


def choose(n_sec, n_ctx, n_tp, enc_out, enc_lengths, dec_lengths, queries, key_weight, value_weight):
    rows = enc_out.shape[0]
    head_width = key_weight.shape[2]
    query_count = queries.shape[1]
    ok = (
        n_ctx == 4
        and head_width % (n_ctx * HD) == 0
        and rows % N_CHUNKS == 0
        and (n_sec * n_tp * (rows // N_CHUNKS)) % 2 == 0
        and query_count % n_ctx == 0
    )
    args = (enc_out, enc_lengths, dec_lengths, queries, key_weight, value_weight)
    if ok:
        return make_fast(n_sec, n_ctx, n_tp, N_CHUNKS)(*args)
    return on_device(*args)
```

```python
import math

import jax
import jax.numpy as jnp
from jax import lax
from jax.sharding import PartitionSpec as P

HD = 64
N_CHUNKS = 1


def document_ids(lengths, places):
    ends = jnp.cumsum(lengths)
    return jnp.sum((places[:, None] >= ends[None, :]).astype(jnp.int32), axis=1)


def on_device(enc_out, enc_lengths, dec_lengths, queries, key_weight, value_weight):
    gathered = lax.all_gather(enc_out, ("section", "tp"), axis=0, tiled=True)
    head_width = key_weight.shape[2]
    heads_here = head_width // HD
    both_weights = jnp.concatenate([key_weight[0], value_weight[0]], axis=1)
    summed = lax.psum_scatter(
        jnp.dot(gathered, both_weights, preferred_element_type=jnp.float32).astype(jnp.bfloat16),
        "ctx",
        scatter_dimension=0,
        tiled=True,
    )
    local_keys = summed[:, :head_width]
    local_values = summed[:, head_width:]
    key_count = local_keys.shape[0]
    key_places = lax.axis_index("ctx") * key_count + jnp.arange(key_count, dtype=jnp.int32)
    enc_doc = document_ids(enc_lengths, key_places)
    section_queries = queries[0]
    query_count = section_queries.shape[0]
    dec_doc = document_ids(dec_lengths, jnp.arange(query_count, dtype=jnp.int32))
    allowed = dec_doc[:, None] == enc_doc[None, :]
    factor = 1.0 / math.sqrt(HD)
    query_heads = section_queries.reshape(query_count, heads_here, HD)
    key_heads = local_keys.reshape(key_count, heads_here, HD)
    value_heads = local_values.reshape(key_count, heads_here, HD)
    scores = (
        jnp.einsum("qhd,khd->hqk", query_heads, key_heads, preferred_element_type=jnp.float32)
        * factor
    )
    scores = jnp.where(allowed[None], scores, jnp.float32(-1e30))
    local_top = jnp.max(scores, axis=2)
    top = lax.pmax(local_top, "ctx")
    weights = jnp.where(allowed[None], jnp.exp(scores - top[:, :, None]), jnp.float32(0.0))
    totals = jnp.sum(weights, axis=2)
    numer = jnp.einsum(
        "hqk,khd->qhd",
        weights.astype(jnp.bfloat16),
        value_heads,
        preferred_element_type=jnp.float32,
    )
    numer = numer.reshape(query_count, head_width)
    numer_share, total_share = (
        lax.psum_scatter(numer.astype(jnp.bfloat16), "ctx", scatter_dimension=0, tiled=True).astype(
            jnp.float32
        ),
        lax.psum_scatter(
            totals.T.astype(jnp.bfloat16), "ctx", scatter_dimension=0, tiled=True
        ).astype(jnp.float32),
    )
    share_rows = numer_share.shape[0]
    result = numer_share.reshape(share_rows, heads_here, HD) / total_share[:, :, None]
    return result.reshape(1, share_rows, head_width).astype(jnp.bfloat16)


def shift_perm(n, d):
    return [(i, (i + d) % n) for i in range(n)]


def xor_perm(n, b):
    return [(i, i ^ b) for i in range(n)]


def make_fast(n_sec, n_ctx, n_tp, n_chunks):
    def fast(enc_out, enc_lengths, dec_lengths, queries, key_weight, value_weight):
        f32, bf16 = jnp.float32, jnp.bfloat16
        s = lax.axis_index("section")
        c = lax.axis_index("ctx")
        t = lax.axis_index("tp")
        rows, feat = enc_out.shape
        head_width = key_weight.shape[2]
        sub = head_width // n_ctx
        cr = rows // n_chunks
        wk = key_weight[0].reshape(feat, n_ctx, sub)
        wv = value_weight[0].reshape(feat, n_ctx, sub)
        yb = c // 2
        xb = c % 2

        def pick(x, i, axis):
            return lax.dynamic_index_in_dim(x, i, axis, keepdims=False)

        def add(a, b):
            return (a.astype(f32) + b.astype(f32)).astype(bf16)

        key_parts, value_parts, places = [], [], []
        for k in range(n_chunks):
            mine = enc_out[k * cr:(k + 1) * cr]
            blocks = [mine]
            for d in range(1, n_tp):
                blocks.append(lax.ppermute(mine, "tp", shift_perm(n_tp, d)))
            tp_stack = jnp.stack(blocks)
            sec_blocks = [tp_stack]
            for d in range(1, n_sec):
                sec_blocks.append(lax.ppermute(tp_stack, "section", shift_perm(n_sec, d)))
            d_sec = jnp.arange(n_sec, dtype=jnp.int32)[:, None, None]
            d_tp = jnp.arange(n_tp, dtype=jnp.int32)[None, :, None]
            r = jnp.arange(cr, dtype=jnp.int32)[None, None, :]
            src = ((s - d_sec) % n_sec) * n_tp + (t - d_tp) % n_tp
            places.append((src * rows + k * cr + r).reshape(-1))
            halves = []
            for blk in sec_blocks:
                e = blk.reshape(n_tp * cr, feat)
                pk = jnp.einsum("tf,fgc->gtc", e, wk, preferred_element_type=f32).astype(bf16)
                pv = jnp.einsum("tf,fgc->gtc", e, wv, preferred_element_type=f32).astype(bf16)
                halves.append((pk.reshape(2, 2, n_tp * cr, sub), pv.reshape(2, 2, n_tp * cr, sub)))
            a_pk, a_pv = halves[0]
            send_k, send_v = pick(a_pk, 1 - yb, 0), pick(a_pv, 1 - yb, 0)
            send_k, send_v, _ = lax.optimization_barrier((send_k, send_v, sec_blocks[1]))
            got = lax.ppermute((send_k, send_v), "ctx", xor_perm(n_ctx, 2))
            s1k = add(pick(a_pk, yb, 0), got[0])
            s1v = add(pick(a_pv, yb, 0), got[1])
            got = lax.ppermute((pick(s1k, 1 - xb, 0), pick(s1v, 1 - xb, 0)), "ctx", xor_perm(n_ctx, 1))
            fa_k = add(pick(s1k, xb, 0), got[0])
            fa_v = add(pick(s1v, xb, 0), got[1])
            b_pk, b_pv = halves[1]
            got = lax.ppermute((pick(b_pk, 1 - xb, 1), pick(b_pv, 1 - xb, 1)), "ctx", xor_perm(n_ctx, 1))
            s2k = add(pick(b_pk, xb, 1), got[0])
            s2v = add(pick(b_pv, xb, 1), got[1])
            got = lax.ppermute((pick(s2k, 1 - yb, 0), pick(s2v, 1 - yb, 0)), "ctx", xor_perm(n_ctx, 2))
            fb_k = add(pick(s2k, yb, 0), got[0])
            fb_v = add(pick(s2v, yb, 0), got[1])
            key_parts += [fa_k, fb_k]
            value_parts += [fa_v, fb_v]

        keys = jnp.concatenate(key_parts, axis=0)
        values = jnp.concatenate(value_parts, axis=0)
        key_places = jnp.concatenate(places)
        key_count = keys.shape[0]
        heads = sub // HD
        enc_doc = document_ids(enc_lengths, key_places)
        section_queries = lax.dynamic_slice_in_dim(queries[0], c * sub, sub, axis=1)
        query_count = section_queries.shape[0]
        dec_doc = document_ids(dec_lengths, jnp.arange(query_count, dtype=jnp.int32))
        allowed = dec_doc[:, None] == enc_doc[None, :]
        factor = 1.0 / math.sqrt(HD)
        query_heads = section_queries.reshape(query_count, heads, HD)
        key_heads = keys.reshape(key_count, heads, HD)
        value_heads = values.reshape(key_count, heads, HD)
        scores = (
            jnp.einsum("qhd,khd->hqk", query_heads, key_heads, preferred_element_type=f32)
            * factor
        )
        scores = jnp.where(allowed[None], scores, f32(-1e30))
        top = jnp.max(scores, axis=2, keepdims=True)
        weights = jnp.where(allowed[None], jnp.exp(scores - top), f32(0.0))
        totals = jnp.sum(weights, axis=2)
        numer = jnp.einsum("hqk,khd->qhd", weights.astype(bf16), value_heads, preferred_element_type=f32)
        context = (numer / totals.T[:, :, None]).astype(bf16).reshape(query_count, sub)
        share = query_count // n_ctx
        blocks = context.reshape(n_ctx, share, sub)
        pieces = [pick(blocks, c, 0)]
        for d in range(1, n_ctx):
            pieces.append(lax.ppermute(pick(blocks, (c + d) % n_ctx, 0), "ctx", shift_perm(n_ctx, d)))
        pieces = jnp.stack(pieces)
        order = (c - jnp.arange(n_ctx, dtype=jnp.int32)) % n_ctx
        out = jnp.take(pieces, order, axis=0)
        return jnp.transpose(out, (1, 0, 2)).reshape(1, share, head_width)

    return fast


def solution(mesh):
    in_specs = (
        P(("section", "tp"), "ctx"),
        P(),
        P(),
        P("section", None, "tp"),
        P("section", "ctx", "tp"),
        P("section", "ctx", "tp"),
    )
    out_specs = P("section", "ctx", "tp")
    n_sec, n_ctx, n_tp = mesh.shape["section"], mesh.shape["ctx"], mesh.shape["tp"]
    return jax.shard_map(
        lambda *a: choose(n_sec, n_ctx, n_tp, *a), mesh=mesh, in_specs=in_specs, out_specs=out_specs, check_vma=False
    )


def choose(n_sec, n_ctx, n_tp, enc_out, enc_lengths, dec_lengths, queries, key_weight, value_weight):
    rows = enc_out.shape[0]
    head_width = key_weight.shape[2]
    query_count = queries.shape[1]
    ok = (
        n_ctx == 4
        and n_sec == 2
        and head_width % (n_ctx * HD) == 0
        and rows % N_CHUNKS == 0
        and (n_sec * n_tp * (rows // N_CHUNKS)) % 2 == 0
        and query_count % n_ctx == 0
    )
    args = (enc_out, enc_lengths, dec_lengths, queries, key_weight, value_weight)
    if ok:
        return make_fast(n_sec, n_ctx, n_tp, N_CHUNKS)(*args)
    return on_device(*args)
```

```python
import math

import jax
import jax.numpy as jnp
from jax import lax
from jax.sharding import PartitionSpec as P

HD = 64
N_CHUNKS = 1


def document_ids(lengths, places):
    ends = jnp.cumsum(lengths)
    return jnp.sum((places[:, None] >= ends[None, :]).astype(jnp.int32), axis=1)


def on_device(enc_out, enc_lengths, dec_lengths, queries, key_weight, value_weight):
    gathered = lax.all_gather(enc_out, ("section", "tp"), axis=0, tiled=True)
    head_width = key_weight.shape[2]
    heads_here = head_width // HD
    both_weights = jnp.concatenate([key_weight[0], value_weight[0]], axis=1)
    summed = lax.psum_scatter(
        jnp.dot(gathered, both_weights, preferred_element_type=jnp.float32).astype(jnp.bfloat16),
        "ctx",
        scatter_dimension=0,
        tiled=True,
    )
    local_keys = summed[:, :head_width]
    local_values = summed[:, head_width:]
    key_count = local_keys.shape[0]
    key_places = lax.axis_index("ctx") * key_count + jnp.arange(key_count, dtype=jnp.int32)
    enc_doc = document_ids(enc_lengths, key_places)
    section_queries = queries[0]
    query_count = section_queries.shape[0]
    dec_doc = document_ids(dec_lengths, jnp.arange(query_count, dtype=jnp.int32))
    allowed = dec_doc[:, None] == enc_doc[None, :]
    factor = 1.0 / math.sqrt(HD)
    query_heads = section_queries.reshape(query_count, heads_here, HD)
    key_heads = local_keys.reshape(key_count, heads_here, HD)
    value_heads = local_values.reshape(key_count, heads_here, HD)
    scores = (
        jnp.einsum("qhd,khd->hqk", query_heads, key_heads, preferred_element_type=jnp.float32)
        * factor
    )
    scores = jnp.where(allowed[None], scores, jnp.float32(-1e30))
    local_top = jnp.max(scores, axis=2)
    top = lax.pmax(local_top, "ctx")
    weights = jnp.where(allowed[None], jnp.exp(scores - top[:, :, None]), jnp.float32(0.0))
    totals = jnp.sum(weights, axis=2)
    numer = jnp.einsum(
        "hqk,khd->qhd",
        weights.astype(jnp.bfloat16),
        value_heads,
        preferred_element_type=jnp.float32,
    )
    numer = numer.reshape(query_count, head_width)
    numer_share, total_share = (
        lax.psum_scatter(numer.astype(jnp.bfloat16), "ctx", scatter_dimension=0, tiled=True).astype(
            jnp.float32
        ),
        lax.psum_scatter(
            totals.T.astype(jnp.bfloat16), "ctx", scatter_dimension=0, tiled=True
        ).astype(jnp.float32),
    )
    share_rows = numer_share.shape[0]
    result = numer_share.reshape(share_rows, heads_here, HD) / total_share[:, :, None]
    return result.reshape(1, share_rows, head_width).astype(jnp.bfloat16)


def shift_perm(n, d):
    return [(i, (i + d) % n) for i in range(n)]


def xor_perm(n, b):
    return [(i, i ^ b) for i in range(n)]


def make_fast(n_sec, n_ctx, n_tp, n_chunks):
    def fast(enc_out, enc_lengths, dec_lengths, queries, key_weight, value_weight):
        f32, bf16 = jnp.float32, jnp.bfloat16
        s = lax.axis_index("section")
        c = lax.axis_index("ctx")
        t = lax.axis_index("tp")
        rows, feat = enc_out.shape
        head_width = key_weight.shape[2]
        sub = head_width // n_ctx
        cr = rows // n_chunks
        wk = key_weight[0].reshape(feat, n_ctx, sub)
        wv = value_weight[0].reshape(feat, n_ctx, sub)
        yb = c // 2
        xb = c % 2

        def pick(x, i, axis):
            return lax.dynamic_index_in_dim(x, i, axis, keepdims=False)

        def add(a, b):
            return (a.astype(f32) + b.astype(f32)).astype(bf16)

        key_parts, value_parts, places = [], [], []
        for k in range(n_chunks):
            mine = enc_out[k * cr:(k + 1) * cr]
            own_moved = [lax.ppermute(mine, "section", shift_perm(n_sec, d)) for d in range(1, n_sec)]
            received = jnp.stack([lax.ppermute(mine, "tp", shift_perm(n_tp, d)) for d in range(1, n_tp)])
            pieces = [mine[None], received]
            for d in range(1, n_sec):
                pieces += [own_moved[d - 1][None], lax.ppermute(received, "section", shift_perm(n_sec, d))]
            e = jnp.concatenate(pieces, axis=0).reshape(n_sec * n_tp * cr, feat)
            d_sec = jnp.arange(n_sec, dtype=jnp.int32)[:, None, None]
            d_tp = jnp.arange(n_tp, dtype=jnp.int32)[None, :, None]
            r = jnp.arange(cr, dtype=jnp.int32)[None, None, :]
            src = ((s - d_sec) % n_sec) * n_tp + (t - d_tp) % n_tp
            places.append((src * rows + k * cr + r).reshape(-1))
            tokens = e.shape[0]
            half = tokens // 2
            pk = jnp.einsum("tf,fgc->gtc", e, wk, preferred_element_type=f32).astype(bf16)
            pv = jnp.einsum("tf,fgc->gtc", e, wv, preferred_element_type=f32).astype(bf16)
            pk = pk.reshape(2, 2, tokens, sub)
            pv = pv.reshape(2, 2, tokens, sub)
            a_pk, a_pv = pk[:, :, :half], pv[:, :, :half]
            got = lax.ppermute((pick(a_pk, 1 - yb, 0), pick(a_pv, 1 - yb, 0)), "ctx", xor_perm(n_ctx, 2))
            s1k = add(pick(a_pk, yb, 0), got[0])
            s1v = add(pick(a_pv, yb, 0), got[1])
            got = lax.ppermute((pick(s1k, 1 - xb, 0), pick(s1v, 1 - xb, 0)), "ctx", xor_perm(n_ctx, 1))
            fa_k = add(pick(s1k, xb, 0), got[0])
            fa_v = add(pick(s1v, xb, 0), got[1])
            b_pk, b_pv = pk[:, :, half:], pv[:, :, half:]
            got = lax.ppermute((pick(b_pk, 1 - xb, 1), pick(b_pv, 1 - xb, 1)), "ctx", xor_perm(n_ctx, 1))
            s2k = add(pick(b_pk, xb, 1), got[0])
            s2v = add(pick(b_pv, xb, 1), got[1])
            got = lax.ppermute((pick(s2k, 1 - yb, 0), pick(s2v, 1 - yb, 0)), "ctx", xor_perm(n_ctx, 2))
            fb_k = add(pick(s2k, yb, 0), got[0])
            fb_v = add(pick(s2v, yb, 0), got[1])
            key_parts += [fa_k, fb_k]
            value_parts += [fa_v, fb_v]

        keys = jnp.concatenate(key_parts, axis=0)
        values = jnp.concatenate(value_parts, axis=0)
        key_places = jnp.concatenate(places)
        key_count = keys.shape[0]
        heads = sub // HD
        enc_doc = document_ids(enc_lengths, key_places)
        section_queries = lax.dynamic_slice_in_dim(queries[0], c * sub, sub, axis=1)
        query_count = section_queries.shape[0]
        dec_doc = document_ids(dec_lengths, jnp.arange(query_count, dtype=jnp.int32))
        allowed = dec_doc[:, None] == enc_doc[None, :]
        factor = 1.0 / math.sqrt(HD)
        query_heads = section_queries.reshape(query_count, heads, HD)
        key_heads = keys.reshape(key_count, heads, HD)
        value_heads = values.reshape(key_count, heads, HD)
        scores = (
            jnp.einsum("qhd,khd->hqk", query_heads, key_heads, preferred_element_type=f32)
            * factor
        )
        scores = jnp.where(allowed[None], scores, f32(-1e30))
        top = jnp.max(scores, axis=2, keepdims=True)
        weights = jnp.where(allowed[None], jnp.exp(scores - top), f32(0.0))
        totals = jnp.sum(weights, axis=2)
        numer = jnp.einsum("hqk,khd->qhd", weights.astype(bf16), value_heads, preferred_element_type=f32)
        context = (numer / totals.T[:, :, None]).astype(bf16).reshape(query_count, sub)
        share = query_count // n_ctx
        blocks = context.reshape(n_ctx, share, sub)
        pieces = [pick(blocks, c, 0)]
        for d in range(1, n_ctx):
            pieces.append(lax.ppermute(pick(blocks, (c + d) % n_ctx, 0), "ctx", shift_perm(n_ctx, d)))
        pieces = jnp.stack(pieces)
        order = (c - jnp.arange(n_ctx, dtype=jnp.int32)) % n_ctx
        out = jnp.take(pieces, order, axis=0)
        return jnp.transpose(out, (1, 0, 2)).reshape(1, share, head_width)

    return fast


def solution(mesh):
    in_specs = (
        P(("section", "tp"), "ctx"),
        P(),
        P(),
        P("section", None, "tp"),
        P("section", "ctx", "tp"),
        P("section", "ctx", "tp"),
    )
    out_specs = P("section", "ctx", "tp")
    n_sec, n_ctx, n_tp = mesh.shape["section"], mesh.shape["ctx"], mesh.shape["tp"]
    return jax.shard_map(
        lambda *a: choose(n_sec, n_ctx, n_tp, *a), mesh=mesh, in_specs=in_specs, out_specs=out_specs, check_vma=False
    )


def choose(n_sec, n_ctx, n_tp, enc_out, enc_lengths, dec_lengths, queries, key_weight, value_weight):
    rows = enc_out.shape[0]
    head_width = key_weight.shape[2]
    query_count = queries.shape[1]
    ok = (
        n_ctx == 4
        and head_width % (n_ctx * HD) == 0
        and rows % N_CHUNKS == 0
        and (n_sec * n_tp * (rows // N_CHUNKS)) % 2 == 0
        and query_count % n_ctx == 0
    )
    args = (enc_out, enc_lengths, dec_lengths, queries, key_weight, value_weight)
    if ok:
        return make_fast(n_sec, n_ctx, n_tp, N_CHUNKS)(*args)
    return on_device(*args)
```

```python
import math

import jax
import jax.numpy as jnp
from jax import lax
from jax.sharding import PartitionSpec as P

HD = 64
N_CHUNKS = 1


def document_ids(lengths, places):
    ends = jnp.cumsum(lengths)
    return jnp.sum((places[:, None] >= ends[None, :]).astype(jnp.int32), axis=1)


def on_device(enc_out, enc_lengths, dec_lengths, queries, key_weight, value_weight):
    gathered = lax.all_gather(enc_out, ("section", "tp"), axis=0, tiled=True)
    head_width = key_weight.shape[2]
    heads_here = head_width // HD
    both_weights = jnp.concatenate([key_weight[0], value_weight[0]], axis=1)
    summed = lax.psum_scatter(
        jnp.dot(gathered, both_weights, preferred_element_type=jnp.float32).astype(jnp.bfloat16),
        "ctx",
        scatter_dimension=0,
        tiled=True,
    )
    local_keys = summed[:, :head_width]
    local_values = summed[:, head_width:]
    key_count = local_keys.shape[0]
    key_places = lax.axis_index("ctx") * key_count + jnp.arange(key_count, dtype=jnp.int32)
    enc_doc = document_ids(enc_lengths, key_places)
    section_queries = queries[0]
    query_count = section_queries.shape[0]
    dec_doc = document_ids(dec_lengths, jnp.arange(query_count, dtype=jnp.int32))
    allowed = dec_doc[:, None] == enc_doc[None, :]
    factor = 1.0 / math.sqrt(HD)
    query_heads = section_queries.reshape(query_count, heads_here, HD)
    key_heads = local_keys.reshape(key_count, heads_here, HD)
    value_heads = local_values.reshape(key_count, heads_here, HD)
    scores = (
        jnp.einsum("qhd,khd->hqk", query_heads, key_heads, preferred_element_type=jnp.float32)
        * factor
    )
    scores = jnp.where(allowed[None], scores, jnp.float32(-1e30))
    local_top = jnp.max(scores, axis=2)
    top = lax.pmax(local_top, "ctx")
    weights = jnp.where(allowed[None], jnp.exp(scores - top[:, :, None]), jnp.float32(0.0))
    totals = jnp.sum(weights, axis=2)
    numer = jnp.einsum(
        "hqk,khd->qhd",
        weights.astype(jnp.bfloat16),
        value_heads,
        preferred_element_type=jnp.float32,
    )
    numer = numer.reshape(query_count, head_width)
    numer_share, total_share = (
        lax.psum_scatter(numer.astype(jnp.bfloat16), "ctx", scatter_dimension=0, tiled=True).astype(
            jnp.float32
        ),
        lax.psum_scatter(
            totals.T.astype(jnp.bfloat16), "ctx", scatter_dimension=0, tiled=True
        ).astype(jnp.float32),
    )
    share_rows = numer_share.shape[0]
    result = numer_share.reshape(share_rows, heads_here, HD) / total_share[:, :, None]
    return result.reshape(1, share_rows, head_width).astype(jnp.bfloat16)


def shift_perm(n, d):
    return [(i, (i + d) % n) for i in range(n)]


def xor_perm(n, b):
    return [(i, i ^ b) for i in range(n)]


def make_fast(n_sec, n_ctx, n_tp, n_chunks):
    def fast(enc_out, enc_lengths, dec_lengths, queries, key_weight, value_weight):
        f32, bf16 = jnp.float32, jnp.bfloat16
        s = lax.axis_index("section")
        c = lax.axis_index("ctx")
        t = lax.axis_index("tp")
        rows, feat = enc_out.shape
        head_width = key_weight.shape[2]
        sub = head_width // n_ctx
        cr = rows // n_chunks
        wk = key_weight[0].reshape(feat, n_ctx, sub)
        wv = value_weight[0].reshape(feat, n_ctx, sub)
        yb = c // 2
        xb = c % 2

        def pick(x, i, axis):
            return lax.dynamic_index_in_dim(x, i, axis, keepdims=False)

        def add(a, b):
            return (a.astype(f32) + b.astype(f32)).astype(bf16)

        key_parts, value_parts, places = [], [], []
        for k in range(n_chunks):
            mine = enc_out[k * cr:(k + 1) * cr]
            own_moved = [lax.ppermute(mine, "section", shift_perm(n_sec, d)) for d in range(1, n_sec)]
            received = jnp.stack([lax.ppermute(mine, "tp", shift_perm(n_tp, d)) for d in range(1, n_tp)])
            pieces = [mine[None], received]
            for d in range(1, n_sec):
                pieces += [own_moved[d - 1][None], lax.ppermute(received, "section", shift_perm(n_sec, d))]
            e = jnp.concatenate(pieces, axis=0).reshape(n_sec * n_tp * cr, feat)
            d_sec = jnp.arange(n_sec, dtype=jnp.int32)[:, None, None]
            d_tp = jnp.arange(n_tp, dtype=jnp.int32)[None, :, None]
            r = jnp.arange(cr, dtype=jnp.int32)[None, None, :]
            src = ((s - d_sec) % n_sec) * n_tp + (t - d_tp) % n_tp
            places.append((src * rows + k * cr + r).reshape(-1))
            tokens = e.shape[0]
            half = tokens // 2
            pk = jnp.einsum("tf,fgc->gtc", e, wk, preferred_element_type=f32).astype(bf16)
            pv = jnp.einsum("tf,fgc->gtc", e, wv, preferred_element_type=f32).astype(bf16)
            pk = pk.reshape(2, 2, tokens, sub)
            pv = pv.reshape(2, 2, tokens, sub)
            a_pk, a_pv = pk[:, :, :half], pv[:, :, :half]
            got = lax.ppermute((pick(a_pk, 1 - yb, 0), pick(a_pv, 1 - yb, 0)), "ctx", xor_perm(n_ctx, 2))
            s1k = add(pick(a_pk, yb, 0), got[0])
            s1v = add(pick(a_pv, yb, 0), got[1])
            got = lax.ppermute((pick(s1k, 1 - xb, 0), pick(s1v, 1 - xb, 0)), "ctx", xor_perm(n_ctx, 1))
            fa_k = add(pick(s1k, xb, 0), got[0])
            fa_v = add(pick(s1v, xb, 0), got[1])
            b_pk, b_pv = pk[:, :, half:], pv[:, :, half:]
            got = lax.ppermute((pick(b_pk, 1 - xb, 1), pick(b_pv, 1 - xb, 1)), "ctx", xor_perm(n_ctx, 1))
            s2k = add(pick(b_pk, xb, 1), got[0])
            s2v = add(pick(b_pv, xb, 1), got[1])
            got = lax.ppermute((pick(s2k, 1 - yb, 0), pick(s2v, 1 - yb, 0)), "ctx", xor_perm(n_ctx, 2))
            fb_k = add(pick(s2k, yb, 0), got[0])
            fb_v = add(pick(s2v, yb, 0), got[1])
            key_parts += [fa_k, fb_k]
            value_parts += [fa_v, fb_v]

        keys = jnp.concatenate(key_parts, axis=0)
        values = jnp.concatenate(value_parts, axis=0)
        key_places = jnp.concatenate(places)
        key_count = keys.shape[0]
        heads = sub // HD
        enc_doc = document_ids(enc_lengths, key_places)
        section_queries = lax.dynamic_slice_in_dim(queries[0], c * sub, sub, axis=1)
        query_count = section_queries.shape[0]
        dec_doc = document_ids(dec_lengths, jnp.arange(query_count, dtype=jnp.int32))
        allowed = dec_doc[:, None] == enc_doc[None, :]
        factor = 1.0 / math.sqrt(HD)
        query_heads = section_queries.reshape(query_count, heads, HD)
        key_heads = keys.reshape(key_count, heads, HD)
        value_heads = values.reshape(key_count, heads, HD)
        scores = (
            jnp.einsum("qhd,khd->hqk", query_heads, key_heads, preferred_element_type=f32)
            * factor
        )
        scores = jnp.where(allowed[None], scores, f32(-1e30))
        top = jnp.max(scores, axis=2, keepdims=True)
        weights = jnp.where(allowed[None], jnp.exp(scores - top), f32(0.0))
        totals = jnp.sum(weights, axis=2)
        numer = jnp.einsum("hqk,khd->qhd", weights.astype(bf16), value_heads, preferred_element_type=f32)
        context = (numer / totals.T[:, :, None]).astype(bf16).reshape(query_count, sub)
        share = query_count // n_ctx
        blocks = context.reshape(n_ctx, share, sub)
        pieces = [pick(blocks, c, 0)]
        for d in range(1, n_ctx):
            pieces.append(lax.ppermute(pick(blocks, (c + d) % n_ctx, 0), "ctx", shift_perm(n_ctx, d)))
        groups = []
        for g in range(n_ctx):
            val = pieces[0]
            for d in range(1, n_ctx):
                val = jnp.where((c - d) % n_ctx == g, pieces[d], val)
            groups.append(val)
        return jnp.concatenate(groups, axis=1).reshape(1, share, head_width)

    return fast


def solution(mesh):
    in_specs = (
        P(("section", "tp"), "ctx"),
        P(),
        P(),
        P("section", None, "tp"),
        P("section", "ctx", "tp"),
        P("section", "ctx", "tp"),
    )
    out_specs = P("section", "ctx", "tp")
    n_sec, n_ctx, n_tp = mesh.shape["section"], mesh.shape["ctx"], mesh.shape["tp"]
    return jax.shard_map(
        lambda *a: choose(n_sec, n_ctx, n_tp, *a), mesh=mesh, in_specs=in_specs, out_specs=out_specs, check_vma=False
    )


def choose(n_sec, n_ctx, n_tp, enc_out, enc_lengths, dec_lengths, queries, key_weight, value_weight):
    rows = enc_out.shape[0]
    head_width = key_weight.shape[2]
    query_count = queries.shape[1]
    ok = (
        n_ctx == 4
        and head_width % (n_ctx * HD) == 0
        and rows % N_CHUNKS == 0
        and (n_sec * n_tp * (rows // N_CHUNKS)) % 2 == 0
        and query_count % n_ctx == 0
    )
    args = (enc_out, enc_lengths, dec_lengths, queries, key_weight, value_weight)
    if ok:
        return make_fast(n_sec, n_ctx, n_tp, N_CHUNKS)(*args)
    return on_device(*args)
```

```python
import math

import jax
import jax.numpy as jnp
from jax import lax
from jax.sharding import PartitionSpec as P

HD = 64
N_CHUNKS = 1


def document_ids(lengths, places):
    ends = jnp.cumsum(lengths)
    return jnp.sum((places[:, None] >= ends[None, :]).astype(jnp.int32), axis=1)


def on_device(enc_out, enc_lengths, dec_lengths, queries, key_weight, value_weight):
    gathered = lax.all_gather(enc_out, ("section", "tp"), axis=0, tiled=True)
    head_width = key_weight.shape[2]
    heads_here = head_width // HD
    both_weights = jnp.concatenate([key_weight[0], value_weight[0]], axis=1)
    summed = lax.psum_scatter(
        jnp.dot(gathered, both_weights, preferred_element_type=jnp.float32).astype(jnp.bfloat16),
        "ctx",
        scatter_dimension=0,
        tiled=True,
    )
    local_keys = summed[:, :head_width]
    local_values = summed[:, head_width:]
    key_count = local_keys.shape[0]
    key_places = lax.axis_index("ctx") * key_count + jnp.arange(key_count, dtype=jnp.int32)
    enc_doc = document_ids(enc_lengths, key_places)
    section_queries = queries[0]
    query_count = section_queries.shape[0]
    dec_doc = document_ids(dec_lengths, jnp.arange(query_count, dtype=jnp.int32))
    allowed = dec_doc[:, None] == enc_doc[None, :]
    factor = 1.0 / math.sqrt(HD)
    query_heads = section_queries.reshape(query_count, heads_here, HD)
    key_heads = local_keys.reshape(key_count, heads_here, HD)
    value_heads = local_values.reshape(key_count, heads_here, HD)
    scores = (
        jnp.einsum("qhd,khd->hqk", query_heads, key_heads, preferred_element_type=jnp.float32)
        * factor
    )
    scores = jnp.where(allowed[None], scores, jnp.float32(-1e30))
    local_top = jnp.max(scores, axis=2)
    top = lax.pmax(local_top, "ctx")
    weights = jnp.where(allowed[None], jnp.exp(scores - top[:, :, None]), jnp.float32(0.0))
    totals = jnp.sum(weights, axis=2)
    numer = jnp.einsum(
        "hqk,khd->qhd",
        weights.astype(jnp.bfloat16),
        value_heads,
        preferred_element_type=jnp.float32,
    )
    numer = numer.reshape(query_count, head_width)
    numer_share, total_share = (
        lax.psum_scatter(numer.astype(jnp.bfloat16), "ctx", scatter_dimension=0, tiled=True).astype(
            jnp.float32
        ),
        lax.psum_scatter(
            totals.T.astype(jnp.bfloat16), "ctx", scatter_dimension=0, tiled=True
        ).astype(jnp.float32),
    )
    share_rows = numer_share.shape[0]
    result = numer_share.reshape(share_rows, heads_here, HD) / total_share[:, :, None]
    return result.reshape(1, share_rows, head_width).astype(jnp.bfloat16)


def shift_perm(n, d):
    return [(i, (i + d) % n) for i in range(n)]


def xor_perm(n, b):
    return [(i, i ^ b) for i in range(n)]


def make_fast(n_sec, n_ctx, n_tp, n_chunks):
    def fast(enc_out, enc_lengths, dec_lengths, queries, key_weight, value_weight):
        f32, bf16 = jnp.float32, jnp.bfloat16
        s = lax.axis_index("section")
        c = lax.axis_index("ctx")
        t = lax.axis_index("tp")
        rows, feat = enc_out.shape
        head_width = key_weight.shape[2]
        sub = head_width // n_ctx
        cr = rows // n_chunks
        wk = key_weight[0].reshape(feat, n_ctx, sub)
        wv = value_weight[0].reshape(feat, n_ctx, sub)
        yb = c // 2
        xb = c % 2

        def pick(x, i, axis):
            return lax.dynamic_index_in_dim(x, i, axis, keepdims=False)

        def add(a, b):
            return (a.astype(f32) + b.astype(f32)).astype(bf16)

        key_parts, value_parts, places = [], [], []
        for k in range(n_chunks):
            mine = enc_out[k * cr:(k + 1) * cr]
            own_moved = [lax.ppermute(mine, "section", shift_perm(n_sec, d)) for d in range(1, n_sec)]
            received = jnp.stack([lax.ppermute(mine, "tp", shift_perm(n_tp, d)) for d in range(1, n_tp)])
            moved = lax.ppermute(received, "section", shift_perm(n_sec, 1))
            own_rows = jnp.concatenate([mine[None], received], axis=0).reshape(n_tp * cr, feat)
            partner_rows = jnp.concatenate([own_moved[0][None], moved], axis=0).reshape(n_tp * cr, feat)
            d_sec = jnp.arange(n_sec, dtype=jnp.int32)[:, None, None]
            d_tp = jnp.arange(n_tp, dtype=jnp.int32)[None, :, None]
            r = jnp.arange(cr, dtype=jnp.int32)[None, None, :]
            src = ((s - d_sec) % n_sec) * n_tp + (t - d_tp) % n_tp
            places.append((src * rows + k * cr + r).reshape(-1))
            half = n_tp * cr

            def project(x):
                pk = jnp.einsum("tf,fgc->gtc", x, wk, preferred_element_type=f32).astype(bf16)
                pv = jnp.einsum("tf,fgc->gtc", x, wv, preferred_element_type=f32).astype(bf16)
                return pk.reshape(2, 2, half, sub), pv.reshape(2, 2, half, sub)

            a_pk, a_pv = project(own_rows)
            send_k, send_v = pick(a_pk, 1 - yb, 0), pick(a_pv, 1 - yb, 0)
            send_k, send_v, _ = lax.optimization_barrier((send_k, send_v, moved))
            got = lax.ppermute((send_k, send_v), "ctx", xor_perm(n_ctx, 2))
            s1k = add(pick(a_pk, yb, 0), got[0])
            s1v = add(pick(a_pv, yb, 0), got[1])
            got = lax.ppermute((pick(s1k, 1 - xb, 0), pick(s1v, 1 - xb, 0)), "ctx", xor_perm(n_ctx, 1))
            fa_k = add(pick(s1k, xb, 0), got[0])
            fa_v = add(pick(s1v, xb, 0), got[1])
            b_pk, b_pv = project(partner_rows)
            got = lax.ppermute((pick(b_pk, 1 - xb, 1), pick(b_pv, 1 - xb, 1)), "ctx", xor_perm(n_ctx, 1))
            s2k = add(pick(b_pk, xb, 1), got[0])
            s2v = add(pick(b_pv, xb, 1), got[1])
            got = lax.ppermute((pick(s2k, 1 - yb, 0), pick(s2v, 1 - yb, 0)), "ctx", xor_perm(n_ctx, 2))
            fb_k = add(pick(s2k, yb, 0), got[0])
            fb_v = add(pick(s2v, yb, 0), got[1])
            key_parts += [fa_k, fb_k]
            value_parts += [fa_v, fb_v]

        keys = jnp.concatenate(key_parts, axis=0)
        values = jnp.concatenate(value_parts, axis=0)
        key_places = jnp.concatenate(places)
        key_count = keys.shape[0]
        heads = sub // HD
        enc_doc = document_ids(enc_lengths, key_places)
        section_queries = lax.dynamic_slice_in_dim(queries[0], c * sub, sub, axis=1)
        query_count = section_queries.shape[0]
        dec_doc = document_ids(dec_lengths, jnp.arange(query_count, dtype=jnp.int32))
        allowed = dec_doc[:, None] == enc_doc[None, :]
        factor = 1.0 / math.sqrt(HD)
        query_heads = section_queries.reshape(query_count, heads, HD)
        key_heads = keys.reshape(key_count, heads, HD)
        value_heads = values.reshape(key_count, heads, HD)
        scores = (
            jnp.einsum("qhd,khd->hqk", query_heads, key_heads, preferred_element_type=f32)
            * factor
        )
        scores = jnp.where(allowed[None], scores, f32(-1e30))
        top = jnp.max(scores, axis=2, keepdims=True)
        weights = jnp.where(allowed[None], jnp.exp(scores - top), f32(0.0))
        totals = jnp.sum(weights, axis=2)
        numer = jnp.einsum("hqk,khd->qhd", weights.astype(bf16), value_heads, preferred_element_type=f32)
        context = (numer / totals.T[:, :, None]).astype(bf16).reshape(query_count, sub)
        share = query_count // n_ctx
        blocks = context.reshape(n_ctx, share, sub)
        pieces = [pick(blocks, c, 0)]
        for d in range(1, n_ctx):
            pieces.append(lax.ppermute(pick(blocks, (c + d) % n_ctx, 0), "ctx", shift_perm(n_ctx, d)))
        groups = []
        for g in range(n_ctx):
            val = pieces[0]
            for d in range(1, n_ctx):
                val = jnp.where((c - d) % n_ctx == g, pieces[d], val)
            groups.append(val)
        return jnp.concatenate(groups, axis=1).reshape(1, share, head_width)

    return fast


def solution(mesh):
    in_specs = (
        P(("section", "tp"), "ctx"),
        P(),
        P(),
        P("section", None, "tp"),
        P("section", "ctx", "tp"),
        P("section", "ctx", "tp"),
    )
    out_specs = P("section", "ctx", "tp")
    n_sec, n_ctx, n_tp = mesh.shape["section"], mesh.shape["ctx"], mesh.shape["tp"]
    return jax.shard_map(
        lambda *a: choose(n_sec, n_ctx, n_tp, *a), mesh=mesh, in_specs=in_specs, out_specs=out_specs, check_vma=False
    )


def choose(n_sec, n_ctx, n_tp, enc_out, enc_lengths, dec_lengths, queries, key_weight, value_weight):
    rows = enc_out.shape[0]
    head_width = key_weight.shape[2]
    query_count = queries.shape[1]
    ok = (
        n_ctx == 4
        and n_sec == 2
        and N_CHUNKS == 1
        and head_width % (n_ctx * HD) == 0
        and rows % N_CHUNKS == 0
        and (n_sec * n_tp * (rows // N_CHUNKS)) % 2 == 0
        and query_count % n_ctx == 0
    )
    args = (enc_out, enc_lengths, dec_lengths, queries, key_weight, value_weight)
    if ok:
        return make_fast(n_sec, n_ctx, n_tp, N_CHUNKS)(*args)
    return on_device(*args)
```

```python
import math

import jax
import jax.numpy as jnp
from jax import lax
from jax.sharding import PartitionSpec as P

HD = 64
N_CHUNKS = 1


def document_ids(lengths, places):
    ends = jnp.cumsum(lengths)
    return jnp.sum((places[:, None] >= ends[None, :]).astype(jnp.int32), axis=1)


def on_device(enc_out, enc_lengths, dec_lengths, queries, key_weight, value_weight):
    gathered = lax.all_gather(enc_out, ("section", "tp"), axis=0, tiled=True)
    head_width = key_weight.shape[2]
    heads_here = head_width // HD
    both_weights = jnp.concatenate([key_weight[0], value_weight[0]], axis=1)
    summed = lax.psum_scatter(
        jnp.dot(gathered, both_weights, preferred_element_type=jnp.float32).astype(jnp.bfloat16),
        "ctx",
        scatter_dimension=0,
        tiled=True,
    )
    local_keys = summed[:, :head_width]
    local_values = summed[:, head_width:]
    key_count = local_keys.shape[0]
    key_places = lax.axis_index("ctx") * key_count + jnp.arange(key_count, dtype=jnp.int32)
    enc_doc = document_ids(enc_lengths, key_places)
    section_queries = queries[0]
    query_count = section_queries.shape[0]
    dec_doc = document_ids(dec_lengths, jnp.arange(query_count, dtype=jnp.int32))
    allowed = dec_doc[:, None] == enc_doc[None, :]
    factor = 1.0 / math.sqrt(HD)
    query_heads = section_queries.reshape(query_count, heads_here, HD)
    key_heads = local_keys.reshape(key_count, heads_here, HD)
    value_heads = local_values.reshape(key_count, heads_here, HD)
    scores = (
        jnp.einsum("qhd,khd->hqk", query_heads, key_heads, preferred_element_type=jnp.float32)
        * factor
    )
    scores = jnp.where(allowed[None], scores, jnp.float32(-1e30))
    local_top = jnp.max(scores, axis=2)
    top = lax.pmax(local_top, "ctx")
    weights = jnp.where(allowed[None], jnp.exp(scores - top[:, :, None]), jnp.float32(0.0))
    totals = jnp.sum(weights, axis=2)
    numer = jnp.einsum(
        "hqk,khd->qhd",
        weights.astype(jnp.bfloat16),
        value_heads,
        preferred_element_type=jnp.float32,
    )
    numer = numer.reshape(query_count, head_width)
    numer_share, total_share = (
        lax.psum_scatter(numer.astype(jnp.bfloat16), "ctx", scatter_dimension=0, tiled=True).astype(
            jnp.float32
        ),
        lax.psum_scatter(
            totals.T.astype(jnp.bfloat16), "ctx", scatter_dimension=0, tiled=True
        ).astype(jnp.float32),
    )
    share_rows = numer_share.shape[0]
    result = numer_share.reshape(share_rows, heads_here, HD) / total_share[:, :, None]
    return result.reshape(1, share_rows, head_width).astype(jnp.bfloat16)


def shift_perm(n, d):
    return [(i, (i + d) % n) for i in range(n)]


def xor_perm(n, b):
    return [(i, i ^ b) for i in range(n)]


def make_fast(n_sec, n_ctx, n_tp, n_chunks):
    def fast(enc_out, enc_lengths, dec_lengths, queries, key_weight, value_weight):
        f32, bf16 = jnp.float32, jnp.bfloat16
        s = lax.axis_index("section")
        c = lax.axis_index("ctx")
        t = lax.axis_index("tp")
        rows, feat = enc_out.shape
        head_width = key_weight.shape[2]
        sub = head_width // n_ctx
        cr = rows // n_chunks
        wk = key_weight[0].reshape(feat, n_ctx, sub)
        wv = value_weight[0].reshape(feat, n_ctx, sub)
        yb = c // 2
        xb = c % 2

        def pick(x, i, axis):
            return lax.dynamic_index_in_dim(x, i, axis, keepdims=False)

        def add(a, b):
            return (a.astype(f32) + b.astype(f32)).astype(bf16)

        key_parts, value_parts, places = [], [], []
        for k in range(n_chunks):
            mine = enc_out[k * cr:(k + 1) * cr]
            own_moved = [lax.ppermute(mine, "section", shift_perm(n_sec, d)) for d in range(1, n_sec)]
            received = jnp.stack([lax.ppermute(mine, "tp", shift_perm(n_tp, d)) for d in range(1, n_tp)])
            moved = lax.ppermute(received, "section", shift_perm(n_sec, 1))
            own_rows = jnp.concatenate([mine[None], received], axis=0).reshape(n_tp * cr, feat)
            partner_rows = jnp.concatenate([own_moved[0][None], moved], axis=0).reshape(n_tp * cr, feat)
            d_sec = jnp.arange(n_sec, dtype=jnp.int32)[:, None, None]
            d_tp = jnp.arange(n_tp, dtype=jnp.int32)[None, :, None]
            r = jnp.arange(cr, dtype=jnp.int32)[None, None, :]
            src = ((s - d_sec) % n_sec) * n_tp + (t - d_tp) % n_tp
            places.append((src * rows + k * cr + r).reshape(-1))
            half = n_tp * cr

            def project(x):
                pk = jnp.einsum("tf,fgc->gtc", x, wk, preferred_element_type=f32).astype(bf16)
                pv = jnp.einsum("tf,fgc->gtc", x, wv, preferred_element_type=f32).astype(bf16)
                return pk.reshape(2, 2, half, sub), pv.reshape(2, 2, half, sub)

            a_pk, a_pv = project(own_rows)
            send_k, send_v = pick(a_pk, 1 - yb, 0), pick(a_pv, 1 - yb, 0)
            send_k, send_v, _ = lax.optimization_barrier((send_k, send_v, moved))
            got = lax.ppermute((send_k, send_v), "ctx", xor_perm(n_ctx, 2))
            s1k = add(pick(a_pk, yb, 0), got[0])
            s1v = add(pick(a_pv, yb, 0), got[1])
            got = lax.ppermute((pick(s1k, 1 - xb, 0), pick(s1v, 1 - xb, 0)), "ctx", xor_perm(n_ctx, 1))
            fa_k = add(pick(s1k, xb, 0), got[0])
            fa_v = add(pick(s1v, xb, 0), got[1])
            b_pk, b_pv = project(partner_rows)
            got = lax.ppermute((pick(b_pk, 1 - xb, 1), pick(b_pv, 1 - xb, 1)), "ctx", xor_perm(n_ctx, 1))
            s2k = add(pick(b_pk, xb, 1), got[0])
            s2v = add(pick(b_pv, xb, 1), got[1])
            got = lax.ppermute((pick(s2k, 1 - yb, 0), pick(s2v, 1 - yb, 0)), "ctx", xor_perm(n_ctx, 2))
            fb_k = add(pick(s2k, yb, 0), got[0])
            fb_v = add(pick(s2v, yb, 0), got[1])
            key_parts += [fa_k, fb_k]
            value_parts += [fa_v, fb_v]

        keys = jnp.concatenate(key_parts, axis=0)
        values = jnp.concatenate(value_parts, axis=0)
        key_places = jnp.concatenate(places)
        key_count = keys.shape[0]
        heads = sub // HD
        enc_doc = document_ids(enc_lengths, key_places)
        section_queries = lax.dynamic_slice_in_dim(queries[0], c * sub, sub, axis=1)
        query_count = section_queries.shape[0]
        share = query_count // n_ctx
        first = c * share
        section_queries = lax.dynamic_slice_in_dim(
            jnp.concatenate([section_queries, section_queries], axis=0), first, query_count, axis=0
        )
        query_places = (first + jnp.arange(query_count, dtype=jnp.int32)) % query_count
        dec_doc = document_ids(dec_lengths, query_places)
        allowed = dec_doc[:, None] == enc_doc[None, :]
        factor = 1.0 / math.sqrt(HD)
        query_heads = section_queries.reshape(query_count, heads, HD)
        key_heads = keys.reshape(key_count, heads, HD)
        value_heads = values.reshape(key_count, heads, HD)
        scores = (
            jnp.einsum("qhd,khd->hqk", query_heads, key_heads, preferred_element_type=f32)
            * factor
        )
        scores = jnp.where(allowed[None], scores, f32(-1e30))
        top = jnp.max(scores, axis=2, keepdims=True)
        weights = jnp.where(allowed[None], jnp.exp(scores - top), f32(0.0))
        totals = jnp.sum(weights, axis=2)
        numer = jnp.einsum("hqk,khd->qhd", weights.astype(bf16), value_heads, preferred_element_type=f32)
        context = (numer / totals.T[:, :, None]).astype(bf16).reshape(query_count, sub)
        blocks = context.reshape(n_ctx, share, sub)
        pieces = [blocks[0]]
        for d in range(1, n_ctx):
            pieces.append(lax.ppermute(blocks[d], "ctx", shift_perm(n_ctx, d)))
        groups = []
        for g in range(n_ctx):
            val = pieces[0]
            for d in range(1, n_ctx):
                val = jnp.where((c - d) % n_ctx == g, pieces[d], val)
            groups.append(val)
        return jnp.concatenate(groups, axis=1).reshape(1, share, head_width)

    return fast


def solution(mesh):
    in_specs = (
        P(("section", "tp"), "ctx"),
        P(),
        P(),
        P("section", None, "tp"),
        P("section", "ctx", "tp"),
        P("section", "ctx", "tp"),
    )
    out_specs = P("section", "ctx", "tp")
    n_sec, n_ctx, n_tp = mesh.shape["section"], mesh.shape["ctx"], mesh.shape["tp"]
    return jax.shard_map(
        lambda *a: choose(n_sec, n_ctx, n_tp, *a), mesh=mesh, in_specs=in_specs, out_specs=out_specs, check_vma=False
    )


def choose(n_sec, n_ctx, n_tp, enc_out, enc_lengths, dec_lengths, queries, key_weight, value_weight):
    rows = enc_out.shape[0]
    head_width = key_weight.shape[2]
    query_count = queries.shape[1]
    ok = (
        n_ctx == 4
        and n_sec == 2
        and N_CHUNKS == 1
        and head_width % (n_ctx * HD) == 0
        and rows % N_CHUNKS == 0
        and (n_sec * n_tp * (rows // N_CHUNKS)) % 2 == 0
        and query_count % n_ctx == 0
    )
    args = (enc_out, enc_lengths, dec_lengths, queries, key_weight, value_weight)
    if ok:
        return make_fast(n_sec, n_ctx, n_tp, N_CHUNKS)(*args)
    return on_device(*args)
```

```python
import math

import jax
import jax.numpy as jnp
from jax import lax
from jax.sharding import PartitionSpec as P

HD = 64
N_CHUNKS = 1


def document_ids(lengths, places):
    ends = jnp.cumsum(lengths)
    return jnp.sum((places[:, None] >= ends[None, :]).astype(jnp.int32), axis=1)


def on_device(enc_out, enc_lengths, dec_lengths, queries, key_weight, value_weight):
    gathered = lax.all_gather(enc_out, ("section", "tp"), axis=0, tiled=True)
    head_width = key_weight.shape[2]
    heads_here = head_width // HD
    both_weights = jnp.concatenate([key_weight[0], value_weight[0]], axis=1)
    summed = lax.psum_scatter(
        jnp.dot(gathered, both_weights, preferred_element_type=jnp.float32).astype(jnp.bfloat16),
        "ctx",
        scatter_dimension=0,
        tiled=True,
    )
    local_keys = summed[:, :head_width]
    local_values = summed[:, head_width:]
    key_count = local_keys.shape[0]
    key_places = lax.axis_index("ctx") * key_count + jnp.arange(key_count, dtype=jnp.int32)
    enc_doc = document_ids(enc_lengths, key_places)
    section_queries = queries[0]
    query_count = section_queries.shape[0]
    dec_doc = document_ids(dec_lengths, jnp.arange(query_count, dtype=jnp.int32))
    allowed = dec_doc[:, None] == enc_doc[None, :]
    factor = 1.0 / math.sqrt(HD)
    query_heads = section_queries.reshape(query_count, heads_here, HD)
    key_heads = local_keys.reshape(key_count, heads_here, HD)
    value_heads = local_values.reshape(key_count, heads_here, HD)
    scores = (
        jnp.einsum("qhd,khd->hqk", query_heads, key_heads, preferred_element_type=jnp.float32)
        * factor
    )
    scores = jnp.where(allowed[None], scores, jnp.float32(-1e30))
    local_top = jnp.max(scores, axis=2)
    top = lax.pmax(local_top, "ctx")
    weights = jnp.where(allowed[None], jnp.exp(scores - top[:, :, None]), jnp.float32(0.0))
    totals = jnp.sum(weights, axis=2)
    numer = jnp.einsum(
        "hqk,khd->qhd",
        weights.astype(jnp.bfloat16),
        value_heads,
        preferred_element_type=jnp.float32,
    )
    numer = numer.reshape(query_count, head_width)
    numer_share, total_share = (
        lax.psum_scatter(numer.astype(jnp.bfloat16), "ctx", scatter_dimension=0, tiled=True).astype(
            jnp.float32
        ),
        lax.psum_scatter(
            totals.T.astype(jnp.bfloat16), "ctx", scatter_dimension=0, tiled=True
        ).astype(jnp.float32),
    )
    share_rows = numer_share.shape[0]
    result = numer_share.reshape(share_rows, heads_here, HD) / total_share[:, :, None]
    return result.reshape(1, share_rows, head_width).astype(jnp.bfloat16)


def shift_perm(n, d):
    return [(i, (i + d) % n) for i in range(n)]


def xor_perm(n, b):
    return [(i, i ^ b) for i in range(n)]


def make_fast(n_sec, n_ctx, n_tp, n_chunks):
    def fast(enc_out, enc_lengths, dec_lengths, queries, key_weight, value_weight):
        f32, bf16 = jnp.float32, jnp.bfloat16
        s = lax.axis_index("section")
        c = lax.axis_index("ctx")
        t = lax.axis_index("tp")
        rows, feat = enc_out.shape
        head_width = key_weight.shape[2]
        sub = head_width // n_ctx
        cr = rows // n_chunks
        wk = key_weight[0].reshape(feat, n_ctx, sub)
        wv = value_weight[0].reshape(feat, n_ctx, sub)
        yb = c // 2
        xb = c % 2

        def pick(x, i, axis):
            return lax.dynamic_index_in_dim(x, i, axis, keepdims=False)

        def add(a, b):
            return (a.astype(f32) + b.astype(f32)).astype(bf16)

        key_parts, value_parts, places = [], [], []
        for k in range(n_chunks):
            mine = enc_out[k * cr:(k + 1) * cr]
            own_moved = [lax.ppermute(mine, "section", shift_perm(n_sec, d)) for d in range(1, n_sec)]
            received = jnp.stack([lax.ppermute(mine, "tp", shift_perm(n_tp, d)) for d in range(1, n_tp)])
            moved = lax.ppermute(received, "section", shift_perm(n_sec, 1))
            own_rows = jnp.concatenate([mine[None], received], axis=0).reshape(n_tp * cr, feat)
            partner_rows = jnp.concatenate([own_moved[0][None], moved], axis=0).reshape(n_tp * cr, feat)
            d_sec = jnp.arange(n_sec, dtype=jnp.int32)[:, None, None]
            d_tp = jnp.arange(n_tp, dtype=jnp.int32)[None, :, None]
            r = jnp.arange(cr, dtype=jnp.int32)[None, None, :]
            src = ((s - d_sec) % n_sec) * n_tp + (t - d_tp) % n_tp
            places.append((src * rows + k * cr + r).reshape(-1))
            half = n_tp * cr

            def project(x):
                pk = jnp.einsum("tf,fgc->gtc", x, wk, preferred_element_type=f32).astype(bf16)
                pv = jnp.einsum("tf,fgc->gtc", x, wv, preferred_element_type=f32).astype(bf16)
                return pk.reshape(2, 2, half, sub), pv.reshape(2, 2, half, sub)

            a_pk, a_pv = project(own_rows)
            send_k, send_v = pick(a_pk, 1 - yb, 0), pick(a_pv, 1 - yb, 0)
            send_k, send_v, _ = lax.optimization_barrier((send_k, send_v, moved))
            got = lax.ppermute((send_k, send_v), "ctx", xor_perm(n_ctx, 2))
            s1k = add(pick(a_pk, yb, 0), got[0])
            s1v = add(pick(a_pv, yb, 0), got[1])
            got = lax.ppermute((pick(s1k, 1 - xb, 0), pick(s1v, 1 - xb, 0)), "ctx", xor_perm(n_ctx, 1))
            fa_k = add(pick(s1k, xb, 0), got[0])
            fa_v = add(pick(s1v, xb, 0), got[1])
            b_pk, b_pv = project(partner_rows)
            got = lax.ppermute((pick(b_pk, 1 - xb, 1), pick(b_pv, 1 - xb, 1)), "ctx", xor_perm(n_ctx, 1))
            s2k = add(pick(b_pk, xb, 1), got[0])
            s2v = add(pick(b_pv, xb, 1), got[1])
            got = lax.ppermute((pick(s2k, 1 - yb, 0), pick(s2v, 1 - yb, 0)), "ctx", xor_perm(n_ctx, 2))
            fb_k = add(pick(s2k, yb, 0), got[0])
            fb_v = add(pick(s2v, yb, 0), got[1])
            key_parts += [fa_k, fb_k]
            value_parts += [fa_v, fb_v]

        keys = jnp.concatenate(key_parts, axis=0)
        values = jnp.concatenate(value_parts, axis=0)
        key_places = jnp.concatenate(places)
        key_count = keys.shape[0]
        heads = sub // HD
        enc_doc = document_ids(enc_lengths, key_places)
        section_queries = lax.dynamic_slice_in_dim(queries[0], c * sub, sub, axis=1)
        query_count = section_queries.shape[0]
        share = query_count // n_ctx
        owners = [c ^ j for j in range(n_ctx)]
        section_queries = jnp.concatenate(
            [lax.dynamic_slice_in_dim(section_queries, o * share, share, axis=0) for o in owners], axis=0
        )
        query_places = jnp.concatenate([o * share + jnp.arange(share, dtype=jnp.int32) for o in owners])
        dec_doc = document_ids(dec_lengths, query_places)
        allowed = dec_doc[:, None] == enc_doc[None, :]
        factor = 1.0 / math.sqrt(HD)
        query_heads = section_queries.reshape(query_count, heads, HD)
        key_heads = keys.reshape(key_count, heads, HD)
        value_heads = values.reshape(key_count, heads, HD)
        scores = (
            jnp.einsum("qhd,khd->hqk", query_heads, key_heads, preferred_element_type=f32)
            * factor
        )
        scores = jnp.where(allowed[None], scores, f32(-1e30))
        top = jnp.max(scores, axis=2, keepdims=True)
        weights = jnp.where(allowed[None], jnp.exp(scores - top), f32(0.0))
        totals = jnp.sum(weights, axis=2)
        numer = jnp.einsum("hqk,khd->qhd", weights.astype(bf16), value_heads, preferred_element_type=f32)
        context = (numer / totals.T[:, :, None]).astype(bf16).reshape(query_count, sub)
        blocks = context.reshape(n_ctx, share, sub)
        got_y = lax.ppermute(blocks[2:4], "ctx", xor_perm(n_ctx, 2))
        got_x = lax.ppermute(jnp.stack([blocks[1], got_y[1]]), "ctx", xor_perm(n_ctx, 1))
        groups = []
        for g in range(n_ctx):
            val = jnp.where(c == g, blocks[0], got_x[1])
            val = jnp.where((c ^ 2) == g, got_y[0], val)
            val = jnp.where((c ^ 1) == g, got_x[0], val)
            groups.append(val)
        return jnp.concatenate(groups, axis=1).reshape(1, share, head_width)

    return fast


def solution(mesh):
    in_specs = (
        P(("section", "tp"), "ctx"),
        P(),
        P(),
        P("section", None, "tp"),
        P("section", "ctx", "tp"),
        P("section", "ctx", "tp"),
    )
    out_specs = P("section", "ctx", "tp")
    n_sec, n_ctx, n_tp = mesh.shape["section"], mesh.shape["ctx"], mesh.shape["tp"]
    return jax.shard_map(
        lambda *a: choose(n_sec, n_ctx, n_tp, *a), mesh=mesh, in_specs=in_specs, out_specs=out_specs, check_vma=False
    )


def choose(n_sec, n_ctx, n_tp, enc_out, enc_lengths, dec_lengths, queries, key_weight, value_weight):
    rows = enc_out.shape[0]
    head_width = key_weight.shape[2]
    query_count = queries.shape[1]
    ok = (
        n_ctx == 4
        and n_sec == 2
        and N_CHUNKS == 1
        and head_width % (n_ctx * HD) == 0
        and rows % N_CHUNKS == 0
        and (n_sec * n_tp * (rows // N_CHUNKS)) % 2 == 0
        and query_count % n_ctx == 0
    )
    args = (enc_out, enc_lengths, dec_lengths, queries, key_weight, value_weight)
    if ok:
        return make_fast(n_sec, n_ctx, n_tp, N_CHUNKS)(*args)
    return on_device(*args)
```

```python
import math

import jax
import jax.numpy as jnp
from jax import lax
from jax.sharding import PartitionSpec as P

HD = 64
N_CHUNKS = 1


def document_ids(lengths, places):
    ends = jnp.cumsum(lengths)
    return jnp.sum((places[:, None] >= ends[None, :]).astype(jnp.int32), axis=1)


def on_device(enc_out, enc_lengths, dec_lengths, queries, key_weight, value_weight):
    gathered = lax.all_gather(enc_out, ("section", "tp"), axis=0, tiled=True)
    head_width = key_weight.shape[2]
    heads_here = head_width // HD
    both_weights = jnp.concatenate([key_weight[0], value_weight[0]], axis=1)
    summed = lax.psum_scatter(
        jnp.dot(gathered, both_weights, preferred_element_type=jnp.float32).astype(jnp.bfloat16),
        "ctx",
        scatter_dimension=0,
        tiled=True,
    )
    local_keys = summed[:, :head_width]
    local_values = summed[:, head_width:]
    key_count = local_keys.shape[0]
    key_places = lax.axis_index("ctx") * key_count + jnp.arange(key_count, dtype=jnp.int32)
    enc_doc = document_ids(enc_lengths, key_places)
    section_queries = queries[0]
    query_count = section_queries.shape[0]
    dec_doc = document_ids(dec_lengths, jnp.arange(query_count, dtype=jnp.int32))
    allowed = dec_doc[:, None] == enc_doc[None, :]
    factor = 1.0 / math.sqrt(HD)
    query_heads = section_queries.reshape(query_count, heads_here, HD)
    key_heads = local_keys.reshape(key_count, heads_here, HD)
    value_heads = local_values.reshape(key_count, heads_here, HD)
    scores = (
        jnp.einsum("qhd,khd->hqk", query_heads, key_heads, preferred_element_type=jnp.float32)
        * factor
    )
    scores = jnp.where(allowed[None], scores, jnp.float32(-1e30))
    local_top = jnp.max(scores, axis=2)
    top = lax.pmax(local_top, "ctx")
    weights = jnp.where(allowed[None], jnp.exp(scores - top[:, :, None]), jnp.float32(0.0))
    totals = jnp.sum(weights, axis=2)
    numer = jnp.einsum(
        "hqk,khd->qhd",
        weights.astype(jnp.bfloat16),
        value_heads,
        preferred_element_type=jnp.float32,
    )
    numer = numer.reshape(query_count, head_width)
    numer_share, total_share = (
        lax.psum_scatter(numer.astype(jnp.bfloat16), "ctx", scatter_dimension=0, tiled=True).astype(
            jnp.float32
        ),
        lax.psum_scatter(
            totals.T.astype(jnp.bfloat16), "ctx", scatter_dimension=0, tiled=True
        ).astype(jnp.float32),
    )
    share_rows = numer_share.shape[0]
    result = numer_share.reshape(share_rows, heads_here, HD) / total_share[:, :, None]
    return result.reshape(1, share_rows, head_width).astype(jnp.bfloat16)


def shift_perm(n, d):
    return [(i, (i + d) % n) for i in range(n)]


def xor_perm(n, b):
    return [(i, i ^ b) for i in range(n)]


def make_fast(n_sec, n_ctx, n_tp, n_chunks):
    def fast(enc_out, enc_lengths, dec_lengths, queries, key_weight, value_weight):
        f32, bf16 = jnp.float32, jnp.bfloat16
        s = lax.axis_index("section")
        c = lax.axis_index("ctx")
        t = lax.axis_index("tp")
        rows, feat = enc_out.shape
        head_width = key_weight.shape[2]
        sub = head_width // n_ctx
        cr = rows // n_chunks
        wk = key_weight[0].reshape(feat, n_ctx, sub)
        wv = value_weight[0].reshape(feat, n_ctx, sub)
        yb = c // 2
        xb = c % 2

        def pick(x, i, axis):
            return lax.dynamic_index_in_dim(x, i, axis, keepdims=False)

        def add(a, b):
            return (a.astype(f32) + b.astype(f32)).astype(bf16)

        key_parts, value_parts, places = [], [], []
        for k in range(n_chunks):
            mine = enc_out[k * cr:(k + 1) * cr]
            own_moved = [lax.ppermute(mine, "section", shift_perm(n_sec, d)) for d in range(1, n_sec)]
            received = jnp.stack([lax.ppermute(mine, "tp", shift_perm(n_tp, d)) for d in range(1, n_tp)])
            moved = lax.ppermute(received, "section", shift_perm(n_sec, 1))
            own_rows = jnp.concatenate([mine[None], received], axis=0).reshape(n_tp * cr, feat)
            partner_rows = jnp.concatenate([own_moved[0][None], moved], axis=0).reshape(n_tp * cr, feat)
            d_sec = jnp.arange(n_sec, dtype=jnp.int32)[:, None, None]
            d_tp = jnp.arange(n_tp, dtype=jnp.int32)[None, :, None]
            r = jnp.arange(cr, dtype=jnp.int32)[None, None, :]
            src = ((s - d_sec) % n_sec) * n_tp + (t - d_tp) % n_tp
            places.append((src * rows + k * cr + r).reshape(-1))
            half = n_tp * cr

            def project(x):
                pk = jnp.einsum("tf,fgc->gtc", x, wk, preferred_element_type=f32).astype(bf16)
                pv = jnp.einsum("tf,fgc->gtc", x, wv, preferred_element_type=f32).astype(bf16)
                return pk.reshape(2, 2, half, sub), pv.reshape(2, 2, half, sub)

            a_pk, a_pv = project(own_rows)
            send_k, send_v = pick(a_pk, 1 - yb, 0), pick(a_pv, 1 - yb, 0)
            send_k, send_v, _ = lax.optimization_barrier((send_k, send_v, moved))
            got = lax.ppermute((send_k, send_v), "ctx", xor_perm(n_ctx, 2))
            s1k = add(pick(a_pk, yb, 0), got[0])
            s1v = add(pick(a_pv, yb, 0), got[1])
            fa_k = add(pick(s1k, xb, 0), lax.ppermute(pick(s1k, 1 - xb, 0), "ctx", xor_perm(n_ctx, 1)))
            b_pk, b_pv = project(partner_rows)
            got = lax.ppermute((pick(b_pk, 1 - xb, 1), pick(b_pv, 1 - xb, 1)), "ctx", xor_perm(n_ctx, 1))
            s2k = add(pick(b_pk, xb, 1), got[0])
            s2v = add(pick(b_pv, xb, 1), got[1])
            fb_k = add(pick(s2k, yb, 0), lax.ppermute(pick(s2k, 1 - yb, 0), "ctx", xor_perm(n_ctx, 2)))
            va, vb, _, _ = lax.optimization_barrier((pick(s1v, 1 - xb, 0), pick(s2v, 1 - yb, 0), fa_k, fb_k))
            fa_v = add(pick(s1v, xb, 0), lax.ppermute(va, "ctx", xor_perm(n_ctx, 1)))
            fb_v = add(pick(s2v, yb, 0), lax.ppermute(vb, "ctx", xor_perm(n_ctx, 2)))
            key_parts += [fa_k, fb_k]
            value_parts += [fa_v, fb_v]

        keys = jnp.concatenate(key_parts, axis=0)
        values = jnp.concatenate(value_parts, axis=0)
        key_places = jnp.concatenate(places)
        key_count = keys.shape[0]
        heads = sub // HD
        enc_doc = document_ids(enc_lengths, key_places)
        section_queries = lax.dynamic_slice_in_dim(queries[0], c * sub, sub, axis=1)
        query_count = section_queries.shape[0]
        share = query_count // n_ctx
        first = c * share
        section_queries = lax.dynamic_slice_in_dim(
            jnp.concatenate([section_queries, section_queries], axis=0), first, query_count, axis=0
        )
        query_places = (first + jnp.arange(query_count, dtype=jnp.int32)) % query_count
        dec_doc = document_ids(dec_lengths, query_places)
        allowed = dec_doc[:, None] == enc_doc[None, :]
        factor = 1.0 / math.sqrt(HD)
        query_heads = section_queries.reshape(query_count, heads, HD)
        key_heads = keys.reshape(key_count, heads, HD)
        value_heads = values.reshape(key_count, heads, HD)
        scores = (
            jnp.einsum("qhd,khd->hqk", query_heads, key_heads, preferred_element_type=f32)
            * factor
        )
        scores = jnp.where(allowed[None], scores, f32(-1e30))
        top = jnp.max(scores, axis=2, keepdims=True)
        weights = jnp.where(allowed[None], jnp.exp(scores - top), f32(0.0))
        totals = jnp.sum(weights, axis=2)
        numer = jnp.einsum("hqk,khd->qhd", weights.astype(bf16), value_heads, preferred_element_type=f32)
        context = (numer / totals.T[:, :, None]).astype(bf16).reshape(query_count, sub)
        blocks = context.reshape(n_ctx, share, sub)
        pieces = [blocks[0]]
        for d in range(1, n_ctx):
            pieces.append(lax.ppermute(blocks[d], "ctx", shift_perm(n_ctx, d)))
        groups = []
        for g in range(n_ctx):
            val = pieces[0]
            for d in range(1, n_ctx):
                val = jnp.where((c - d) % n_ctx == g, pieces[d], val)
            groups.append(val)
        return jnp.concatenate(groups, axis=1).reshape(1, share, head_width)

    return fast


def solution(mesh):
    in_specs = (
        P(("section", "tp"), "ctx"),
        P(),
        P(),
        P("section", None, "tp"),
        P("section", "ctx", "tp"),
        P("section", "ctx", "tp"),
    )
    out_specs = P("section", "ctx", "tp")
    n_sec, n_ctx, n_tp = mesh.shape["section"], mesh.shape["ctx"], mesh.shape["tp"]
    return jax.shard_map(
        lambda *a: choose(n_sec, n_ctx, n_tp, *a), mesh=mesh, in_specs=in_specs, out_specs=out_specs, check_vma=False
    )


def choose(n_sec, n_ctx, n_tp, enc_out, enc_lengths, dec_lengths, queries, key_weight, value_weight):
    rows = enc_out.shape[0]
    head_width = key_weight.shape[2]
    query_count = queries.shape[1]
    ok = (
        n_ctx == 4
        and n_sec == 2
        and N_CHUNKS == 1
        and head_width % (n_ctx * HD) == 0
        and rows % N_CHUNKS == 0
        and (n_sec * n_tp * (rows // N_CHUNKS)) % 2 == 0
        and query_count % n_ctx == 0
    )
    args = (enc_out, enc_lengths, dec_lengths, queries, key_weight, value_weight)
    if ok:
        return make_fast(n_sec, n_ctx, n_tp, N_CHUNKS)(*args)
    return on_device(*args)
```

```python
import math

import jax
import jax.numpy as jnp
from jax import lax
from jax.sharding import PartitionSpec as P

HD = 64
N_CHUNKS = 1


def document_ids(lengths, places):
    ends = jnp.cumsum(lengths)
    return jnp.sum((places[:, None] >= ends[None, :]).astype(jnp.int32), axis=1)


def on_device(enc_out, enc_lengths, dec_lengths, queries, key_weight, value_weight):
    gathered = lax.all_gather(enc_out, ("section", "tp"), axis=0, tiled=True)
    head_width = key_weight.shape[2]
    heads_here = head_width // HD
    both_weights = jnp.concatenate([key_weight[0], value_weight[0]], axis=1)
    summed = lax.psum_scatter(
        jnp.dot(gathered, both_weights, preferred_element_type=jnp.float32).astype(jnp.bfloat16),
        "ctx",
        scatter_dimension=0,
        tiled=True,
    )
    local_keys = summed[:, :head_width]
    local_values = summed[:, head_width:]
    key_count = local_keys.shape[0]
    key_places = lax.axis_index("ctx") * key_count + jnp.arange(key_count, dtype=jnp.int32)
    enc_doc = document_ids(enc_lengths, key_places)
    section_queries = queries[0]
    query_count = section_queries.shape[0]
    dec_doc = document_ids(dec_lengths, jnp.arange(query_count, dtype=jnp.int32))
    allowed = dec_doc[:, None] == enc_doc[None, :]
    factor = 1.0 / math.sqrt(HD)
    query_heads = section_queries.reshape(query_count, heads_here, HD)
    key_heads = local_keys.reshape(key_count, heads_here, HD)
    value_heads = local_values.reshape(key_count, heads_here, HD)
    scores = (
        jnp.einsum("qhd,khd->hqk", query_heads, key_heads, preferred_element_type=jnp.float32)
        * factor
    )
    scores = jnp.where(allowed[None], scores, jnp.float32(-1e30))
    local_top = jnp.max(scores, axis=2)
    top = lax.pmax(local_top, "ctx")
    weights = jnp.where(allowed[None], jnp.exp(scores - top[:, :, None]), jnp.float32(0.0))
    totals = jnp.sum(weights, axis=2)
    numer = jnp.einsum(
        "hqk,khd->qhd",
        weights.astype(jnp.bfloat16),
        value_heads,
        preferred_element_type=jnp.float32,
    )
    numer = numer.reshape(query_count, head_width)
    numer_share, total_share = (
        lax.psum_scatter(numer.astype(jnp.bfloat16), "ctx", scatter_dimension=0, tiled=True).astype(
            jnp.float32
        ),
        lax.psum_scatter(
            totals.T.astype(jnp.bfloat16), "ctx", scatter_dimension=0, tiled=True
        ).astype(jnp.float32),
    )
    share_rows = numer_share.shape[0]
    result = numer_share.reshape(share_rows, heads_here, HD) / total_share[:, :, None]
    return result.reshape(1, share_rows, head_width).astype(jnp.bfloat16)


def shift_perm(n, d):
    return [(i, (i + d) % n) for i in range(n)]


def xor_perm(n, b):
    return [(i, i ^ b) for i in range(n)]


def make_fast(n_sec, n_ctx, n_tp, n_chunks):
    def fast(enc_out, enc_lengths, dec_lengths, queries, key_weight, value_weight):
        f32, bf16 = jnp.float32, jnp.bfloat16
        s = lax.axis_index("section")
        c = lax.axis_index("ctx")
        t = lax.axis_index("tp")
        rows, feat = enc_out.shape
        head_width = key_weight.shape[2]
        sub = head_width // n_ctx
        cr = rows // n_chunks
        wk = key_weight[0].reshape(feat, n_ctx, sub)
        wv = value_weight[0].reshape(feat, n_ctx, sub)
        yb = c // 2
        xb = c % 2

        def pick(x, i, axis):
            return lax.dynamic_index_in_dim(x, i, axis, keepdims=False)

        def add(a, b):
            return (a.astype(f32) + b.astype(f32)).astype(bf16)

        key_parts, value_parts, places = [], [], []
        for k in range(n_chunks):
            mine = enc_out[k * cr:(k + 1) * cr]
            own_moved = [lax.ppermute(mine, "section", shift_perm(n_sec, d)) for d in range(1, n_sec)]
            received = jnp.stack([lax.ppermute(mine, "tp", shift_perm(n_tp, d)) for d in range(1, n_tp)])
            moved = lax.ppermute(received, "section", shift_perm(n_sec, 1))
            own_rows = jnp.concatenate([mine[None], received], axis=0).reshape(n_tp * cr, feat)
            partner_rows = jnp.concatenate([own_moved[0][None], moved], axis=0).reshape(n_tp * cr, feat)
            d_sec = jnp.arange(n_sec, dtype=jnp.int32)[:, None, None]
            d_tp = jnp.arange(n_tp, dtype=jnp.int32)[None, :, None]
            r = jnp.arange(cr, dtype=jnp.int32)[None, None, :]
            src = ((s - d_sec) % n_sec) * n_tp + (t - d_tp) % n_tp
            places.append((src * rows + k * cr + r).reshape(-1))
            half = n_tp * cr

            def project(x):
                pk = jnp.einsum("tf,fgc->gtc", x, wk, preferred_element_type=f32).astype(bf16)
                pv = jnp.einsum("tf,fgc->gtc", x, wv, preferred_element_type=f32).astype(bf16)
                return pk.reshape(2, 2, half, sub), pv.reshape(2, 2, half, sub)

            a_pk, a_pv = project(own_rows)
            send_k, send_v = pick(a_pk, 1 - yb, 0), pick(a_pv, 1 - yb, 0)
            send_k, send_v, _ = lax.optimization_barrier((send_k, send_v, moved))
            got = lax.ppermute((send_k, send_v), "ctx", xor_perm(n_ctx, 2))
            s1k = add(pick(a_pk, yb, 0), got[0])
            s1v = add(pick(a_pv, yb, 0), got[1])
            got = lax.ppermute((pick(s1k, 1 - xb, 0), pick(s1v, 1 - xb, 0)), "ctx", xor_perm(n_ctx, 1))
            fa_k = add(pick(s1k, xb, 0), got[0])
            fa_v = add(pick(s1v, xb, 0), got[1])
            b_pk, b_pv = project(partner_rows)
            got = lax.ppermute((pick(b_pk, 1 - xb, 1), pick(b_pv, 1 - xb, 1)), "ctx", xor_perm(n_ctx, 1))
            s2k = add(pick(b_pk, xb, 1), got[0])
            s2v = add(pick(b_pv, xb, 1), got[1])
            got = lax.ppermute((pick(s2k, 1 - yb, 0), pick(s2v, 1 - yb, 0)), "ctx", xor_perm(n_ctx, 2))
            fb_k = add(pick(s2k, yb, 0), got[0])
            fb_v = add(pick(s2v, yb, 0), got[1])
            key_parts += [fa_k, fb_k]
            value_parts += [fa_v, fb_v]

        keys = jnp.concatenate(key_parts, axis=0)
        values = jnp.concatenate(value_parts, axis=0)
        key_places = jnp.concatenate(places)
        key_count = keys.shape[0]
        heads = sub // HD
        enc_doc = document_ids(enc_lengths, key_places)
        section_queries = lax.dynamic_slice_in_dim(queries[0], c * sub, sub, axis=1)
        query_count = section_queries.shape[0]
        share = query_count // n_ctx
        first = c * share
        section_queries = lax.dynamic_slice_in_dim(
            jnp.concatenate([section_queries, section_queries], axis=0), first, query_count, axis=0
        )
        query_places = (first + jnp.arange(query_count, dtype=jnp.int32)) % query_count
        dec_doc = document_ids(dec_lengths, query_places)
        factor = 1.0 / math.sqrt(HD)
        key_heads = keys.reshape(key_count, heads, HD)
        value_heads = values.reshape(key_count, heads, HD)

        def attend(rows_):
            count = rows_.stop - rows_.start
            allowed = dec_doc[rows_, None] == enc_doc[None, :]
            query_heads = section_queries[rows_].reshape(count, heads, HD)
            scores = (
                jnp.einsum("qhd,khd->hqk", query_heads, key_heads, preferred_element_type=f32)
                * factor
            )
            scores = jnp.where(allowed[None], scores, f32(-1e30))
            top = jnp.max(scores, axis=2, keepdims=True)
            weights = jnp.where(allowed[None], jnp.exp(scores - top), f32(0.0))
            totals = jnp.sum(weights, axis=2)
            numer = jnp.einsum("hqk,khd->qhd", weights.astype(bf16), value_heads, preferred_element_type=f32)
            return (numer / totals.T[:, :, None]).astype(bf16).reshape(count, sub)

        remote = attend(slice(share, query_count)).reshape(n_ctx - 1, share, sub)
        pieces = [None]
        for d in range(1, n_ctx):
            pieces.append(lax.ppermute(remote[d - 1], "ctx", shift_perm(n_ctx, d)))
        pieces[0] = attend(slice(0, share))
        groups = []
        for g in range(n_ctx):
            val = pieces[0]
            for d in range(1, n_ctx):
                val = jnp.where((c - d) % n_ctx == g, pieces[d], val)
            groups.append(val)
        return jnp.concatenate(groups, axis=1).reshape(1, share, head_width)

    return fast


def solution(mesh):
    in_specs = (
        P(("section", "tp"), "ctx"),
        P(),
        P(),
        P("section", None, "tp"),
        P("section", "ctx", "tp"),
        P("section", "ctx", "tp"),
    )
    out_specs = P("section", "ctx", "tp")
    n_sec, n_ctx, n_tp = mesh.shape["section"], mesh.shape["ctx"], mesh.shape["tp"]
    return jax.shard_map(
        lambda *a: choose(n_sec, n_ctx, n_tp, *a), mesh=mesh, in_specs=in_specs, out_specs=out_specs, check_vma=False
    )


def choose(n_sec, n_ctx, n_tp, enc_out, enc_lengths, dec_lengths, queries, key_weight, value_weight):
    rows = enc_out.shape[0]
    head_width = key_weight.shape[2]
    query_count = queries.shape[1]
    ok = (
        n_ctx == 4
        and n_sec == 2
        and N_CHUNKS == 1
        and head_width % (n_ctx * HD) == 0
        and rows % N_CHUNKS == 0
        and (n_sec * n_tp * (rows // N_CHUNKS)) % 2 == 0
        and query_count % n_ctx == 0
    )
    args = (enc_out, enc_lengths, dec_lengths, queries, key_weight, value_weight)
    if ok:
        return make_fast(n_sec, n_ctx, n_tp, N_CHUNKS)(*args)
    return on_device(*args)
```

```python
import math

import jax
import jax.numpy as jnp
from jax import lax
from jax.sharding import PartitionSpec as P

HD = 64
N_CHUNKS = 1


def document_ids(lengths, places):
    ends = jnp.cumsum(lengths)
    return jnp.sum((places[:, None] >= ends[None, :]).astype(jnp.int32), axis=1)


def on_device(enc_out, enc_lengths, dec_lengths, queries, key_weight, value_weight):
    gathered = lax.all_gather(enc_out, ("section", "tp"), axis=0, tiled=True)
    head_width = key_weight.shape[2]
    heads_here = head_width // HD
    both_weights = jnp.concatenate([key_weight[0], value_weight[0]], axis=1)
    summed = lax.psum_scatter(
        jnp.dot(gathered, both_weights, preferred_element_type=jnp.float32).astype(jnp.bfloat16),
        "ctx",
        scatter_dimension=0,
        tiled=True,
    )
    local_keys = summed[:, :head_width]
    local_values = summed[:, head_width:]
    key_count = local_keys.shape[0]
    key_places = lax.axis_index("ctx") * key_count + jnp.arange(key_count, dtype=jnp.int32)
    enc_doc = document_ids(enc_lengths, key_places)
    section_queries = queries[0]
    query_count = section_queries.shape[0]
    dec_doc = document_ids(dec_lengths, jnp.arange(query_count, dtype=jnp.int32))
    allowed = dec_doc[:, None] == enc_doc[None, :]
    factor = 1.0 / math.sqrt(HD)
    query_heads = section_queries.reshape(query_count, heads_here, HD)
    key_heads = local_keys.reshape(key_count, heads_here, HD)
    value_heads = local_values.reshape(key_count, heads_here, HD)
    scores = (
        jnp.einsum("qhd,khd->hqk", query_heads, key_heads, preferred_element_type=jnp.float32)
        * factor
    )
    scores = jnp.where(allowed[None], scores, jnp.float32(-1e30))
    local_top = jnp.max(scores, axis=2)
    top = lax.pmax(local_top, "ctx")
    weights = jnp.where(allowed[None], jnp.exp(scores - top[:, :, None]), jnp.float32(0.0))
    totals = jnp.sum(weights, axis=2)
    numer = jnp.einsum(
        "hqk,khd->qhd",
        weights.astype(jnp.bfloat16),
        value_heads,
        preferred_element_type=jnp.float32,
    )
    numer = numer.reshape(query_count, head_width)
    numer_share, total_share = (
        lax.psum_scatter(numer.astype(jnp.bfloat16), "ctx", scatter_dimension=0, tiled=True).astype(
            jnp.float32
        ),
        lax.psum_scatter(
            totals.T.astype(jnp.bfloat16), "ctx", scatter_dimension=0, tiled=True
        ).astype(jnp.float32),
    )
    share_rows = numer_share.shape[0]
    result = numer_share.reshape(share_rows, heads_here, HD) / total_share[:, :, None]
    return result.reshape(1, share_rows, head_width).astype(jnp.bfloat16)


def shift_perm(n, d):
    return [(i, (i + d) % n) for i in range(n)]


def xor_perm(n, b):
    return [(i, i ^ b) for i in range(n)]


def make_fast(n_sec, n_ctx, n_tp, n_chunks):
    def fast(enc_out, enc_lengths, dec_lengths, queries, key_weight, value_weight):
        f32, bf16 = jnp.float32, jnp.bfloat16
        s = lax.axis_index("section")
        c = lax.axis_index("ctx")
        t = lax.axis_index("tp")
        rows, feat = enc_out.shape
        head_width = key_weight.shape[2]
        sub = head_width // n_ctx
        cr = rows // n_chunks
        wk = key_weight[0].reshape(feat, n_ctx, sub)
        wv = value_weight[0].reshape(feat, n_ctx, sub)
        yb = c // 2
        xb = c % 2

        def pick(x, i, axis):
            return lax.dynamic_index_in_dim(x, i, axis, keepdims=False)

        def add(a, b):
            return (a.astype(f32) + b.astype(f32)).astype(bf16)

        key_parts, value_parts, places = [], [], []
        for k in range(n_chunks):
            mine = enc_out[k * cr:(k + 1) * cr]
            own_moved = [lax.ppermute(mine, "section", shift_perm(n_sec, d)) for d in range(1, n_sec)]
            received = jnp.stack([lax.ppermute(mine, "tp", shift_perm(n_tp, d)) for d in range(1, n_tp)])
            moved = lax.ppermute(received, "section", shift_perm(n_sec, 1))
            own_rows = jnp.concatenate([mine[None], received], axis=0).reshape(n_tp * cr, feat)
            partner_rows = jnp.concatenate([own_moved[0][None], moved], axis=0).reshape(n_tp * cr, feat)
            d_sec = jnp.arange(n_sec, dtype=jnp.int32)[:, None, None]
            d_tp = jnp.arange(n_tp, dtype=jnp.int32)[None, :, None]
            r = jnp.arange(cr, dtype=jnp.int32)[None, None, :]
            src = ((s - d_sec) % n_sec) * n_tp + (t - d_tp) % n_tp
            places.append((src * rows + k * cr + r).reshape(-1))
            half = n_tp * cr

            def project(x):
                pk = jnp.einsum("tf,fgc->gtc", x, wk, preferred_element_type=f32).astype(bf16)
                pv = jnp.einsum("tf,fgc->gtc", x, wv, preferred_element_type=f32).astype(bf16)
                return pk.reshape(2, 2, half, sub), pv.reshape(2, 2, half, sub)

            a_pk, a_pv = project(own_rows)
            send_k, send_v = pick(a_pk, 1 - yb, 0), pick(a_pv, 1 - yb, 0)
            send_k, send_v, _ = lax.optimization_barrier((send_k, send_v, moved))
            got = lax.ppermute(jnp.stack([send_k, send_v]), "ctx", xor_perm(n_ctx, 2))
            s1k = add(pick(a_pk, yb, 0), got[0])
            s1v = add(pick(a_pv, yb, 0), got[1])
            got = lax.ppermute(jnp.stack([pick(s1k, 1 - xb, 0), pick(s1v, 1 - xb, 0)]), "ctx", xor_perm(n_ctx, 1))
            fa_k = add(pick(s1k, xb, 0), got[0])
            fa_v = add(pick(s1v, xb, 0), got[1])
            b_pk, b_pv = project(partner_rows)
            got = lax.ppermute(jnp.stack([pick(b_pk, 1 - xb, 1), pick(b_pv, 1 - xb, 1)]), "ctx", xor_perm(n_ctx, 1))
            s2k = add(pick(b_pk, xb, 1), got[0])
            s2v = add(pick(b_pv, xb, 1), got[1])
            got = lax.ppermute(jnp.stack([pick(s2k, 1 - yb, 0), pick(s2v, 1 - yb, 0)]), "ctx", xor_perm(n_ctx, 2))
            fb_k = add(pick(s2k, yb, 0), got[0])
            fb_v = add(pick(s2v, yb, 0), got[1])
            key_parts += [fa_k, fb_k]
            value_parts += [fa_v, fb_v]

        keys = jnp.concatenate(key_parts, axis=0)
        values = jnp.concatenate(value_parts, axis=0)
        key_places = jnp.concatenate(places)
        key_count = keys.shape[0]
        heads = sub // HD
        enc_doc = document_ids(enc_lengths, key_places)
        section_queries = lax.dynamic_slice_in_dim(queries[0], c * sub, sub, axis=1)
        query_count = section_queries.shape[0]
        share = query_count // n_ctx
        first = c * share
        section_queries = lax.dynamic_slice_in_dim(
            jnp.concatenate([section_queries, section_queries], axis=0), first, query_count, axis=0
        )
        query_places = (first + jnp.arange(query_count, dtype=jnp.int32)) % query_count
        dec_doc = document_ids(dec_lengths, query_places)
        allowed = dec_doc[:, None] == enc_doc[None, :]
        factor = 1.0 / math.sqrt(HD)
        query_heads = section_queries.reshape(query_count, heads, HD)
        key_heads = keys.reshape(key_count, heads, HD)
        value_heads = values.reshape(key_count, heads, HD)
        scores = (
            jnp.einsum("qhd,khd->hqk", query_heads, key_heads, preferred_element_type=f32)
            * factor
        )
        scores = jnp.where(allowed[None], scores, f32(-1e30))
        top = jnp.max(scores, axis=2, keepdims=True)
        weights = jnp.where(allowed[None], jnp.exp(scores - top), f32(0.0))
        totals = jnp.sum(weights, axis=2)
        numer = jnp.einsum("hqk,khd->qhd", weights.astype(bf16), value_heads, preferred_element_type=f32)
        context = (numer / totals.T[:, :, None]).astype(bf16).reshape(query_count, sub)
        blocks = context.reshape(n_ctx, share, sub)
        pieces = [blocks[0]]
        for d in range(1, n_ctx):
            pieces.append(lax.ppermute(blocks[d], "ctx", shift_perm(n_ctx, d)))
        groups = []
        for g in range(n_ctx):
            val = pieces[0]
            for d in range(1, n_ctx):
                val = jnp.where((c - d) % n_ctx == g, pieces[d], val)
            groups.append(val)
        return jnp.concatenate(groups, axis=1).reshape(1, share, head_width)

    return fast


def solution(mesh):
    in_specs = (
        P(("section", "tp"), "ctx"),
        P(),
        P(),
        P("section", None, "tp"),
        P("section", "ctx", "tp"),
        P("section", "ctx", "tp"),
    )
    out_specs = P("section", "ctx", "tp")
    n_sec, n_ctx, n_tp = mesh.shape["section"], mesh.shape["ctx"], mesh.shape["tp"]
    return jax.shard_map(
        lambda *a: choose(n_sec, n_ctx, n_tp, *a), mesh=mesh, in_specs=in_specs, out_specs=out_specs, check_vma=False
    )


def choose(n_sec, n_ctx, n_tp, enc_out, enc_lengths, dec_lengths, queries, key_weight, value_weight):
    rows = enc_out.shape[0]
    head_width = key_weight.shape[2]
    query_count = queries.shape[1]
    ok = (
        n_ctx == 4
        and n_sec == 2
        and N_CHUNKS == 1
        and head_width % (n_ctx * HD) == 0
        and rows % N_CHUNKS == 0
        and (n_sec * n_tp * (rows // N_CHUNKS)) % 2 == 0
        and query_count % n_ctx == 0
    )
    args = (enc_out, enc_lengths, dec_lengths, queries, key_weight, value_weight)
    if ok:
        return make_fast(n_sec, n_ctx, n_tp, N_CHUNKS)(*args)
    return on_device(*args)
```

```python
import math

import jax
import jax.numpy as jnp
from jax import lax
from jax.sharding import PartitionSpec as P

HD = 64
N_CHUNKS = 1


def document_ids(lengths, places):
    ends = jnp.cumsum(lengths)
    return jnp.sum((places[:, None] >= ends[None, :]).astype(jnp.int32), axis=1)


def on_device(enc_out, enc_lengths, dec_lengths, queries, key_weight, value_weight):
    gathered = lax.all_gather(enc_out, ("section", "tp"), axis=0, tiled=True)
    head_width = key_weight.shape[2]
    heads_here = head_width // HD
    both_weights = jnp.concatenate([key_weight[0], value_weight[0]], axis=1)
    summed = lax.psum_scatter(
        jnp.dot(gathered, both_weights, preferred_element_type=jnp.float32).astype(jnp.bfloat16),
        "ctx",
        scatter_dimension=0,
        tiled=True,
    )
    local_keys = summed[:, :head_width]
    local_values = summed[:, head_width:]
    key_count = local_keys.shape[0]
    key_places = lax.axis_index("ctx") * key_count + jnp.arange(key_count, dtype=jnp.int32)
    enc_doc = document_ids(enc_lengths, key_places)
    section_queries = queries[0]
    query_count = section_queries.shape[0]
    dec_doc = document_ids(dec_lengths, jnp.arange(query_count, dtype=jnp.int32))
    allowed = dec_doc[:, None] == enc_doc[None, :]
    factor = 1.0 / math.sqrt(HD)
    query_heads = section_queries.reshape(query_count, heads_here, HD)
    key_heads = local_keys.reshape(key_count, heads_here, HD)
    value_heads = local_values.reshape(key_count, heads_here, HD)
    scores = (
        jnp.einsum("qhd,khd->hqk", query_heads, key_heads, preferred_element_type=jnp.float32)
        * factor
    )
    scores = jnp.where(allowed[None], scores, jnp.float32(-1e30))
    local_top = jnp.max(scores, axis=2)
    top = lax.pmax(local_top, "ctx")
    weights = jnp.where(allowed[None], jnp.exp(scores - top[:, :, None]), jnp.float32(0.0))
    totals = jnp.sum(weights, axis=2)
    numer = jnp.einsum(
        "hqk,khd->qhd",
        weights.astype(jnp.bfloat16),
        value_heads,
        preferred_element_type=jnp.float32,
    )
    numer = numer.reshape(query_count, head_width)
    numer_share, total_share = (
        lax.psum_scatter(numer.astype(jnp.bfloat16), "ctx", scatter_dimension=0, tiled=True).astype(
            jnp.float32
        ),
        lax.psum_scatter(
            totals.T.astype(jnp.bfloat16), "ctx", scatter_dimension=0, tiled=True
        ).astype(jnp.float32),
    )
    share_rows = numer_share.shape[0]
    result = numer_share.reshape(share_rows, heads_here, HD) / total_share[:, :, None]
    return result.reshape(1, share_rows, head_width).astype(jnp.bfloat16)


def shift_perm(n, d):
    return [(i, (i + d) % n) for i in range(n)]


def xor_perm(n, b):
    return [(i, i ^ b) for i in range(n)]


def make_fast(n_sec, n_ctx, n_tp, n_chunks):
    def fast(enc_out, enc_lengths, dec_lengths, queries, key_weight, value_weight):
        f32, bf16 = jnp.float32, jnp.bfloat16
        s = lax.axis_index("section")
        c = lax.axis_index("ctx")
        t = lax.axis_index("tp")
        rows, feat = enc_out.shape
        head_width = key_weight.shape[2]
        sub = head_width // n_ctx
        cr = rows // n_chunks
        wk = key_weight[0].reshape(feat, n_ctx, sub)
        wv = value_weight[0].reshape(feat, n_ctx, sub)
        yb = c // 2
        xb = c % 2

        def pick(x, i, axis):
            return lax.dynamic_index_in_dim(x, i, axis, keepdims=False)

        def add(a, b):
            return (a.astype(f32) + b.astype(f32)).astype(bf16)

        key_parts, value_parts, places = [], [], []
        for k in range(n_chunks):
            mine = enc_out[k * cr:(k + 1) * cr]
            own_moved = [lax.ppermute(mine, "section", shift_perm(n_sec, d)) for d in range(1, n_sec)]
            received = jnp.stack([lax.ppermute(mine, "tp", shift_perm(n_tp, d)) for d in range(1, n_tp)])
            moved = lax.ppermute(received, "section", shift_perm(n_sec, 1))
            own_rows = jnp.concatenate([mine[None], received], axis=0).reshape(n_tp * cr, feat)
            partner_rows = jnp.concatenate([own_moved[0][None], moved], axis=0).reshape(n_tp * cr, feat)
            d_sec = jnp.arange(n_sec, dtype=jnp.int32)[:, None, None]
            d_tp = jnp.arange(n_tp, dtype=jnp.int32)[None, :, None]
            r = jnp.arange(cr, dtype=jnp.int32)[None, None, :]
            src = ((s - d_sec) % n_sec) * n_tp + (t - d_tp) % n_tp
            places.append((src * rows + k * cr + r).reshape(-1))
            half = n_tp * cr

            def project(x):
                pk = jnp.einsum("tf,fgc->gtc", x, wk, preferred_element_type=f32).astype(bf16)
                pv = jnp.einsum("tf,fgc->gtc", x, wv, preferred_element_type=f32).astype(bf16)
                return pk.reshape(2, 2, half, sub), pv.reshape(2, 2, half, sub)

            a_pk, a_pv = project(own_rows)
            send_k, send_v = pick(a_pk, 1 - yb, 0), pick(a_pv, 1 - yb, 0)
            send_k, send_v, _ = lax.optimization_barrier((send_k, send_v, moved))
            got = lax.ppermute((send_k, send_v), "ctx", xor_perm(n_ctx, 2))
            partner_rows, _ = lax.optimization_barrier((partner_rows, got))
            s1k = add(pick(a_pk, yb, 0), got[0])
            s1v = add(pick(a_pv, yb, 0), got[1])
            got = lax.ppermute((pick(s1k, 1 - xb, 0), pick(s1v, 1 - xb, 0)), "ctx", xor_perm(n_ctx, 1))
            fa_k = add(pick(s1k, xb, 0), got[0])
            fa_v = add(pick(s1v, xb, 0), got[1])
            b_pk, b_pv = project(partner_rows)
            got = lax.ppermute((pick(b_pk, 1 - xb, 1), pick(b_pv, 1 - xb, 1)), "ctx", xor_perm(n_ctx, 1))
            s2k = add(pick(b_pk, xb, 1), got[0])
            s2v = add(pick(b_pv, xb, 1), got[1])
            got = lax.ppermute((pick(s2k, 1 - yb, 0), pick(s2v, 1 - yb, 0)), "ctx", xor_perm(n_ctx, 2))
            fb_k = add(pick(s2k, yb, 0), got[0])
            fb_v = add(pick(s2v, yb, 0), got[1])
            key_parts += [fa_k, fb_k]
            value_parts += [fa_v, fb_v]

        keys = jnp.concatenate(key_parts, axis=0)
        values = jnp.concatenate(value_parts, axis=0)
        key_places = jnp.concatenate(places)
        key_count = keys.shape[0]
        heads = sub // HD
        enc_doc = document_ids(enc_lengths, key_places)
        section_queries = lax.dynamic_slice_in_dim(queries[0], c * sub, sub, axis=1)
        query_count = section_queries.shape[0]
        share = query_count // n_ctx
        first = c * share
        section_queries = lax.dynamic_slice_in_dim(
            jnp.concatenate([section_queries, section_queries], axis=0), first, query_count, axis=0
        )
        query_places = (first + jnp.arange(query_count, dtype=jnp.int32)) % query_count
        dec_doc = document_ids(dec_lengths, query_places)
        allowed = dec_doc[:, None] == enc_doc[None, :]
        factor = 1.0 / math.sqrt(HD)
        query_heads = section_queries.reshape(query_count, heads, HD)
        key_heads = keys.reshape(key_count, heads, HD)
        value_heads = values.reshape(key_count, heads, HD)
        scores = (
            jnp.einsum("qhd,khd->hqk", query_heads, key_heads, preferred_element_type=f32)
            * factor
        )
        scores = jnp.where(allowed[None], scores, f32(-1e30))
        top = jnp.max(scores, axis=2, keepdims=True)
        weights = jnp.where(allowed[None], jnp.exp(scores - top), f32(0.0))
        totals = jnp.sum(weights, axis=2)
        numer = jnp.einsum("hqk,khd->qhd", weights.astype(bf16), value_heads, preferred_element_type=f32)
        context = (numer / totals.T[:, :, None]).astype(bf16).reshape(query_count, sub)
        blocks = context.reshape(n_ctx, share, sub)
        pieces = [blocks[0]]
        for d in range(1, n_ctx):
            pieces.append(lax.ppermute(blocks[d], "ctx", shift_perm(n_ctx, d)))
        groups = []
        for g in range(n_ctx):
            val = pieces[0]
            for d in range(1, n_ctx):
                val = jnp.where((c - d) % n_ctx == g, pieces[d], val)
            groups.append(val)
        return jnp.concatenate(groups, axis=1).reshape(1, share, head_width)

    return fast


def solution(mesh):
    in_specs = (
        P(("section", "tp"), "ctx"),
        P(),
        P(),
        P("section", None, "tp"),
        P("section", "ctx", "tp"),
        P("section", "ctx", "tp"),
    )
    out_specs = P("section", "ctx", "tp")
    n_sec, n_ctx, n_tp = mesh.shape["section"], mesh.shape["ctx"], mesh.shape["tp"]
    return jax.shard_map(
        lambda *a: choose(n_sec, n_ctx, n_tp, *a), mesh=mesh, in_specs=in_specs, out_specs=out_specs, check_vma=False
    )


def choose(n_sec, n_ctx, n_tp, enc_out, enc_lengths, dec_lengths, queries, key_weight, value_weight):
    rows = enc_out.shape[0]
    head_width = key_weight.shape[2]
    query_count = queries.shape[1]
    ok = (
        n_ctx == 4
        and n_sec == 2
        and N_CHUNKS == 1
        and head_width % (n_ctx * HD) == 0
        and rows % N_CHUNKS == 0
        and (n_sec * n_tp * (rows // N_CHUNKS)) % 2 == 0
        and query_count % n_ctx == 0
    )
    args = (enc_out, enc_lengths, dec_lengths, queries, key_weight, value_weight)
    if ok:
        return make_fast(n_sec, n_ctx, n_tp, N_CHUNKS)(*args)
    return on_device(*args)
```

```python
import math

import jax
import jax.numpy as jnp
from jax import lax
from jax.sharding import PartitionSpec as P

HD = 64
N_CHUNKS = 1


def document_ids(lengths, places):
    ends = jnp.cumsum(lengths)
    return jnp.sum((places[:, None] >= ends[None, :]).astype(jnp.int32), axis=1)


def on_device(enc_out, enc_lengths, dec_lengths, queries, key_weight, value_weight):
    gathered = lax.all_gather(enc_out, ("section", "tp"), axis=0, tiled=True)
    head_width = key_weight.shape[2]
    heads_here = head_width // HD
    both_weights = jnp.concatenate([key_weight[0], value_weight[0]], axis=1)
    summed = lax.psum_scatter(
        jnp.dot(gathered, both_weights, preferred_element_type=jnp.float32).astype(jnp.bfloat16),
        "ctx",
        scatter_dimension=0,
        tiled=True,
    )
    local_keys = summed[:, :head_width]
    local_values = summed[:, head_width:]
    key_count = local_keys.shape[0]
    key_places = lax.axis_index("ctx") * key_count + jnp.arange(key_count, dtype=jnp.int32)
    enc_doc = document_ids(enc_lengths, key_places)
    section_queries = queries[0]
    query_count = section_queries.shape[0]
    dec_doc = document_ids(dec_lengths, jnp.arange(query_count, dtype=jnp.int32))
    allowed = dec_doc[:, None] == enc_doc[None, :]
    factor = 1.0 / math.sqrt(HD)
    query_heads = section_queries.reshape(query_count, heads_here, HD)
    key_heads = local_keys.reshape(key_count, heads_here, HD)
    value_heads = local_values.reshape(key_count, heads_here, HD)
    scores = (
        jnp.einsum("qhd,khd->hqk", query_heads, key_heads, preferred_element_type=jnp.float32)
        * factor
    )
    scores = jnp.where(allowed[None], scores, jnp.float32(-1e30))
    local_top = jnp.max(scores, axis=2)
    top = lax.pmax(local_top, "ctx")
    weights = jnp.where(allowed[None], jnp.exp(scores - top[:, :, None]), jnp.float32(0.0))
    totals = jnp.sum(weights, axis=2)
    numer = jnp.einsum(
        "hqk,khd->qhd",
        weights.astype(jnp.bfloat16),
        value_heads,
        preferred_element_type=jnp.float32,
    )
    numer = numer.reshape(query_count, head_width)
    numer_share, total_share = (
        lax.psum_scatter(numer.astype(jnp.bfloat16), "ctx", scatter_dimension=0, tiled=True).astype(
            jnp.float32
        ),
        lax.psum_scatter(
            totals.T.astype(jnp.bfloat16), "ctx", scatter_dimension=0, tiled=True
        ).astype(jnp.float32),
    )
    share_rows = numer_share.shape[0]
    result = numer_share.reshape(share_rows, heads_here, HD) / total_share[:, :, None]
    return result.reshape(1, share_rows, head_width).astype(jnp.bfloat16)


def shift_perm(n, d):
    return [(i, (i + d) % n) for i in range(n)]


def xor_perm(n, b):
    return [(i, i ^ b) for i in range(n)]


def make_fast(n_sec, n_ctx, n_tp, n_chunks):
    def fast(enc_out, enc_lengths, dec_lengths, queries, key_weight, value_weight):
        f32, bf16 = jnp.float32, jnp.bfloat16
        s = lax.axis_index("section")
        c = lax.axis_index("ctx")
        t = lax.axis_index("tp")
        rows, feat = enc_out.shape
        head_width = key_weight.shape[2]
        sub = head_width // n_ctx
        cr = rows // n_chunks
        wk = key_weight[0].reshape(feat, n_ctx, sub)
        wv = value_weight[0].reshape(feat, n_ctx, sub)
        yb = c // 2
        xb = c % 2

        def pick(x, i, axis):
            return lax.dynamic_index_in_dim(x, i, axis, keepdims=False)

        def add(a, b):
            return (a.astype(f32) + b.astype(f32)).astype(bf16)

        key_parts, value_parts, places = [], [], []
        for k in range(n_chunks):
            mine = enc_out[k * cr:(k + 1) * cr]
            own_moved = [lax.ppermute(mine, "section", shift_perm(n_sec, d)) for d in range(1, n_sec)]
            received = jnp.stack([lax.ppermute(mine, "tp", shift_perm(n_tp, d)) for d in range(1, n_tp)])
            moved = lax.ppermute(received, "section", shift_perm(n_sec, 1))
            own_rows = jnp.concatenate([mine[None], received], axis=0).reshape(n_tp * cr, feat)
            partner_rows = jnp.concatenate([own_moved[0][None], moved], axis=0).reshape(n_tp * cr, feat)
            d_sec = jnp.arange(n_sec, dtype=jnp.int32)[:, None, None]
            d_tp = jnp.arange(n_tp, dtype=jnp.int32)[None, :, None]
            r = jnp.arange(cr, dtype=jnp.int32)[None, None, :]
            src = ((s - d_sec) % n_sec) * n_tp + (t - d_tp) % n_tp
            places.append((src * rows + k * cr + r).reshape(-1))
            half = n_tp * cr

            def project(x):
                pk = jnp.einsum("tf,fgc->gtc", x, wk, preferred_element_type=f32).astype(bf16)
                pv = jnp.einsum("tf,fgc->gtc", x, wv, preferred_element_type=f32).astype(bf16)
                return pk.reshape(2, 2, half, sub), pv.reshape(2, 2, half, sub)

            def y_first(pk, pv):
                got = lax.ppermute((pick(pk, 1 - yb, 0), pick(pv, 1 - yb, 0)), "ctx", xor_perm(n_ctx, 2))
                sk, sv = add(pick(pk, yb, 0), got[0]), add(pick(pv, yb, 0), got[1])
                got = lax.ppermute((pick(sk, 1 - xb, 0), pick(sv, 1 - xb, 0)), "ctx", xor_perm(n_ctx, 1))
                return add(pick(sk, xb, 0), got[0]), add(pick(sv, xb, 0), got[1])

            def x_first(pk, pv):
                got = lax.ppermute((pick(pk, 1 - xb, 1), pick(pv, 1 - xb, 1)), "ctx", xor_perm(n_ctx, 1))
                sk, sv = add(pick(pk, xb, 1), got[0]), add(pick(pv, xb, 1), got[1])
                got = lax.ppermute((pick(sk, 1 - yb, 0), pick(sv, 1 - yb, 0)), "ctx", xor_perm(n_ctx, 2))
                return add(pick(sk, yb, 0), got[0]), add(pick(sv, yb, 0), got[1])

            quarter = half // 2
            lo, hi = slice(0, quarter), slice(quarter, half)
            a_pk, a_pv = project(own_rows)
            a_pk, a_pv, _ = lax.optimization_barrier((a_pk, a_pv, moved))
            a1 = y_first(a_pk[:, :, lo], a_pv[:, :, lo])
            a2 = x_first(a_pk[:, :, hi], a_pv[:, :, hi])
            b_pk, b_pv = project(partner_rows)
            b1 = y_first(b_pk[:, :, lo], b_pv[:, :, lo])
            b2 = x_first(b_pk[:, :, hi], b_pv[:, :, hi])
            key_parts += [a1[0], a2[0], b1[0], b2[0]]
            value_parts += [a1[1], a2[1], b1[1], b2[1]]

        keys = jnp.concatenate(key_parts, axis=0)
        values = jnp.concatenate(value_parts, axis=0)
        key_places = jnp.concatenate(places)
        key_count = keys.shape[0]
        heads = sub // HD
        enc_doc = document_ids(enc_lengths, key_places)
        section_queries = lax.dynamic_slice_in_dim(queries[0], c * sub, sub, axis=1)
        query_count = section_queries.shape[0]
        share = query_count // n_ctx
        first = c * share
        section_queries = lax.dynamic_slice_in_dim(
            jnp.concatenate([section_queries, section_queries], axis=0), first, query_count, axis=0
        )
        query_places = (first + jnp.arange(query_count, dtype=jnp.int32)) % query_count
        dec_doc = document_ids(dec_lengths, query_places)
        allowed = dec_doc[:, None] == enc_doc[None, :]
        factor = 1.0 / math.sqrt(HD)
        query_heads = section_queries.reshape(query_count, heads, HD)
        key_heads = keys.reshape(key_count, heads, HD)
        value_heads = values.reshape(key_count, heads, HD)
        scores = (
            jnp.einsum("qhd,khd->hqk", query_heads, key_heads, preferred_element_type=f32)
            * factor
        )
        scores = jnp.where(allowed[None], scores, f32(-1e30))
        top = jnp.max(scores, axis=2, keepdims=True)
        weights = jnp.where(allowed[None], jnp.exp(scores - top), f32(0.0))
        totals = jnp.sum(weights, axis=2)
        numer = jnp.einsum("hqk,khd->qhd", weights.astype(bf16), value_heads, preferred_element_type=f32)
        context = (numer / totals.T[:, :, None]).astype(bf16).reshape(query_count, sub)
        blocks = context.reshape(n_ctx, share, sub)
        pieces = [blocks[0]]
        for d in range(1, n_ctx):
            pieces.append(lax.ppermute(blocks[d], "ctx", shift_perm(n_ctx, d)))
        groups = []
        for g in range(n_ctx):
            val = pieces[0]
            for d in range(1, n_ctx):
                val = jnp.where((c - d) % n_ctx == g, pieces[d], val)
            groups.append(val)
        return jnp.concatenate(groups, axis=1).reshape(1, share, head_width)

    return fast


def solution(mesh):
    in_specs = (
        P(("section", "tp"), "ctx"),
        P(),
        P(),
        P("section", None, "tp"),
        P("section", "ctx", "tp"),
        P("section", "ctx", "tp"),
    )
    out_specs = P("section", "ctx", "tp")
    n_sec, n_ctx, n_tp = mesh.shape["section"], mesh.shape["ctx"], mesh.shape["tp"]
    return jax.shard_map(
        lambda *a: choose(n_sec, n_ctx, n_tp, *a), mesh=mesh, in_specs=in_specs, out_specs=out_specs, check_vma=False
    )


def choose(n_sec, n_ctx, n_tp, enc_out, enc_lengths, dec_lengths, queries, key_weight, value_weight):
    rows = enc_out.shape[0]
    head_width = key_weight.shape[2]
    query_count = queries.shape[1]
    ok = (
        n_ctx == 4
        and n_sec == 2
        and (n_tp * rows) % 2 == 0
        and N_CHUNKS == 1
        and head_width % (n_ctx * HD) == 0
        and rows % N_CHUNKS == 0
        and (n_sec * n_tp * (rows // N_CHUNKS)) % 2 == 0
        and query_count % n_ctx == 0
    )
    args = (enc_out, enc_lengths, dec_lengths, queries, key_weight, value_weight)
    if ok:
        return make_fast(n_sec, n_ctx, n_tp, N_CHUNKS)(*args)
    return on_device(*args)
```

```python
import math

import jax
import jax.numpy as jnp
from jax import lax
from jax.sharding import PartitionSpec as P

HD = 64
N_CHUNKS = 1


def document_ids(lengths, places):
    ends = jnp.cumsum(lengths)
    return jnp.sum((places[:, None] >= ends[None, :]).astype(jnp.int32), axis=1)


def on_device(enc_out, enc_lengths, dec_lengths, queries, key_weight, value_weight):
    gathered = lax.all_gather(enc_out, ("section", "tp"), axis=0, tiled=True)
    head_width = key_weight.shape[2]
    heads_here = head_width // HD
    both_weights = jnp.concatenate([key_weight[0], value_weight[0]], axis=1)
    summed = lax.psum_scatter(
        jnp.dot(gathered, both_weights, preferred_element_type=jnp.float32).astype(jnp.bfloat16),
        "ctx",
        scatter_dimension=0,
        tiled=True,
    )
    local_keys = summed[:, :head_width]
    local_values = summed[:, head_width:]
    key_count = local_keys.shape[0]
    key_places = lax.axis_index("ctx") * key_count + jnp.arange(key_count, dtype=jnp.int32)
    enc_doc = document_ids(enc_lengths, key_places)
    section_queries = queries[0]
    query_count = section_queries.shape[0]
    dec_doc = document_ids(dec_lengths, jnp.arange(query_count, dtype=jnp.int32))
    allowed = dec_doc[:, None] == enc_doc[None, :]
    factor = 1.0 / math.sqrt(HD)
    query_heads = section_queries.reshape(query_count, heads_here, HD)
    key_heads = local_keys.reshape(key_count, heads_here, HD)
    value_heads = local_values.reshape(key_count, heads_here, HD)
    scores = (
        jnp.einsum("qhd,khd->hqk", query_heads, key_heads, preferred_element_type=jnp.float32)
        * factor
    )
    scores = jnp.where(allowed[None], scores, jnp.float32(-1e30))
    local_top = jnp.max(scores, axis=2)
    top = lax.pmax(local_top, "ctx")
    weights = jnp.where(allowed[None], jnp.exp(scores - top[:, :, None]), jnp.float32(0.0))
    totals = jnp.sum(weights, axis=2)
    numer = jnp.einsum(
        "hqk,khd->qhd",
        weights.astype(jnp.bfloat16),
        value_heads,
        preferred_element_type=jnp.float32,
    )
    numer = numer.reshape(query_count, head_width)
    numer_share, total_share = (
        lax.psum_scatter(numer.astype(jnp.bfloat16), "ctx", scatter_dimension=0, tiled=True).astype(
            jnp.float32
        ),
        lax.psum_scatter(
            totals.T.astype(jnp.bfloat16), "ctx", scatter_dimension=0, tiled=True
        ).astype(jnp.float32),
    )
    share_rows = numer_share.shape[0]
    result = numer_share.reshape(share_rows, heads_here, HD) / total_share[:, :, None]
    return result.reshape(1, share_rows, head_width).astype(jnp.bfloat16)


def shift_perm(n, d):
    return [(i, (i + d) % n) for i in range(n)]


def xor_perm(n, b):
    return [(i, i ^ b) for i in range(n)]


def make_fast(n_sec, n_ctx, n_tp, n_chunks):
    def fast(enc_out, enc_lengths, dec_lengths, queries, key_weight, value_weight):
        f32, bf16 = jnp.float32, jnp.bfloat16
        s = lax.axis_index("section")
        c = lax.axis_index("ctx")
        t = lax.axis_index("tp")
        rows, feat = enc_out.shape
        head_width = key_weight.shape[2]
        sub = head_width // n_ctx
        cr = rows // n_chunks
        wk = key_weight[0].reshape(feat, n_ctx, sub)
        wv = value_weight[0].reshape(feat, n_ctx, sub)
        yb = c // 2
        xb = c % 2

        def pick(x, i, axis):
            return lax.dynamic_index_in_dim(x, i, axis, keepdims=False)

        def add(a, b):
            return (a.astype(f32) + b.astype(f32)).astype(bf16)

        key_parts, value_parts, places = [], [], []
        for k in range(n_chunks):
            mine = enc_out[k * cr:(k + 1) * cr]
            own_moved = [lax.ppermute(mine, "section", shift_perm(n_sec, d)) for d in range(1, n_sec)]
            received = jnp.stack([lax.ppermute(mine, "tp", shift_perm(n_tp, d)) for d in range(1, n_tp)])
            moved = lax.ppermute(received, "section", shift_perm(n_sec, 1))
            own_rows = jnp.concatenate([mine[None], received], axis=0).reshape(n_tp * cr, feat)
            partner_rows = jnp.concatenate([own_moved[0][None], moved], axis=0).reshape(n_tp * cr, feat)
            d_sec = jnp.arange(n_sec, dtype=jnp.int32)[:, None, None]
            d_tp = jnp.arange(n_tp, dtype=jnp.int32)[None, :, None]
            r = jnp.arange(cr, dtype=jnp.int32)[None, None, :]
            src = ((s - d_sec) % n_sec) * n_tp + (t - d_tp) % n_tp
            places.append((src * rows + k * cr + r).reshape(-1))
            half = n_tp * cr

            def project(x):
                pk = jnp.einsum("tf,fgc->gtc", x, wk, preferred_element_type=f32).astype(bf16)
                pv = jnp.einsum("tf,fgc->gtc", x, wv, preferred_element_type=f32).astype(bf16)
                return pk.reshape(2, 2, half, sub), pv.reshape(2, 2, half, sub)

            a_pk, a_pv = project(own_rows)
            send_k, send_v = pick(a_pk, 1 - yb, 0), pick(a_pv, 1 - yb, 0)
            send_k, send_v, _ = lax.optimization_barrier((send_k, send_v, moved))
            got = lax.ppermute((send_k, send_v), "ctx", xor_perm(n_ctx, 2))
            ok, ov = pick(a_pk, yb, 0), pick(a_pv, yb, 0)
            out_k = add(pick(ok, 1 - xb, 0), pick(got[0], 1 - xb, 0))
            out_v = add(pick(ov, 1 - xb, 0), pick(got[1], 1 - xb, 0))
            got2 = lax.ppermute((out_k, out_v), "ctx", xor_perm(n_ctx, 1))
            fa_k = add(add(pick(ok, xb, 0), pick(got[0], xb, 0)), got2[0])
            fa_v = add(add(pick(ov, xb, 0), pick(got[1], xb, 0)), got2[1])
            b_pk, b_pv = project(partner_rows)
            got = lax.ppermute((pick(b_pk, 1 - xb, 1), pick(b_pv, 1 - xb, 1)), "ctx", xor_perm(n_ctx, 1))
            ok, ov = pick(b_pk, xb, 1), pick(b_pv, xb, 1)
            out_k = add(pick(ok, 1 - yb, 0), pick(got[0], 1 - yb, 0))
            out_v = add(pick(ov, 1 - yb, 0), pick(got[1], 1 - yb, 0))
            got2 = lax.ppermute((out_k, out_v), "ctx", xor_perm(n_ctx, 2))
            fb_k = add(add(pick(ok, yb, 0), pick(got[0], yb, 0)), got2[0])
            fb_v = add(add(pick(ov, yb, 0), pick(got[1], yb, 0)), got2[1])
            key_parts += [fa_k, fb_k]
            value_parts += [fa_v, fb_v]

        keys = jnp.concatenate(key_parts, axis=0)
        values = jnp.concatenate(value_parts, axis=0)
        key_places = jnp.concatenate(places)
        key_count = keys.shape[0]
        heads = sub // HD
        enc_doc = document_ids(enc_lengths, key_places)
        section_queries = lax.dynamic_slice_in_dim(queries[0], c * sub, sub, axis=1)
        query_count = section_queries.shape[0]
        share = query_count // n_ctx
        first = c * share
        section_queries = lax.dynamic_slice_in_dim(
            jnp.concatenate([section_queries, section_queries], axis=0), first, query_count, axis=0
        )
        query_places = (first + jnp.arange(query_count, dtype=jnp.int32)) % query_count
        dec_doc = document_ids(dec_lengths, query_places)
        allowed = dec_doc[:, None] == enc_doc[None, :]
        factor = 1.0 / math.sqrt(HD)
        query_heads = section_queries.reshape(query_count, heads, HD)
        key_heads = keys.reshape(key_count, heads, HD)
        value_heads = values.reshape(key_count, heads, HD)
        scores = (
            jnp.einsum("qhd,khd->hqk", query_heads, key_heads, preferred_element_type=f32)
            * factor
        )
        scores = jnp.where(allowed[None], scores, f32(-1e30))
        top = jnp.max(scores, axis=2, keepdims=True)
        weights = jnp.where(allowed[None], jnp.exp(scores - top), f32(0.0))
        totals = jnp.sum(weights, axis=2)
        numer = jnp.einsum("hqk,khd->qhd", weights.astype(bf16), value_heads, preferred_element_type=f32)
        context = (numer / totals.T[:, :, None]).astype(bf16).reshape(query_count, sub)
        blocks = context.reshape(n_ctx, share, sub)
        pieces = [blocks[0]]
        for d in range(1, n_ctx):
            pieces.append(lax.ppermute(blocks[d], "ctx", shift_perm(n_ctx, d)))
        groups = []
        for g in range(n_ctx):
            val = pieces[0]
            for d in range(1, n_ctx):
                val = jnp.where((c - d) % n_ctx == g, pieces[d], val)
            groups.append(val)
        return jnp.concatenate(groups, axis=1).reshape(1, share, head_width)

    return fast


def solution(mesh):
    in_specs = (
        P(("section", "tp"), "ctx"),
        P(),
        P(),
        P("section", None, "tp"),
        P("section", "ctx", "tp"),
        P("section", "ctx", "tp"),
    )
    out_specs = P("section", "ctx", "tp")
    n_sec, n_ctx, n_tp = mesh.shape["section"], mesh.shape["ctx"], mesh.shape["tp"]
    return jax.shard_map(
        lambda *a: choose(n_sec, n_ctx, n_tp, *a), mesh=mesh, in_specs=in_specs, out_specs=out_specs, check_vma=False
    )


def choose(n_sec, n_ctx, n_tp, enc_out, enc_lengths, dec_lengths, queries, key_weight, value_weight):
    rows = enc_out.shape[0]
    head_width = key_weight.shape[2]
    query_count = queries.shape[1]
    ok = (
        n_ctx == 4
        and n_sec == 2
        and N_CHUNKS == 1
        and head_width % (n_ctx * HD) == 0
        and rows % N_CHUNKS == 0
        and (n_sec * n_tp * (rows // N_CHUNKS)) % 2 == 0
        and query_count % n_ctx == 0
    )
    args = (enc_out, enc_lengths, dec_lengths, queries, key_weight, value_weight)
    if ok:
        return make_fast(n_sec, n_ctx, n_tp, N_CHUNKS)(*args)
    return on_device(*args)
```

```python
import math

import jax
import jax.numpy as jnp
from jax import lax
from jax.sharding import PartitionSpec as P

HD = 64
N_CHUNKS = 1


def document_ids(lengths, places):
    ends = jnp.cumsum(lengths)
    return jnp.sum((places[:, None] >= ends[None, :]).astype(jnp.int32), axis=1)


def on_device(enc_out, enc_lengths, dec_lengths, queries, key_weight, value_weight):
    gathered = lax.all_gather(enc_out, ("section", "tp"), axis=0, tiled=True)
    head_width = key_weight.shape[2]
    heads_here = head_width // HD
    both_weights = jnp.concatenate([key_weight[0], value_weight[0]], axis=1)
    summed = lax.psum_scatter(
        jnp.dot(gathered, both_weights, preferred_element_type=jnp.float32).astype(jnp.bfloat16),
        "ctx",
        scatter_dimension=0,
        tiled=True,
    )
    local_keys = summed[:, :head_width]
    local_values = summed[:, head_width:]
    key_count = local_keys.shape[0]
    key_places = lax.axis_index("ctx") * key_count + jnp.arange(key_count, dtype=jnp.int32)
    enc_doc = document_ids(enc_lengths, key_places)
    section_queries = queries[0]
    query_count = section_queries.shape[0]
    dec_doc = document_ids(dec_lengths, jnp.arange(query_count, dtype=jnp.int32))
    allowed = dec_doc[:, None] == enc_doc[None, :]
    factor = 1.0 / math.sqrt(HD)
    query_heads = section_queries.reshape(query_count, heads_here, HD)
    key_heads = local_keys.reshape(key_count, heads_here, HD)
    value_heads = local_values.reshape(key_count, heads_here, HD)
    scores = (
        jnp.einsum("qhd,khd->hqk", query_heads, key_heads, preferred_element_type=jnp.float32)
        * factor
    )
    scores = jnp.where(allowed[None], scores, jnp.float32(-1e30))
    local_top = jnp.max(scores, axis=2)
    top = lax.pmax(local_top, "ctx")
    weights = jnp.where(allowed[None], jnp.exp(scores - top[:, :, None]), jnp.float32(0.0))
    totals = jnp.sum(weights, axis=2)
    numer = jnp.einsum(
        "hqk,khd->qhd",
        weights.astype(jnp.bfloat16),
        value_heads,
        preferred_element_type=jnp.float32,
    )
    numer = numer.reshape(query_count, head_width)
    numer_share, total_share = (
        lax.psum_scatter(numer.astype(jnp.bfloat16), "ctx", scatter_dimension=0, tiled=True).astype(
            jnp.float32
        ),
        lax.psum_scatter(
            totals.T.astype(jnp.bfloat16), "ctx", scatter_dimension=0, tiled=True
        ).astype(jnp.float32),
    )
    share_rows = numer_share.shape[0]
    result = numer_share.reshape(share_rows, heads_here, HD) / total_share[:, :, None]
    return result.reshape(1, share_rows, head_width).astype(jnp.bfloat16)


def shift_perm(n, d):
    return [(i, (i + d) % n) for i in range(n)]


def xor_perm(n, b):
    return [(i, i ^ b) for i in range(n)]


def make_fast(n_sec, n_ctx, n_tp, n_chunks):
    def fast(enc_out, enc_lengths, dec_lengths, queries, key_weight, value_weight):
        f32, bf16 = jnp.float32, jnp.bfloat16
        s = lax.axis_index("section")
        c = lax.axis_index("ctx")
        t = lax.axis_index("tp")
        rows, feat = enc_out.shape
        head_width = key_weight.shape[2]
        sub = head_width // n_ctx
        cr = rows // n_chunks
        wk = key_weight[0].reshape(feat, n_ctx, sub)
        wv = value_weight[0].reshape(feat, n_ctx, sub)
        yb = c // 2
        xb = c % 2

        def pick(x, i, axis):
            return lax.dynamic_index_in_dim(x, i, axis, keepdims=False)

        def add(a, b):
            return (a.astype(f32) + b.astype(f32)).astype(bf16)

        key_parts, value_parts, places = [], [], []
        for k in range(n_chunks):
            mine = enc_out[k * cr:(k + 1) * cr]
            own_moved = [lax.ppermute(mine, "section", shift_perm(n_sec, d)) for d in range(1, n_sec)]
            received = jnp.stack([lax.ppermute(mine, "tp", shift_perm(n_tp, d)) for d in range(1, n_tp)])
            moved = lax.ppermute(received, "section", shift_perm(n_sec, 1))
            own_rows = jnp.concatenate([mine[None], received], axis=0).reshape(n_tp * cr, feat)
            partner_rows = jnp.concatenate([own_moved[0][None], moved], axis=0).reshape(n_tp * cr, feat)
            d_sec = jnp.arange(n_sec, dtype=jnp.int32)[:, None, None]
            d_tp = jnp.arange(n_tp, dtype=jnp.int32)[None, :, None]
            r = jnp.arange(cr, dtype=jnp.int32)[None, None, :]
            src = ((s - d_sec) % n_sec) * n_tp + (t - d_tp) % n_tp
            places.append((src * rows + k * cr + r).reshape(-1))
            half = n_tp * cr

            def project(x):
                pk = jnp.einsum("tf,fgc->gtc", x, wk, preferred_element_type=f32).astype(bf16)
                pv = jnp.einsum("tf,fgc->gtc", x, wv, preferred_element_type=f32).astype(bf16)
                return pk.reshape(2, 2, half, sub), pv.reshape(2, 2, half, sub)

            a_pk, a_pv = project(own_rows)
            send_k, send_v = pick(a_pk, 1 - yb, 0), pick(a_pv, 1 - yb, 0)
            send_k, send_v, _ = lax.optimization_barrier((send_k, send_v, moved))
            got = lax.ppermute((send_k, send_v), "ctx", xor_perm(n_ctx, 2))
            s1k = add(pick(a_pk, yb, 0), got[0])
            s1v = add(pick(a_pv, yb, 0), got[1])
            got = lax.ppermute((pick(s1k, 1 - xb, 0), pick(s1v, 1 - xb, 0)), "ctx", xor_perm(n_ctx, 1))
            fa_k = add(pick(s1k, xb, 0), got[0])
            fa_v = add(pick(s1v, xb, 0), got[1])
            b_pk, b_pv = project(partner_rows)
            got = lax.ppermute((pick(b_pk, 1 - xb, 1), pick(b_pv, 1 - xb, 1)), "ctx", xor_perm(n_ctx, 1))
            s2k = add(pick(b_pk, xb, 1), got[0])
            s2v = add(pick(b_pv, xb, 1), got[1])
            got = lax.ppermute((pick(s2k, 1 - yb, 0), pick(s2v, 1 - yb, 0)), "ctx", xor_perm(n_ctx, 2))
            fb_k = add(pick(s2k, yb, 0), got[0])
            fb_v = add(pick(s2v, yb, 0), got[1])
            key_parts += [fa_k, fb_k]
            value_parts += [fa_v, fb_v]

        keys = jnp.concatenate(key_parts, axis=0)
        values = jnp.concatenate(value_parts, axis=0)
        key_places = jnp.concatenate(places)
        key_count = keys.shape[0]
        heads = sub // HD
        enc_doc = document_ids(enc_lengths, key_places)
        section_queries = lax.dynamic_slice_in_dim(queries[0], c * sub, sub, axis=1)
        query_count = section_queries.shape[0]
        share = query_count // n_ctx
        first = c * share
        section_queries = lax.dynamic_slice_in_dim(
            jnp.concatenate([section_queries, section_queries], axis=0), first, query_count, axis=0
        )
        query_places = (first + jnp.arange(query_count, dtype=jnp.int32)) % query_count
        dec_doc = document_ids(dec_lengths, query_places)
        allowed = dec_doc[:, None] == enc_doc[None, :]
        factor = 1.0 / math.sqrt(HD)
        query_heads = section_queries.reshape(query_count, heads, HD)
        key_heads = keys.reshape(key_count, heads, HD)
        value_heads = values.reshape(key_count, heads, HD)
        scores = (
            jnp.einsum("qhd,khd->hqk", query_heads, key_heads, preferred_element_type=f32)
            * factor
        )
        scores = lax.optimization_barrier(jnp.where(allowed[None], scores, f32(-1e30)))
        top = jnp.max(scores, axis=2, keepdims=True)
        weights = jnp.where(allowed[None], jnp.exp(scores - top), f32(0.0))
        totals = jnp.sum(weights, axis=2)
        numer = jnp.einsum("hqk,khd->qhd", weights.astype(bf16), value_heads, preferred_element_type=f32)
        context = (numer / totals.T[:, :, None]).astype(bf16).reshape(query_count, sub)
        blocks = context.reshape(n_ctx, share, sub)
        pieces = [blocks[0]]
        for d in range(1, n_ctx):
            pieces.append(lax.ppermute(blocks[d], "ctx", shift_perm(n_ctx, d)))
        groups = []
        for g in range(n_ctx):
            val = pieces[0]
            for d in range(1, n_ctx):
                val = jnp.where((c - d) % n_ctx == g, pieces[d], val)
            groups.append(val)
        return jnp.concatenate(groups, axis=1).reshape(1, share, head_width)

    return fast


def solution(mesh):
    in_specs = (
        P(("section", "tp"), "ctx"),
        P(),
        P(),
        P("section", None, "tp"),
        P("section", "ctx", "tp"),
        P("section", "ctx", "tp"),
    )
    out_specs = P("section", "ctx", "tp")
    n_sec, n_ctx, n_tp = mesh.shape["section"], mesh.shape["ctx"], mesh.shape["tp"]
    return jax.shard_map(
        lambda *a: choose(n_sec, n_ctx, n_tp, *a), mesh=mesh, in_specs=in_specs, out_specs=out_specs, check_vma=False
    )


def choose(n_sec, n_ctx, n_tp, enc_out, enc_lengths, dec_lengths, queries, key_weight, value_weight):
    rows = enc_out.shape[0]
    head_width = key_weight.shape[2]
    query_count = queries.shape[1]
    ok = (
        n_ctx == 4
        and n_sec == 2
        and N_CHUNKS == 1
        and head_width % (n_ctx * HD) == 0
        and rows % N_CHUNKS == 0
        and (n_sec * n_tp * (rows // N_CHUNKS)) % 2 == 0
        and query_count % n_ctx == 0
    )
    args = (enc_out, enc_lengths, dec_lengths, queries, key_weight, value_weight)
    if ok:
        return make_fast(n_sec, n_ctx, n_tp, N_CHUNKS)(*args)
    return on_device(*args)
```
